32 devices in a mesh: groups: 2 (over y), seq: 4 (over z), dp: 2 (over x), head: 2 (over core).
Axes of the slice: x: 2, y: 2, z: 4, core: 2. Of those that a mesh axis runs over, the one named last changes fastest.
Arguments:
- queries: bfloat16 [4, 512, 2048], P(('groups', 'dp'), 'seq', 'head'), parts along dimension 0, may hold values from -8 to 8
- keys: bfloat16 [4, 512, 2048], P(('groups', 'dp'), 'seq', 'head'), parts along dimension 0, may hold values from -8 to 8
- values: bfloat16 [4, 512, 2048], P(('groups', 'dp'), 'seq', 'head'), parts along dimension 0, may hold values from -12 to 12
- pattern: int32 [4, 8, 2], P(('groups', 'dp'), 'seq'), parts along dimension 0, may hold values from -2 to 2, as said below
- out_weight: bfloat16 [4096, 2048], P('seq', 'head'), may hold values from -0.125 to 0.125
- cotangent: bfloat16 [4, 512, 4096], P(('groups', 'dp'), 'seq'), parts along dimension 0, may hold values from -6 to 6
Outputs:
- attention: bfloat16 [4, 512, 2048], P(('groups', 'dp'), 'seq', 'head'), parts along dimension 0
- query_grad: bfloat16 [4, 512, 2048], P(('groups', 'dp'), 'seq', 'head'), parts along dimension 0
- key_grad: bfloat16 [4, 512, 2048], P(('groups', 'dp'), 'seq', 'head'), parts along dimension 0
- value_grad: bfloat16 [4, 512, 2048], P(('groups', 'dp'), 'seq', 'head'), parts along dimension 0
- weight_grad: float32 [8192, 2048], P(('groups', 'seq'), 'head'), parts along dimension 0
The draws below stay inside these ranges and needn't reach their ends.
There are 2 independent parts, one for each index of `groups`. The reference program is written for one: setup_inputs(seed, part) draws one part's arguments, and reference() takes and returns one part's arrays. A program takes and returns all parts, laid end to end along the dimension named above; an argument that names none is the same for every part. Nothing has to cross between parts.
Inputs may be any that keep to these rules, and one draw needn't show every extreme that they name: `pattern`: each row holds 2 different block offsets from -2, -1, 1, 2, each keeping the block inside its document.
All inputs are finite; a program needn't handle non-finite values.
Results may differ from the reference program's by a relative error of at most 0.0099.
Values may be sent and summed in bfloat16 or wider, within the bound.
No kernel may reach another device: no remote copies, remote signals or barrier semaphores. Data moves between devices by JAX's collectives and lax.ppermute only.
A program may use at most 128 MiB of HBM per device.

```python
import math
import jax
import jax.numpy as jnp
from jax import lax

D = 4096
HEAD_DIM = 128
BLK = 64
NEAR = 2
LEN = 512
NBLK = 8
HEADS = 16
HK = 2048
DOCS = 2
N_SEQ = 4


def drawn_pair(key):
    base = jax.random.fold_in(key, 23)
    key_query, key_key = jax.random.split(base, 2)
    shape = (DOCS, LEN, HEADS * HEAD_DIM)
    query_part = jnp.clip(jax.random.normal(key_query, shape, jnp.float32), -5.0, 5.0)
    key_part = jnp.clip(jax.random.normal(key_key, shape, jnp.float32), -5.0, 5.0)
    return (query_part.astype(jnp.bfloat16), key_part.astype(jnp.bfloat16))


def draw_queries(key, part):
    return drawn_pair(key)[0]


def draw_keys(key, part):
    return drawn_pair(key)[1]


def draw_pattern(key, part):
    offsets = jnp.array([-2, -1, 1, 2], dtype=jnp.int32)
    targets = jnp.arange(NBLK, dtype=jnp.int32)[:, None] + offsets[None, :]
    invalid = jnp.logical_or(targets < 0, targets >= NBLK).astype(jnp.int32)
    ranks = jax.random.randint(key, (DOCS, NBLK, 4), 0, 1000, dtype=jnp.int32) * 4 + jnp.arange(4, dtype=jnp.int32)
    ranks = ranks + 100000 * invalid[None, :, :]
    order = jnp.argsort(ranks, axis=-1)[..., :NEAR]
    return offsets[order].astype(jnp.int32)


def strengthened(drawn, key, source, target, shards_of, factor):
    owner, partner = [(jnp.arange(drawn.shape[position]) // (drawn.shape[position] // shards_of)).reshape([-1 if axis == position else 1 for axis in range(drawn.ndim)]) for position in (source, target)]
    chosen = jax.random.permutation(key, shards_of)[partner]
    strong = (owner == chosen) | (owner == (partner + shards_of // 2) % shards_of)
    return jnp.where(strong, factor * drawn, drawn)


def shard_levels(rng, shape, cuts, low, top_value):
    def one(position, parts):
        heights = jax.random.uniform(jax.random.fold_in(jax.random.fold_in(rng, 6), position), (parts,), jnp.float32, low / len(cuts), top_value / len(cuts))
        return jnp.repeat(jnp.exp(heights), shape[position] // parts).reshape((-1,) + (1,) * (len(shape) - position - 1))

    loudness = one(*cuts[0])
    for cut in cuts[1:]:
        loudness = loudness * one(*cut)
    return loudness


def scatter_about(own_key, extent, deviation, limit, cuts=(), held_as=jnp.bfloat16):
    values = deviation * jax.random.normal(own_key, extent, jnp.float32)
    if cuts:
        values = values * shard_levels(own_key, extent, cuts, -0.22, 0.18)
    return jnp.clip(values, -limit, limit).astype(held_as)


def heavy_noise(rng, dims, scale, reach, pieces, heavy, kind=jnp.bfloat16):
    drawn = scale * jax.random.normal(rng, dims, jnp.float32)
    if pieces:
        drawn = drawn * shard_levels(rng, dims, pieces, -0.22, 0.18)
    return jnp.clip(strengthened(drawn, jax.random.fold_in(rng, 3), *heavy), -reach, reach).astype(kind)


def setup_inputs(seed: int = 0, part: int = 0) -> dict:
    seeds = jax.random.split(jax.random.key(seed), 7)
    part_splits = jax.random.split(jax.random.fold_in(seeds[6], part), 7)
    queries = draw_queries(jax.random.fold_in(jax.random.fold_in(seeds[6], part), 71), part)
    keys = draw_keys(jax.random.fold_in(jax.random.fold_in(seeds[6], part), 71), part)
    values = scatter_about(part_splits[2], (DOCS, LEN, HK), 2.0, 12.0, ((0, 2), (1, 4), (2, 2)))
    pattern = draw_pattern(jax.random.fold_in(jax.random.fold_in(seeds[6], part), 71), part)
    out_weight = scatter_about(seeds[4], (D, HK), HK ** -0.5, 0.125, ((0, 4), (1, 2)))
    cotangent = heavy_noise(part_splits[5], (DOCS, LEN, D), 1.0, 6.0, ((0, 2), (1, 4)), (1, 2, 4, 2.0))
    return dict(queries=queries, keys=keys, values=values, pattern=pattern, out_weight=out_weight, cotangent=cotangent)


def pool_pairs(source):
    shaped = source.reshape(source.shape[0], source.shape[1] // 2, 2, source.shape[2])
    return lax.optimization_barrier(jnp.sum(shaped, axis=2)) * 0.5

def one_document(inputs):
    query_doc, key_doc, value_doc, pattern_doc, cotangent_doc, out_weight = inputs
    levels = N_SEQ.bit_length() - 1
    heads = HK // HEAD_DIM
    score_scale = 1.0 / math.sqrt(HEAD_DIM)
    block_ids = jnp.arange(NBLK, dtype=jnp.int32)
    chosen = jnp.concatenate([block_ids[:, None], block_ids[:, None] + pattern_doc.astype(jnp.int32)], axis=1) + 2
    key_value = jnp.stack([key_doc, value_doc])
    blocked = key_value.reshape(2, NBLK, BLK, HK)
    padded = jnp.pad(blocked, ((0, 0), (2, 2), (0, 0), (0, 0)))
    near_pair = padded[:, chosen].reshape(2, NBLK, (NEAR + 1) * BLK, HK)
    pooled = key_value.astype(jnp.float32)
    far_list = []
    sibling_list = []
    for level_no in range(1, levels + 1):
        pooled = pool_pairs(pooled)
        level_blocks = pooled.reshape(2, NBLK >> level_no, BLK, HK)
        sibling = jnp.bitwise_xor(jnp.right_shift(block_ids, level_no), 1)
        sibling_list.append(sibling)
        far_list.append(level_blocks[:, sibling])
    far_pair = jnp.stack(far_list, axis=2).reshape(2, NBLK, levels * BLK, HK).astype(jnp.bfloat16)
    all_pair = jnp.concatenate([near_pair, far_pair], axis=2)
    width_keys = all_pair.shape[2]
    query_heads = query_doc.reshape(NBLK, BLK, heads, HEAD_DIM).astype(jnp.float32)
    key_heads = all_pair[0].reshape(NBLK, width_keys, heads, HEAD_DIM).astype(jnp.float32)
    value_heads = all_pair[1].reshape(NBLK, width_keys, heads, HEAD_DIM).astype(jnp.float32)
    scores = jnp.einsum('bqhe,bkhe->bhqk', query_heads, key_heads) * score_scale
    softmax_w = jax.nn.softmax(scores, axis=-1)
    rounded_w = softmax_w.astype(jnp.bfloat16).astype(jnp.float32)
    output = jnp.einsum('bhqk,bkhe->bqhe', rounded_w, value_heads)
    attention = output.reshape(LEN, HK).astype(jnp.bfloat16)
    attn_grad = jnp.dot(cotangent_doc, out_weight, preferred_element_type=jnp.float32).astype(jnp.bfloat16)
    weight_part = jnp.dot(cotangent_doc.T, attention, preferred_element_type=jnp.float32)
    grad_heads = attn_grad.reshape(NBLK, BLK, heads, HEAD_DIM).astype(jnp.float32)
    prob_grad = jnp.einsum('bqhe,bkhe->bhqk', grad_heads, value_heads)
    row_dot = lax.optimization_barrier(jnp.sum(softmax_w * prob_grad, axis=-1, keepdims=True))
    score_grad = (softmax_w * (prob_grad - row_dot)).astype(jnp.bfloat16).astype(jnp.float32)
    query_grad = (jnp.einsum('bhqk,bkhe->bqhe', score_grad, key_heads) * score_scale).reshape(LEN, HK).astype(jnp.bfloat16)
    row_key = jnp.einsum('bhqk,bqhe->bkhe', score_grad, query_heads) * score_scale
    row_value = jnp.einsum('bhqk,bqhe->bkhe', rounded_w, grad_heads)
    row_grads = jnp.stack([row_key, row_value]).reshape(2, NBLK, NEAR + 1 + levels, BLK, HK)
    near_back = jnp.zeros((2, NBLK + 4, BLK, HK), jnp.float32).at[:, chosen].add(row_grads[:, :, :NEAR + 1])
    token_grad = near_back[:, 2:NBLK + 2].reshape(2, LEN, HK)
    for level_no in range(1, levels + 1):
        level_rows = row_grads[:, :, NEAR + level_no]
        level_back = jnp.zeros((2, NBLK >> level_no, BLK, HK), jnp.float32).at[:, sibling_list[level_no - 1]].add(level_rows)
        level_back = level_back.reshape(2, LEN >> level_no, HK)
        token_grad = token_grad + jnp.repeat(level_back, 2 ** level_no, axis=1) / float(2 ** level_no)
    key_grad = token_grad[0].astype(jnp.bfloat16)
    value_grad = token_grad[1].astype(jnp.bfloat16)
    return (attention, query_grad, key_grad, value_grad, weight_part)

def reference(queries, keys, values, pattern, out_weight, cotangent):

    def per_doc(inputs):
        return one_document(inputs + (out_weight,))
    attention, query_grad, key_grad, value_grad, weight_parts = lax.map(per_doc, (queries, keys, values, pattern, cotangent))
    weight_grad = lax.optimization_barrier(jnp.sum(weight_parts, axis=0))
    return (attention, query_grad, key_grad, value_grad, weight_grad)
```

```python
import math

import jax
import jax.numpy as jnp
from jax import lax
from jax.sharding import PartitionSpec as P

HEAD_DIM = 128
NEAR = 2


def extended(cells, sides, width):
    for axis, dim in sides:
        count = lax.axis_size(axis)
        ends = count - 1
        head = lax.slice_in_dim(cells, 0, width, axis=dim)
        tail = lax.slice_in_dim(cells, cells.shape[dim] - width, cells.shape[dim], axis=dim)
        cells = jnp.concatenate(
            [
                lax.ppermute(tail, axis, [(i, (i + 1) % count) for i in range(ends)]),
                cells,
                lax.ppermute(head, axis, [((i + 1) % count, i) for i in range(ends)]),
            ],
            axis=dim,
        )
    return cells


def swapped(shard, axis, stride):
    return lax.ppermute(shard, axis, [(i, i ^ 1 << stride) for i in range(lax.axis_size(axis))])


def pool_pairs(source):
    shaped = source.reshape(
        source.shape[0], source.shape[1], source.shape[2] // 2, 2, source.shape[3]
    )
    return jnp.sum(shaped, axis=3) * 0.5


def pick_blocks(blocks_doc, chosen_doc):
    return blocks_doc[:, chosen_doc]


def place_blocks(grad_doc, chosen_doc):
    holder = jnp.zeros((grad_doc.shape[0], 6, grad_doc.shape[3], grad_doc.shape[4]), jnp.float32)
    return holder.at[:, chosen_doc].add(grad_doc)


def shards(queries, keys, values, pattern, out_weight, cotangent):
    doc_count, tok_count, head_cols = queries.shape
    block = tok_count // 2
    heads = head_cols // HEAD_DIM
    seq_count = lax.axis_size("seq")
    levels = seq_count.bit_length() - 1
    position = lax.axis_index("seq")
    score_scale = 1.0 / math.sqrt(HEAD_DIM)
    near_width = (NEAR + 1) * block
    key_value = jnp.stack([keys, values])
    padded = extended(key_value, (("seq", 2),), tok_count)
    blocks_six = padded.reshape(2, doc_count, 6, block, head_cols)
    local_ids = jnp.arange(2, dtype=jnp.int32)[None, :, None]
    chosen = jnp.concatenate([local_ids, local_ids + pattern], axis=2) + 2
    near_pair = jax.vmap(pick_blocks, in_axes=(1, 0), out_axes=1)(blocks_six, chosen)
    near_pair = near_pair.reshape(2, doc_count, 2, near_width, head_cols)
    pooled = pool_pairs(key_value.astype(jnp.float32))
    siblings = []
    own_level = pooled
    for level_no in range(levels):
        other = swapped(own_level, "seq", level_no)
        siblings.append(other)
        if level_no + 1 < levels:
            upper = position >> level_no & 1 == 1
            joined = jnp.where(
                upper,
                jnp.concatenate([other, own_level], axis=2),
                jnp.concatenate([own_level, other], axis=2),
            )
            own_level = pool_pairs(joined)
    far_pair = jnp.concatenate(siblings, axis=2).astype(jnp.bfloat16)
    query_heads = queries.reshape(doc_count, 2, block, heads, HEAD_DIM)
    near_k = near_pair[0].reshape(doc_count, 2, near_width, heads, HEAD_DIM)
    near_v = near_pair[1].reshape(doc_count, 2, near_width, heads, HEAD_DIM)
    far_k = far_pair[0].reshape(doc_count, levels * block, heads, HEAD_DIM)
    far_v = far_pair[1].reshape(doc_count, levels * block, heads, HEAD_DIM)
    score_near = (
        jnp.einsum("dbqhe,dbkhe->dbhqk", query_heads, near_k, preferred_element_type=jnp.float32)
        * score_scale
    )
    score_far = (
        jnp.einsum("dbqhe,dkhe->dbhqk", query_heads, far_k, preferred_element_type=jnp.float32)
        * score_scale
    )
    top = jnp.maximum(
        jnp.max(score_near, axis=-1, keepdims=True), jnp.max(score_far, axis=-1, keepdims=True)
    )
    exp_near = jnp.exp(score_near - top)
    exp_far = jnp.exp(score_far - top)
    total = jnp.sum(exp_near, axis=-1, keepdims=True) + jnp.sum(exp_far, axis=-1, keepdims=True)
    weight_near = exp_near / total
    weight_far = exp_far / total
    rounded_near = weight_near.astype(jnp.bfloat16)
    rounded_far = weight_far.astype(jnp.bfloat16)
    output = jnp.einsum(
        "dbhqk,dbkhe->dbqhe", rounded_near, near_v, preferred_element_type=jnp.float32
    )
    output = output + jnp.einsum(
        "dbhqk,dkhe->dbqhe", rounded_far, far_v, preferred_element_type=jnp.float32
    )
    attention = output.reshape(doc_count, tok_count, head_cols).astype(jnp.bfloat16)
    feat_count = cotangent.shape[2] // seq_count
    cot_split = jnp.transpose(
        cotangent.reshape(doc_count, tok_count, seq_count, feat_count), (2, 0, 1, 3)
    )
    by_feature = lax.all_to_all(cot_split, "seq", 0, 0, tiled=True)
    grad_part = jnp.einsum(
        "sdtf,fc->sdtc", by_feature, out_weight, preferred_element_type=jnp.float32
    )
    attn_grad = lax.psum_scatter(grad_part, "seq", scatter_dimension=0, tiled=True)
    attn_grad = attn_grad.reshape(doc_count * tok_count, head_cols).astype(jnp.bfloat16)
    feat_docs = jnp.transpose(by_feature, (1, 0, 2, 3)).reshape(
        doc_count, seq_count * tok_count, feat_count
    )
    whole_output = lax.all_gather(attention, "seq", axis=1, tiled=True)
    dp_count = lax.axis_size("dp")
    if dp_count == 2:
        feat_docs = jnp.concatenate([feat_docs, swapped(feat_docs, "dp", 0)], axis=0)
        whole_output = jnp.concatenate([whole_output, swapped(whole_output, "dp", 0)], axis=0)
    else:
        feat_docs = lax.all_gather(feat_docs, "dp", axis=0, tiled=True)
        whole_output = lax.all_gather(whole_output, "dp", axis=0, tiled=True)
    weight_grad = jnp.einsum(
        "dtc,dtw->cw", feat_docs, whole_output, preferred_element_type=jnp.float32
    )
    grad_heads = attn_grad.reshape(doc_count, 2, block, heads, HEAD_DIM)
    prob_near = jnp.einsum(
        "dbqhe,dbkhe->dbhqk", grad_heads, near_v, preferred_element_type=jnp.float32
    )
    prob_far = jnp.einsum(
        "dbqhe,dkhe->dbhqk", grad_heads, far_v, preferred_element_type=jnp.float32
    )
    row_dot = jnp.sum(weight_near * prob_near, axis=-1, keepdims=True) + jnp.sum(
        weight_far * prob_far, axis=-1, keepdims=True
    )
    grad_near = (weight_near * (prob_near - row_dot)).astype(jnp.bfloat16)
    grad_far = (weight_far * (prob_far - row_dot)).astype(jnp.bfloat16)
    query_sum = jnp.einsum(
        "dbhqk,dbkhe->dbqhe", grad_near, near_k, preferred_element_type=jnp.float32
    )
    query_sum = query_sum + jnp.einsum(
        "dbhqk,dkhe->dbqhe", grad_far, far_k, preferred_element_type=jnp.float32
    )
    query_grad = (
        (query_sum * score_scale).reshape(doc_count, tok_count, head_cols).astype(jnp.bfloat16)
    )
    near_key_rows = (
        jnp.einsum("dbhqk,dbqhe->dbkhe", grad_near, query_heads, preferred_element_type=jnp.float32)
        * score_scale
    )
    near_value_rows = jnp.einsum(
        "dbhqk,dbqhe->dbkhe", rounded_near, grad_heads, preferred_element_type=jnp.float32
    )
    far_key_rows = (
        jnp.einsum("dbhqk,dbqhe->dkhe", grad_far, query_heads, preferred_element_type=jnp.float32)
        * score_scale
    )
    far_value_rows = jnp.einsum(
        "dbhqk,dbqhe->dkhe", rounded_far, grad_heads, preferred_element_type=jnp.float32
    )
    near_rows = jnp.stack([near_key_rows, near_value_rows]).reshape(
        2, doc_count, 2, NEAR + 1, block, head_cols
    )
    back_six = jax.vmap(place_blocks, in_axes=(1, 0), out_axes=1)(near_rows, chosen)
    rims = jnp.concatenate([back_six[:, :, 0:2], back_six[:, :, 4:6]], axis=2).reshape(
        2, doc_count, 2 * tok_count, head_cols
    )
    beside_all = extended(rims, (("seq", 2),), tok_count)
    token_grad = back_six[:, :, 2:4].reshape(2, doc_count, tok_count, head_cols)
    token_grad = token_grad + beside_all[:, :, :tok_count] + beside_all[:, :, 3 * tok_count :]
    far_rows = jnp.stack([far_key_rows, far_value_rows]).reshape(
        2, doc_count, levels, block, head_cols
    )
    carried = jnp.zeros((2, doc_count, block, head_cols), jnp.float32)
    for level_no in reversed(range(levels)):
        message = far_rows[:, :, level_no]
        mine = jnp.zeros_like(message)
        if level_no + 1 < levels:
            upper = position >> level_no & 1 == 1
            spread = jnp.repeat(carried, 2, axis=2) * 0.5
            lower_half = spread[:, :, :block]
            upper_half = spread[:, :, block:]
            mine = jnp.where(upper, upper_half, lower_half)
            message = message + jnp.where(upper, lower_half, upper_half)
        returned = swapped(message, "seq", level_no)
        carried = returned + mine
    token_grad = token_grad + jnp.repeat(carried, 2, axis=2) * 0.5
    key_grad = token_grad[0].astype(jnp.bfloat16)
    value_grad = token_grad[1].astype(jnp.bfloat16)
    return (attention, query_grad, key_grad, value_grad, weight_grad)


def solution(mesh):
    in_specs = (
        P(("groups", "dp"), "seq", "head"),
        P(("groups", "dp"), "seq", "head"),
        P(("groups", "dp"), "seq", "head"),
        P(("groups", "dp"), "seq", None),
        P("seq", "head"),
        P(("groups", "dp"), "seq", None),
    )
    out_specs = (
        P(("groups", "dp"), "seq", "head"),
        P(("groups", "dp"), "seq", "head"),
        P(("groups", "dp"), "seq", "head"),
        P(("groups", "dp"), "seq", "head"),
        P(("groups", "seq"), "head"),
    )
    return jax.shard_map(shards, mesh=mesh, in_specs=in_specs, out_specs=out_specs, check_vma=False)
```

```python
import math

import jax
import jax.numpy as jnp
from jax import lax
from jax.sharding import PartitionSpec as P

HEAD_DIM = 128
NEAR = 2


def extended(cells, sides, width):
    for axis, dim in sides:
        count = lax.axis_size(axis)
        ends = count - 1
        head = lax.slice_in_dim(cells, 0, width, axis=dim)
        tail = lax.slice_in_dim(cells, cells.shape[dim] - width, cells.shape[dim], axis=dim)
        cells = jnp.concatenate(
            [
                lax.ppermute(tail, axis, [(i, (i + 1) % count) for i in range(ends)]),
                cells,
                lax.ppermute(head, axis, [((i + 1) % count, i) for i in range(ends)]),
            ],
            axis=dim,
        )
    return cells


def swapped(shard, axis, stride):
    return lax.ppermute(shard, axis, [(i, i ^ 1 << stride) for i in range(lax.axis_size(axis))])


def pool_pairs(source):
    shaped = source.reshape(
        source.shape[0], source.shape[1], source.shape[2] // 2, 2, source.shape[3]
    )
    return jnp.sum(shaped, axis=3) * 0.5


def pick_blocks(blocks_doc, chosen_doc):
    return blocks_doc[:, chosen_doc]


def place_blocks(grad_doc, chosen_doc):
    holder = jnp.zeros((grad_doc.shape[0], 6, grad_doc.shape[3], grad_doc.shape[4]), jnp.float32)
    return holder.at[:, chosen_doc].add(grad_doc)


def shards(queries, keys, values, pattern, out_weight, cotangent):
    doc_count, tok_count, head_cols = queries.shape
    block = tok_count // 2
    heads = head_cols // HEAD_DIM
    seq_count = lax.axis_size("seq")
    levels = seq_count.bit_length() - 1
    position = lax.axis_index("seq")
    score_scale = 1.0 / math.sqrt(HEAD_DIM)
    near_width = (NEAR + 1) * block
    key_value = jnp.stack([keys, values])
    padded = extended(key_value, (("seq", 2),), tok_count)
    blocks_six = padded.reshape(2, doc_count, 6, block, head_cols)
    local_ids = jnp.arange(2, dtype=jnp.int32)[None, :, None]
    chosen = jnp.concatenate([local_ids, local_ids + pattern], axis=2) + 2
    near_pair = jax.vmap(pick_blocks, in_axes=(1, 0), out_axes=1)(blocks_six, chosen)
    near_pair = near_pair.reshape(2, doc_count, 2, near_width, head_cols)
    pooled = pool_pairs(key_value.astype(jnp.float32))
    siblings = []
    own_level = pooled
    for level_no in range(levels):
        other = swapped(own_level, "seq", level_no)
        siblings.append(other)
        if level_no + 1 < levels:
            upper = position >> level_no & 1 == 1
            joined = jnp.where(
                upper,
                jnp.concatenate([other, own_level], axis=2),
                jnp.concatenate([own_level, other], axis=2),
            )
            own_level = pool_pairs(joined)
    far_pair = jnp.concatenate(siblings, axis=2).astype(jnp.bfloat16)
    query_heads = queries.reshape(doc_count, 2, block, heads, HEAD_DIM)
    near_k = near_pair[0].reshape(doc_count, 2, near_width, heads, HEAD_DIM)
    near_v = near_pair[1].reshape(doc_count, 2, near_width, heads, HEAD_DIM)
    far_k = far_pair[0].reshape(doc_count, levels * block, heads, HEAD_DIM)
    far_v = far_pair[1].reshape(doc_count, levels * block, heads, HEAD_DIM)
    score_near = (
        jnp.einsum("dbqhe,dbkhe->dbhqk", query_heads, near_k, preferred_element_type=jnp.float32)
        * score_scale
    )
    score_far = (
        jnp.einsum("dbqhe,dkhe->dbhqk", query_heads, far_k, preferred_element_type=jnp.float32)
        * score_scale
    )
    top = jnp.maximum(
        jnp.max(score_near, axis=-1, keepdims=True), jnp.max(score_far, axis=-1, keepdims=True)
    )
    exp_near = jnp.exp(score_near - top)
    exp_far = jnp.exp(score_far - top)
    total = jnp.sum(exp_near, axis=-1, keepdims=True) + jnp.sum(exp_far, axis=-1, keepdims=True)
    weight_near = exp_near / total
    weight_far = exp_far / total
    rounded_near = weight_near.astype(jnp.bfloat16)
    rounded_far = weight_far.astype(jnp.bfloat16)
    output = jnp.einsum(
        "dbhqk,dbkhe->dbqhe", rounded_near, near_v, preferred_element_type=jnp.float32
    )
    output = output + jnp.einsum(
        "dbhqk,dkhe->dbqhe", rounded_far, far_v, preferred_element_type=jnp.float32
    )
    attention = output.reshape(doc_count, tok_count, head_cols).astype(jnp.bfloat16)
    feat_count = cotangent.shape[2] // seq_count
    cot_rows = cotangent.reshape(doc_count * tok_count, cotangent.shape[2])
    out_rows = attention.reshape(doc_count * tok_count, head_cols)
    own_cols = lax.dynamic_slice_in_dim(cot_rows, position * feat_count, feat_count, axis=1)
    grad_sum = jnp.dot(own_cols, out_weight, preferred_element_type=jnp.float32)
    feat_list = [own_cols]
    out_list = [out_rows]
    for step in range(1, seq_count):
        pairs = [(i, i ^ step) for i in range(seq_count)]
        sent = lax.dynamic_slice_in_dim(
            cot_rows, (position ^ step) * feat_count, feat_count, axis=1
        )
        got = lax.ppermute(sent, "seq", pairs)
        part = jnp.dot(got, out_weight, preferred_element_type=jnp.float32)
        back = lax.ppermute(part.astype(jnp.bfloat16), "seq", pairs)
        grad_sum = grad_sum + back.astype(jnp.float32)
        feat_list.append(got)
        out_list.append(lax.ppermute(out_rows, "seq", pairs))
    attn_grad = grad_sum.astype(jnp.bfloat16)
    feat_docs = jnp.concatenate(feat_list, axis=0)
    whole_output = jnp.concatenate(out_list, axis=0)
    dp_count = lax.axis_size("dp")
    if dp_count == 2:
        feat_docs = jnp.concatenate([feat_docs, swapped(feat_docs, "dp", 0)], axis=0)
        whole_output = jnp.concatenate([whole_output, swapped(whole_output, "dp", 0)], axis=0)
    else:
        feat_docs = lax.all_gather(feat_docs, "dp", axis=0, tiled=True)
        whole_output = lax.all_gather(whole_output, "dp", axis=0, tiled=True)
    weight_grad = jnp.einsum(
        "tc,tw->cw", feat_docs, whole_output, preferred_element_type=jnp.float32
    )
    grad_heads = attn_grad.reshape(doc_count, 2, block, heads, HEAD_DIM)
    prob_near = jnp.einsum(
        "dbqhe,dbkhe->dbhqk", grad_heads, near_v, preferred_element_type=jnp.float32
    )
    prob_far = jnp.einsum(
        "dbqhe,dkhe->dbhqk", grad_heads, far_v, preferred_element_type=jnp.float32
    )
    row_dot = jnp.sum(weight_near * prob_near, axis=-1, keepdims=True) + jnp.sum(
        weight_far * prob_far, axis=-1, keepdims=True
    )
    grad_near = (weight_near * (prob_near - row_dot)).astype(jnp.bfloat16)
    grad_far = (weight_far * (prob_far - row_dot)).astype(jnp.bfloat16)
    query_sum = jnp.einsum(
        "dbhqk,dbkhe->dbqhe", grad_near, near_k, preferred_element_type=jnp.float32
    )
    query_sum = query_sum + jnp.einsum(
        "dbhqk,dkhe->dbqhe", grad_far, far_k, preferred_element_type=jnp.float32
    )
    query_grad = (
        (query_sum * score_scale).reshape(doc_count, tok_count, head_cols).astype(jnp.bfloat16)
    )
    near_key_rows = (
        jnp.einsum("dbhqk,dbqhe->dbkhe", grad_near, query_heads, preferred_element_type=jnp.float32)
        * score_scale
    )
    near_value_rows = jnp.einsum(
        "dbhqk,dbqhe->dbkhe", rounded_near, grad_heads, preferred_element_type=jnp.float32
    )
    far_key_rows = (
        jnp.einsum("dbhqk,dbqhe->dkhe", grad_far, query_heads, preferred_element_type=jnp.float32)
        * score_scale
    )
    far_value_rows = jnp.einsum(
        "dbhqk,dbqhe->dkhe", rounded_far, grad_heads, preferred_element_type=jnp.float32
    )
    near_rows = jnp.stack([near_key_rows, near_value_rows]).reshape(
        2, doc_count, 2, NEAR + 1, block, head_cols
    )
    back_six = jax.vmap(place_blocks, in_axes=(1, 0), out_axes=1)(near_rows, chosen)
    rims = jnp.concatenate([back_six[:, :, 0:2], back_six[:, :, 4:6]], axis=2).reshape(
        2, doc_count, 2 * tok_count, head_cols
    )
    beside_all = extended(rims.astype(jnp.bfloat16), (("seq", 2),), tok_count).astype(
        jnp.float32
    )
    token_grad = back_six[:, :, 2:4].reshape(2, doc_count, tok_count, head_cols)
    token_grad = token_grad + beside_all[:, :, :tok_count] + beside_all[:, :, 3 * tok_count :]
    far_rows = jnp.stack([far_key_rows, far_value_rows]).reshape(
        2, doc_count, levels, block, head_cols
    )
    carried = jnp.zeros((2, doc_count, block, head_cols), jnp.float32)
    for level_no in reversed(range(levels)):
        message = far_rows[:, :, level_no]
        mine = jnp.zeros_like(message)
        if level_no + 1 < levels:
            upper = position >> level_no & 1 == 1
            spread = jnp.repeat(carried, 2, axis=2) * 0.5
            lower_half = spread[:, :, :block]
            upper_half = spread[:, :, block:]
            mine = jnp.where(upper, upper_half, lower_half)
            message = message + jnp.where(upper, lower_half, upper_half)
        returned = swapped(message.astype(jnp.bfloat16), "seq", level_no).astype(jnp.float32)
        carried = returned + mine
    token_grad = token_grad + jnp.repeat(carried, 2, axis=2) * 0.5
    key_grad = token_grad[0].astype(jnp.bfloat16)
    value_grad = token_grad[1].astype(jnp.bfloat16)
    return (attention, query_grad, key_grad, value_grad, weight_grad)


def solution(mesh):
    in_specs = (
        P(("groups", "dp"), "seq", "head"),
        P(("groups", "dp"), "seq", "head"),
        P(("groups", "dp"), "seq", "head"),
        P(("groups", "dp"), "seq", None),
        P("seq", "head"),
        P(("groups", "dp"), "seq", None),
    )
    out_specs = (
        P(("groups", "dp"), "seq", "head"),
        P(("groups", "dp"), "seq", "head"),
        P(("groups", "dp"), "seq", "head"),
        P(("groups", "dp"), "seq", "head"),
        P(("groups", "seq"), "head"),
    )
    return jax.shard_map(shards, mesh=mesh, in_specs=in_specs, out_specs=out_specs, check_vma=False)
```

```python
import math

import jax
import jax.numpy as jnp
from jax import lax
from jax.sharding import PartitionSpec as P

HEAD_DIM = 128
NEAR = 2


def extended(cells, sides, width):
    for axis, dim in sides:
        count = lax.axis_size(axis)
        ends = count - 1
        head = lax.slice_in_dim(cells, 0, width, axis=dim)
        tail = lax.slice_in_dim(cells, cells.shape[dim] - width, cells.shape[dim], axis=dim)
        cells = jnp.concatenate(
            [
                lax.ppermute(tail, axis, [(i, (i + 1) % count) for i in range(ends)]),
                cells,
                lax.ppermute(head, axis, [((i + 1) % count, i) for i in range(ends)]),
            ],
            axis=dim,
        )
    return cells


def swapped(shard, axis, stride):
    return lax.ppermute(shard, axis, [(i, i ^ 1 << stride) for i in range(lax.axis_size(axis))])


def pool_pairs(source):
    shaped = source.reshape(
        source.shape[0], source.shape[1], source.shape[2] // 2, 2, source.shape[3]
    )
    return jnp.sum(shaped, axis=3) * 0.5


def pick_blocks(blocks_doc, chosen_doc):
    return blocks_doc[:, chosen_doc]


def place_blocks(grad_doc, chosen_doc):
    holder = jnp.zeros((grad_doc.shape[0], 6, grad_doc.shape[3], grad_doc.shape[4]), jnp.float32)
    return holder.at[:, chosen_doc].add(grad_doc)


def shards(queries, keys, values, pattern, out_weight, cotangent):
    doc_count, tok_count, head_cols = queries.shape
    block = tok_count // 2
    heads = head_cols // HEAD_DIM
    seq_count = lax.axis_size("seq")
    levels = seq_count.bit_length() - 1
    position = lax.axis_index("seq")
    score_scale = 1.0 / math.sqrt(HEAD_DIM)
    near_width = (NEAR + 1) * block
    key_value = jnp.stack([keys, values])
    padded = extended(key_value, (("seq", 2),), tok_count)
    blocks_six = padded.reshape(2, doc_count, 6, block, head_cols)
    local_ids = jnp.arange(2, dtype=jnp.int32)[None, :, None]
    chosen = jnp.concatenate([local_ids, local_ids + pattern], axis=2) + 2
    near_pair = jax.vmap(pick_blocks, in_axes=(1, 0), out_axes=1)(blocks_six, chosen)
    near_pair = near_pair.reshape(2, doc_count, 2, near_width, head_cols)
    pieces = []
    level_rows = key_value.astype(jnp.float32)
    for level_no in range(levels):
        level_rows = pool_pairs(level_rows)
        pieces.append(level_rows.astype(jnp.bfloat16))
    feat_count = cotangent.shape[2] // seq_count
    cot_rows = cotangent.reshape(doc_count * tok_count, cotangent.shape[2])
    cot_height = doc_count * tok_count
    far_parts = []
    got_list = []
    for step in range(1, seq_count):
        pairs = [(i, i ^ step) for i in range(seq_count)]
        piece = pieces[step.bit_length() - 1]
        sent = lax.dynamic_slice_in_dim(
            cot_rows, (position ^ step) * feat_count, feat_count, axis=1
        )
        if feat_count == head_cols:
            payload = jnp.concatenate([sent, piece.reshape(-1, head_cols)], axis=0)
            arrived = lax.ppermute(payload, "seq", pairs)
            got = arrived[:cot_height]
            far_parts.append(arrived[cot_height:].reshape(piece.shape))
        else:
            got = lax.ppermute(sent, "seq", pairs)
            far_parts.append(lax.ppermute(piece, "seq", pairs))
        got_list.append(got)
    far_pair = jnp.concatenate(far_parts, axis=2)
    query_heads = queries.reshape(doc_count, 2, block, heads, HEAD_DIM)
    near_k = near_pair[0].reshape(doc_count, 2, near_width, heads, HEAD_DIM)
    near_v = near_pair[1].reshape(doc_count, 2, near_width, heads, HEAD_DIM)
    far_k = far_pair[0].reshape(doc_count, levels * block, heads, HEAD_DIM)
    far_v = far_pair[1].reshape(doc_count, levels * block, heads, HEAD_DIM)
    score_near = (
        jnp.einsum("dbqhe,dbkhe->dbhqk", query_heads, near_k, preferred_element_type=jnp.float32)
        * score_scale
    )
    score_far = (
        jnp.einsum("dbqhe,dkhe->dbhqk", query_heads, far_k, preferred_element_type=jnp.float32)
        * score_scale
    )
    top = jnp.maximum(
        jnp.max(score_near, axis=-1, keepdims=True), jnp.max(score_far, axis=-1, keepdims=True)
    )
    exp_near = jnp.exp(score_near - top)
    exp_far = jnp.exp(score_far - top)
    total = jnp.sum(exp_near, axis=-1, keepdims=True) + jnp.sum(exp_far, axis=-1, keepdims=True)
    weight_near = exp_near / total
    weight_far = exp_far / total
    rounded_near = weight_near.astype(jnp.bfloat16)
    rounded_far = weight_far.astype(jnp.bfloat16)
    output = jnp.einsum(
        "dbhqk,dbkhe->dbqhe", rounded_near, near_v, preferred_element_type=jnp.float32
    )
    output = output + jnp.einsum(
        "dbhqk,dkhe->dbqhe", rounded_far, far_v, preferred_element_type=jnp.float32
    )
    attention = output.reshape(doc_count, tok_count, head_cols).astype(jnp.bfloat16)
    out_rows = attention.reshape(doc_count * tok_count, head_cols)
    own_cols = lax.dynamic_slice_in_dim(cot_rows, position * feat_count, feat_count, axis=1)
    grad_sum = jnp.dot(own_cols, out_weight, preferred_element_type=jnp.float32)
    feat_list = [own_cols]
    out_list = [out_rows]
    for step in range(1, seq_count):
        pairs = [(i, i ^ step) for i in range(seq_count)]
        got = got_list[step - 1]
        part = jnp.dot(got, out_weight, preferred_element_type=jnp.float32)
        back = lax.ppermute(part.astype(jnp.bfloat16), "seq", pairs)
        grad_sum = grad_sum + back.astype(jnp.float32)
        feat_list.append(got)
        out_list.append(lax.ppermute(out_rows, "seq", pairs))
    attn_grad = grad_sum.astype(jnp.bfloat16)
    feat_docs = jnp.concatenate(feat_list, axis=0)
    whole_output = jnp.concatenate(out_list, axis=0)
    dp_count = lax.axis_size("dp")
    if dp_count == 2:
        feat_docs = jnp.concatenate([feat_docs, swapped(feat_docs, "dp", 0)], axis=0)
        whole_output = jnp.concatenate([whole_output, swapped(whole_output, "dp", 0)], axis=0)
    else:
        feat_docs = lax.all_gather(feat_docs, "dp", axis=0, tiled=True)
        whole_output = lax.all_gather(whole_output, "dp", axis=0, tiled=True)
    weight_grad = jnp.einsum(
        "tc,tw->cw", feat_docs, whole_output, preferred_element_type=jnp.float32
    )
    grad_heads = attn_grad.reshape(doc_count, 2, block, heads, HEAD_DIM)
    prob_near = jnp.einsum(
        "dbqhe,dbkhe->dbhqk", grad_heads, near_v, preferred_element_type=jnp.float32
    )
    prob_far = jnp.einsum(
        "dbqhe,dkhe->dbhqk", grad_heads, far_v, preferred_element_type=jnp.float32
    )
    row_dot = jnp.sum(weight_near * prob_near, axis=-1, keepdims=True) + jnp.sum(
        weight_far * prob_far, axis=-1, keepdims=True
    )
    grad_near = (weight_near * (prob_near - row_dot)).astype(jnp.bfloat16)
    grad_far = (weight_far * (prob_far - row_dot)).astype(jnp.bfloat16)
    query_sum = jnp.einsum(
        "dbhqk,dbkhe->dbqhe", grad_near, near_k, preferred_element_type=jnp.float32
    )
    query_sum = query_sum + jnp.einsum(
        "dbhqk,dkhe->dbqhe", grad_far, far_k, preferred_element_type=jnp.float32
    )
    query_grad = (
        (query_sum * score_scale).reshape(doc_count, tok_count, head_cols).astype(jnp.bfloat16)
    )
    near_key_rows = (
        jnp.einsum("dbhqk,dbqhe->dbkhe", grad_near, query_heads, preferred_element_type=jnp.float32)
        * score_scale
    )
    near_value_rows = jnp.einsum(
        "dbhqk,dbqhe->dbkhe", rounded_near, grad_heads, preferred_element_type=jnp.float32
    )
    far_key_rows = (
        jnp.einsum("dbhqk,dbqhe->dkhe", grad_far, query_heads, preferred_element_type=jnp.float32)
        * score_scale
    )
    far_value_rows = jnp.einsum(
        "dbhqk,dbqhe->dkhe", rounded_far, grad_heads, preferred_element_type=jnp.float32
    )
    near_rows = jnp.stack([near_key_rows, near_value_rows]).reshape(
        2, doc_count, 2, NEAR + 1, block, head_cols
    )
    back_six = jax.vmap(place_blocks, in_axes=(1, 0), out_axes=1)(near_rows, chosen)
    rims = jnp.concatenate([back_six[:, :, 0:2], back_six[:, :, 4:6]], axis=2).reshape(
        2, doc_count, 2 * tok_count, head_cols
    )
    beside_all = extended(rims.astype(jnp.bfloat16), (("seq", 2),), tok_count).astype(
        jnp.float32
    )
    token_grad = back_six[:, :, 2:4].reshape(2, doc_count, tok_count, head_cols)
    token_grad = token_grad + beside_all[:, :, :tok_count] + beside_all[:, :, 3 * tok_count :]
    far_rows = jnp.stack([far_key_rows, far_value_rows]).reshape(
        2, doc_count, levels * block, head_cols
    )
    level_sums = [None] * levels
    offset = 0
    for step in range(1, seq_count):
        level_no = step.bit_length() - 1
        height = pieces[level_no].shape[2]
        segment = lax.slice_in_dim(far_rows, offset, offset + height, axis=2)
        offset += height
        returned = lax.ppermute(
            segment.astype(jnp.bfloat16), "seq", [(i, i ^ step) for i in range(seq_count)]
        ).astype(jnp.float32)
        if level_sums[level_no] is None:
            level_sums[level_no] = returned
        else:
            level_sums[level_no] = level_sums[level_no] + returned
    for level_no in range(levels):
        spread = 2 ** (level_no + 1)
        token_grad = token_grad + jnp.repeat(level_sums[level_no], spread, axis=2) / float(spread)
    key_grad = token_grad[0].astype(jnp.bfloat16)
    value_grad = token_grad[1].astype(jnp.bfloat16)
    return (attention, query_grad, key_grad, value_grad, weight_grad)


def solution(mesh):
    in_specs = (
        P(("groups", "dp"), "seq", "head"),
        P(("groups", "dp"), "seq", "head"),
        P(("groups", "dp"), "seq", "head"),
        P(("groups", "dp"), "seq", None),
        P("seq", "head"),
        P(("groups", "dp"), "seq", None),
    )
    out_specs = (
        P(("groups", "dp"), "seq", "head"),
        P(("groups", "dp"), "seq", "head"),
        P(("groups", "dp"), "seq", "head"),
        P(("groups", "dp"), "seq", "head"),
        P(("groups", "seq"), "head"),
    )
    return jax.shard_map(shards, mesh=mesh, in_specs=in_specs, out_specs=out_specs, check_vma=False)
```

```python
import math

import jax
import jax.numpy as jnp
from jax import lax
from jax.sharding import PartitionSpec as P

HEAD_DIM = 128
NEAR = 2


def extended(cells, sides, width):
    for axis, dim in sides:
        count = lax.axis_size(axis)
        ends = count - 1
        head = lax.slice_in_dim(cells, 0, width, axis=dim)
        tail = lax.slice_in_dim(cells, cells.shape[dim] - width, cells.shape[dim], axis=dim)
        cells = jnp.concatenate(
            [
                lax.ppermute(tail, axis, [(i, (i + 1) % count) for i in range(ends)]),
                cells,
                lax.ppermute(head, axis, [((i + 1) % count, i) for i in range(ends)]),
            ],
            axis=dim,
        )
    return cells


def swapped(shard, axis, stride):
    return lax.ppermute(shard, axis, [(i, i ^ 1 << stride) for i in range(lax.axis_size(axis))])


def pool_pairs(source):
    shaped = source.reshape(
        source.shape[0], source.shape[1], source.shape[2] // 2, 2, source.shape[3]
    )
    return jnp.sum(shaped, axis=3) * 0.5


def pick_blocks(blocks_doc, chosen_doc):
    return blocks_doc[:, chosen_doc]


def place_blocks(grad_doc, chosen_doc):
    holder = jnp.zeros((grad_doc.shape[0], 6, grad_doc.shape[3], grad_doc.shape[4]), jnp.float32)
    return holder.at[:, chosen_doc].add(grad_doc)


def shards(queries, keys, values, pattern, out_weight, cotangent):
    doc_count, tok_count, head_cols = queries.shape
    block = tok_count // 2
    heads = head_cols // HEAD_DIM
    seq_count = lax.axis_size("seq")
    levels = seq_count.bit_length() - 1
    position = lax.axis_index("seq")
    score_scale = 1.0 / math.sqrt(HEAD_DIM)
    near_width = (NEAR + 1) * block
    key_value = jnp.stack([keys, values])
    padded = extended(key_value, (("seq", 2),), tok_count)
    blocks_six = padded.reshape(2, doc_count, 6, block, head_cols)
    local_ids = jnp.arange(2, dtype=jnp.int32)[None, :, None]
    chosen = jnp.concatenate([local_ids, local_ids + pattern], axis=2) + 2
    near_pair = jax.vmap(pick_blocks, in_axes=(1, 0), out_axes=1)(blocks_six, chosen)
    near_pair = near_pair.reshape(2, doc_count, 2, near_width, head_cols)
    pieces = []
    level_rows = key_value.astype(jnp.float32)
    for level_no in range(levels):
        level_rows = pool_pairs(level_rows)
        pieces.append(level_rows.astype(jnp.bfloat16))
    feat_count = cotangent.shape[2] // seq_count
    cot_rows = cotangent.reshape(doc_count * tok_count, cotangent.shape[2])
    cot_height = doc_count * tok_count
    far_parts = []
    got_list = []
    for step in range(1, seq_count):
        pairs = [(i, i ^ step) for i in range(seq_count)]
        piece = pieces[step.bit_length() - 1]
        sent = lax.dynamic_slice_in_dim(
            cot_rows, (position ^ step) * feat_count, feat_count, axis=1
        )
        if feat_count == head_cols:
            payload = jnp.concatenate([sent, piece.reshape(-1, head_cols)], axis=0)
            arrived = lax.ppermute(payload, "seq", pairs)
            got = arrived[:cot_height]
            far_parts.append(arrived[cot_height:].reshape(piece.shape))
        else:
            got = lax.ppermute(sent, "seq", pairs)
            far_parts.append(lax.ppermute(piece, "seq", pairs))
        got_list.append(got)
    far_levels = []
    for level_no in range(levels):
        count = 1 << level_no
        group = jnp.stack(far_parts[count - 1 : 2 * count - 1], axis=0)
        order = jnp.arange(count, dtype=jnp.int32) ^ (position & (count - 1))
        group = jnp.take(group, order, axis=0)
        far_levels.append(
            jnp.moveaxis(group, 0, 2).reshape(2, doc_count, count * group.shape[3], head_cols)
        )
    far_pair = jnp.concatenate(far_levels, axis=2)
    query_heads = queries.reshape(doc_count, 2, block, heads, HEAD_DIM)
    near_k = near_pair[0].reshape(doc_count, 2, near_width, heads, HEAD_DIM)
    near_v = near_pair[1].reshape(doc_count, 2, near_width, heads, HEAD_DIM)
    far_k = far_pair[0].reshape(doc_count, levels * block, heads, HEAD_DIM)
    far_v = far_pair[1].reshape(doc_count, levels * block, heads, HEAD_DIM)
    score_near = (
        jnp.einsum("dbqhe,dbkhe->dbhqk", query_heads, near_k, preferred_element_type=jnp.float32)
        * score_scale
    )
    score_far = (
        jnp.einsum("dbqhe,dkhe->dbhqk", query_heads, far_k, preferred_element_type=jnp.float32)
        * score_scale
    )
    top = jnp.maximum(
        jnp.max(score_near, axis=-1, keepdims=True), jnp.max(score_far, axis=-1, keepdims=True)
    )
    exp_near = jnp.exp(score_near - top)
    exp_far = jnp.exp(score_far - top)
    total = jnp.sum(exp_near, axis=-1, keepdims=True) + jnp.sum(exp_far, axis=-1, keepdims=True)
    weight_near = exp_near / total
    weight_far = exp_far / total
    rounded_near = weight_near.astype(jnp.bfloat16)
    rounded_far = weight_far.astype(jnp.bfloat16)
    output = jnp.einsum(
        "dbhqk,dbkhe->dbqhe", rounded_near, near_v, preferred_element_type=jnp.float32
    )
    output = output + jnp.einsum(
        "dbhqk,dkhe->dbqhe", rounded_far, far_v, preferred_element_type=jnp.float32
    )
    attention = output.reshape(doc_count, tok_count, head_cols).astype(jnp.bfloat16)
    out_rows = attention.reshape(doc_count * tok_count, head_cols)
    own_cols = lax.dynamic_slice_in_dim(cot_rows, position * feat_count, feat_count, axis=1)
    grad_sum = jnp.dot(own_cols, out_weight, preferred_element_type=jnp.float32)
    feat_list = [own_cols]
    out_list = [out_rows]
    for step in range(1, seq_count):
        pairs = [(i, i ^ step) for i in range(seq_count)]
        got = got_list[step - 1]
        part = jnp.dot(got, out_weight, preferred_element_type=jnp.float32)
        back = lax.ppermute(part.astype(jnp.bfloat16), "seq", pairs)
        grad_sum = grad_sum + back.astype(jnp.float32)
        feat_list.append(got)
        out_list.append(lax.ppermute(out_rows, "seq", pairs))
    attn_grad = grad_sum.astype(jnp.bfloat16)
    feat_docs = jnp.concatenate(feat_list, axis=0)
    whole_output = jnp.concatenate(out_list, axis=0)
    dp_count = lax.axis_size("dp")
    if dp_count == 2:
        feat_docs = jnp.concatenate([feat_docs, swapped(feat_docs, "dp", 0)], axis=0)
        whole_output = jnp.concatenate([whole_output, swapped(whole_output, "dp", 0)], axis=0)
    else:
        feat_docs = lax.all_gather(feat_docs, "dp", axis=0, tiled=True)
        whole_output = lax.all_gather(whole_output, "dp", axis=0, tiled=True)
    weight_grad = jnp.einsum(
        "tc,tw->cw", feat_docs, whole_output, preferred_element_type=jnp.float32
    )
    grad_heads = attn_grad.reshape(doc_count, 2, block, heads, HEAD_DIM)
    prob_near = jnp.einsum(
        "dbqhe,dbkhe->dbhqk", grad_heads, near_v, preferred_element_type=jnp.float32
    )
    prob_far = jnp.einsum(
        "dbqhe,dkhe->dbhqk", grad_heads, far_v, preferred_element_type=jnp.float32
    )
    row_dot = jnp.sum(weight_near * prob_near, axis=-1, keepdims=True) + jnp.sum(
        weight_far * prob_far, axis=-1, keepdims=True
    )
    grad_near = (weight_near * (prob_near - row_dot)).astype(jnp.bfloat16)
    grad_far = (weight_far * (prob_far - row_dot)).astype(jnp.bfloat16)
    query_sum = jnp.einsum(
        "dbhqk,dbkhe->dbqhe", grad_near, near_k, preferred_element_type=jnp.float32
    )
    query_sum = query_sum + jnp.einsum(
        "dbhqk,dkhe->dbqhe", grad_far, far_k, preferred_element_type=jnp.float32
    )
    query_grad = (
        (query_sum * score_scale).reshape(doc_count, tok_count, head_cols).astype(jnp.bfloat16)
    )
    near_key_rows = (
        jnp.einsum("dbhqk,dbqhe->dbkhe", grad_near, query_heads, preferred_element_type=jnp.float32)
        * score_scale
    )
    near_value_rows = jnp.einsum(
        "dbhqk,dbqhe->dbkhe", rounded_near, grad_heads, preferred_element_type=jnp.float32
    )
    far_key_rows = (
        jnp.einsum("dbhqk,dbqhe->dkhe", grad_far, query_heads, preferred_element_type=jnp.float32)
        * score_scale
    )
    far_value_rows = jnp.einsum(
        "dbhqk,dbqhe->dkhe", rounded_far, grad_heads, preferred_element_type=jnp.float32
    )
    near_rows = jnp.stack([near_key_rows, near_value_rows]).reshape(
        2, doc_count, 2, NEAR + 1, block, head_cols
    )
    back_six = jax.vmap(place_blocks, in_axes=(1, 0), out_axes=1)(near_rows, chosen)
    rims = jnp.concatenate([back_six[:, :, 0:2], back_six[:, :, 4:6]], axis=2).reshape(
        2, doc_count, 2 * tok_count, head_cols
    )
    beside_all = extended(rims.astype(jnp.bfloat16), (("seq", 2),), tok_count).astype(
        jnp.float32
    )
    token_grad = back_six[:, :, 2:4].reshape(2, doc_count, tok_count, head_cols)
    token_grad = token_grad + beside_all[:, :, :tok_count] + beside_all[:, :, 3 * tok_count :]
    far_rows = jnp.stack([far_key_rows, far_value_rows]).reshape(
        2, doc_count, levels * block, head_cols
    )
    far_rows = far_rows.reshape(2, doc_count, levels, block, head_cols)
    carried = jnp.zeros((2, doc_count, block, head_cols), jnp.float32)
    for level_no in reversed(range(levels)):
        message = far_rows[:, :, level_no]
        mine = jnp.zeros_like(message)
        if level_no + 1 < levels:
            upper = position >> level_no & 1 == 1
            spread = jnp.repeat(carried, 2, axis=2) * 0.5
            lower_half = spread[:, :, :block]
            upper_half = spread[:, :, block:]
            mine = jnp.where(upper, upper_half, lower_half)
            message = message + jnp.where(upper, lower_half, upper_half)
        returned = swapped(message.astype(jnp.bfloat16), "seq", level_no).astype(jnp.float32)
        carried = returned + mine
    token_grad = token_grad + jnp.repeat(carried, 2, axis=2) * 0.5
    key_grad = token_grad[0].astype(jnp.bfloat16)
    value_grad = token_grad[1].astype(jnp.bfloat16)
    return (attention, query_grad, key_grad, value_grad, weight_grad)


def solution(mesh):
    in_specs = (
        P(("groups", "dp"), "seq", "head"),
        P(("groups", "dp"), "seq", "head"),
        P(("groups", "dp"), "seq", "head"),
        P(("groups", "dp"), "seq", None),
        P("seq", "head"),
        P(("groups", "dp"), "seq", None),
    )
    out_specs = (
        P(("groups", "dp"), "seq", "head"),
        P(("groups", "dp"), "seq", "head"),
        P(("groups", "dp"), "seq", "head"),
        P(("groups", "dp"), "seq", "head"),
        P(("groups", "seq"), "head"),
    )
    return jax.shard_map(shards, mesh=mesh, in_specs=in_specs, out_specs=out_specs, check_vma=False)
```

```python
import math

import jax
import jax.numpy as jnp
from jax import lax
from jax.sharding import PartitionSpec as P

HEAD_DIM = 128
NEAR = 2


def extended(cells, sides, width):
    for axis, dim in sides:
        count = lax.axis_size(axis)
        ends = count - 1
        head = lax.slice_in_dim(cells, 0, width, axis=dim)
        tail = lax.slice_in_dim(cells, cells.shape[dim] - width, cells.shape[dim], axis=dim)
        cells = jnp.concatenate(
            [
                lax.ppermute(tail, axis, [(i, (i + 1) % count) for i in range(ends)]),
                cells,
                lax.ppermute(head, axis, [((i + 1) % count, i) for i in range(ends)]),
            ],
            axis=dim,
        )
    return cells


def swapped(shard, axis, stride):
    return lax.ppermute(shard, axis, [(i, i ^ 1 << stride) for i in range(lax.axis_size(axis))])


def pool_pairs(source):
    shaped = source.reshape(
        source.shape[0], source.shape[1], source.shape[2] // 2, 2, source.shape[3]
    )
    return jnp.sum(shaped, axis=3) * 0.5


def pick_blocks(blocks_doc, chosen_doc):
    return blocks_doc[:, chosen_doc]


def place_blocks(grad_doc, chosen_doc):
    holder = jnp.zeros((grad_doc.shape[0], 6, grad_doc.shape[3], grad_doc.shape[4]), jnp.float32)
    return holder.at[:, chosen_doc].add(grad_doc)


def shards(queries, keys, values, pattern, out_weight, cotangent):
    doc_count, tok_count, head_cols = queries.shape
    block = tok_count // 2
    heads = head_cols // HEAD_DIM
    seq_count = lax.axis_size("seq")
    levels = seq_count.bit_length() - 1
    position = lax.axis_index("seq")
    score_scale = 1.0 / math.sqrt(HEAD_DIM)
    near_width = (NEAR + 1) * block
    key_value = jnp.stack([keys, values])
    padded = extended(key_value, (("seq", 2),), tok_count)
    blocks_six = padded.reshape(2, doc_count, 6, block, head_cols)
    local_ids = jnp.arange(2, dtype=jnp.int32)[None, :, None]
    chosen = jnp.concatenate([local_ids, local_ids + pattern], axis=2) + 2
    near_pair = jax.vmap(pick_blocks, in_axes=(1, 0), out_axes=1)(blocks_six, chosen)
    near_pair = near_pair.reshape(2, doc_count, 2, near_width, head_cols)
    pooled = pool_pairs(key_value.astype(jnp.float32))
    siblings = []
    own_level = pooled
    for level_no in range(levels):
        other = swapped(own_level, "seq", level_no)
        siblings.append(other)
        if level_no + 1 < levels:
            upper = position >> level_no & 1 == 1
            joined = jnp.where(
                upper,
                jnp.concatenate([other, own_level], axis=2),
                jnp.concatenate([own_level, other], axis=2),
            )
            own_level = pool_pairs(joined)
    far_pair = jnp.concatenate(siblings, axis=2).astype(jnp.bfloat16)
    cot_rows, near_pair, far_pair = lax.optimization_barrier(
        (cotangent.reshape(doc_count * tok_count, cotangent.shape[2]), near_pair, far_pair)
    )
    query_heads = queries.reshape(doc_count, 2, block, heads, HEAD_DIM)
    near_k = near_pair[0].reshape(doc_count, 2, near_width, heads, HEAD_DIM)
    near_v = near_pair[1].reshape(doc_count, 2, near_width, heads, HEAD_DIM)
    far_k = far_pair[0].reshape(doc_count, levels * block, heads, HEAD_DIM)
    far_v = far_pair[1].reshape(doc_count, levels * block, heads, HEAD_DIM)
    score_near = (
        jnp.einsum("dbqhe,dbkhe->dbhqk", query_heads, near_k, preferred_element_type=jnp.float32)
        * score_scale
    )
    score_far = (
        jnp.einsum("dbqhe,dkhe->dbhqk", query_heads, far_k, preferred_element_type=jnp.float32)
        * score_scale
    )
    top = jnp.maximum(
        jnp.max(score_near, axis=-1, keepdims=True), jnp.max(score_far, axis=-1, keepdims=True)
    )
    exp_near = jnp.exp(score_near - top)
    exp_far = jnp.exp(score_far - top)
    total = jnp.sum(exp_near, axis=-1, keepdims=True) + jnp.sum(exp_far, axis=-1, keepdims=True)
    weight_near = exp_near / total
    weight_far = exp_far / total
    rounded_near = weight_near.astype(jnp.bfloat16)
    rounded_far = weight_far.astype(jnp.bfloat16)
    output = jnp.einsum(
        "dbhqk,dbkhe->dbqhe", rounded_near, near_v, preferred_element_type=jnp.float32
    )
    output = output + jnp.einsum(
        "dbhqk,dkhe->dbqhe", rounded_far, far_v, preferred_element_type=jnp.float32
    )
    attention = output.reshape(doc_count, tok_count, head_cols).astype(jnp.bfloat16)
    feat_count = cotangent.shape[2] // seq_count
    out_rows = attention.reshape(doc_count * tok_count, head_cols)
    own_cols = lax.dynamic_slice_in_dim(cot_rows, position * feat_count, feat_count, axis=1)
    grad_sum = jnp.dot(own_cols, out_weight, preferred_element_type=jnp.float32)
    feat_list = [own_cols]
    out_list = [out_rows]
    for step in range(1, seq_count):
        pairs = [(i, i ^ step) for i in range(seq_count)]
        sent = lax.dynamic_slice_in_dim(
            cot_rows, (position ^ step) * feat_count, feat_count, axis=1
        )
        got = lax.ppermute(sent, "seq", pairs)
        part = jnp.dot(got, out_weight, preferred_element_type=jnp.float32)
        back = lax.ppermute(part.astype(jnp.bfloat16), "seq", pairs)
        grad_sum = grad_sum + back.astype(jnp.float32)
        feat_list.append(got)
        out_list.append(lax.ppermute(out_rows, "seq", pairs))
    attn_grad = grad_sum.astype(jnp.bfloat16)
    feat_docs = jnp.concatenate(feat_list, axis=0)
    whole_output = jnp.concatenate(out_list, axis=0)
    dp_count = lax.axis_size("dp")
    if dp_count == 2:
        feat_docs = jnp.concatenate([feat_docs, swapped(feat_docs, "dp", 0)], axis=0)
        whole_output = jnp.concatenate([whole_output, swapped(whole_output, "dp", 0)], axis=0)
    else:
        feat_docs = lax.all_gather(feat_docs, "dp", axis=0, tiled=True)
        whole_output = lax.all_gather(whole_output, "dp", axis=0, tiled=True)
    weight_grad = jnp.einsum(
        "tc,tw->cw", feat_docs, whole_output, preferred_element_type=jnp.float32
    )
    grad_heads = attn_grad.reshape(doc_count, 2, block, heads, HEAD_DIM)
    prob_near = jnp.einsum(
        "dbqhe,dbkhe->dbhqk", grad_heads, near_v, preferred_element_type=jnp.float32
    )
    prob_far = jnp.einsum(
        "dbqhe,dkhe->dbhqk", grad_heads, far_v, preferred_element_type=jnp.float32
    )
    row_dot = jnp.sum(weight_near * prob_near, axis=-1, keepdims=True) + jnp.sum(
        weight_far * prob_far, axis=-1, keepdims=True
    )
    grad_near = (weight_near * (prob_near - row_dot)).astype(jnp.bfloat16)
    grad_far = (weight_far * (prob_far - row_dot)).astype(jnp.bfloat16)
    query_sum = jnp.einsum(
        "dbhqk,dbkhe->dbqhe", grad_near, near_k, preferred_element_type=jnp.float32
    )
    query_sum = query_sum + jnp.einsum(
        "dbhqk,dkhe->dbqhe", grad_far, far_k, preferred_element_type=jnp.float32
    )
    query_grad = (
        (query_sum * score_scale).reshape(doc_count, tok_count, head_cols).astype(jnp.bfloat16)
    )
    near_key_rows = (
        jnp.einsum("dbhqk,dbqhe->dbkhe", grad_near, query_heads, preferred_element_type=jnp.float32)
        * score_scale
    )
    near_value_rows = jnp.einsum(
        "dbhqk,dbqhe->dbkhe", rounded_near, grad_heads, preferred_element_type=jnp.float32
    )
    far_key_rows = (
        jnp.einsum("dbhqk,dbqhe->dkhe", grad_far, query_heads, preferred_element_type=jnp.float32)
        * score_scale
    )
    far_value_rows = jnp.einsum(
        "dbhqk,dbqhe->dkhe", rounded_far, grad_heads, preferred_element_type=jnp.float32
    )
    near_rows = jnp.stack([near_key_rows, near_value_rows]).reshape(
        2, doc_count, 2, NEAR + 1, block, head_cols
    )
    back_six = jax.vmap(place_blocks, in_axes=(1, 0), out_axes=1)(near_rows, chosen)
    rims = jnp.concatenate([back_six[:, :, 0:2], back_six[:, :, 4:6]], axis=2).reshape(
        2, doc_count, 2 * tok_count, head_cols
    )
    beside_all = extended(rims.astype(jnp.bfloat16), (("seq", 2),), tok_count).astype(
        jnp.float32
    )
    token_grad = back_six[:, :, 2:4].reshape(2, doc_count, tok_count, head_cols)
    token_grad = token_grad + beside_all[:, :, :tok_count] + beside_all[:, :, 3 * tok_count :]
    far_rows = jnp.stack([far_key_rows, far_value_rows]).reshape(
        2, doc_count, levels, block, head_cols
    )
    carried = jnp.zeros((2, doc_count, block, head_cols), jnp.float32)
    for level_no in reversed(range(levels)):
        message = far_rows[:, :, level_no]
        mine = jnp.zeros_like(message)
        if level_no + 1 < levels:
            upper = position >> level_no & 1 == 1
            spread = jnp.repeat(carried, 2, axis=2) * 0.5
            lower_half = spread[:, :, :block]
            upper_half = spread[:, :, block:]
            mine = jnp.where(upper, upper_half, lower_half)
            message = message + jnp.where(upper, lower_half, upper_half)
        returned = swapped(message.astype(jnp.bfloat16), "seq", level_no).astype(jnp.float32)
        carried = returned + mine
    token_grad = token_grad + jnp.repeat(carried, 2, axis=2) * 0.5
    key_grad = token_grad[0].astype(jnp.bfloat16)
    value_grad = token_grad[1].astype(jnp.bfloat16)
    return (attention, query_grad, key_grad, value_grad, weight_grad)


def solution(mesh):
    in_specs = (
        P(("groups", "dp"), "seq", "head"),
        P(("groups", "dp"), "seq", "head"),
        P(("groups", "dp"), "seq", "head"),
        P(("groups", "dp"), "seq", None),
        P("seq", "head"),
        P(("groups", "dp"), "seq", None),
    )
    out_specs = (
        P(("groups", "dp"), "seq", "head"),
        P(("groups", "dp"), "seq", "head"),
        P(("groups", "dp"), "seq", "head"),
        P(("groups", "dp"), "seq", "head"),
        P(("groups", "seq"), "head"),
    )
    return jax.shard_map(shards, mesh=mesh, in_specs=in_specs, out_specs=out_specs, check_vma=False)
```

```python
import math

import jax
import jax.numpy as jnp
from jax import lax
from jax.sharding import PartitionSpec as P

HEAD_DIM = 128
NEAR = 2


def extended(cells, sides, width):
    for axis, dim in sides:
        count = lax.axis_size(axis)
        ends = count - 1
        head = lax.slice_in_dim(cells, 0, width, axis=dim)
        tail = lax.slice_in_dim(cells, cells.shape[dim] - width, cells.shape[dim], axis=dim)
        cells = jnp.concatenate(
            [
                lax.ppermute(tail, axis, [(i, (i + 1) % count) for i in range(ends)]),
                cells,
                lax.ppermute(head, axis, [((i + 1) % count, i) for i in range(ends)]),
            ],
            axis=dim,
        )
    return cells


def swapped(shard, axis, stride):
    return lax.ppermute(shard, axis, [(i, i ^ 1 << stride) for i in range(lax.axis_size(axis))])


def pool_pairs(source):
    shaped = source.reshape(
        source.shape[0], source.shape[1], source.shape[2] // 2, 2, source.shape[3]
    )
    return jnp.sum(shaped, axis=3) * 0.5


def pick_blocks(blocks_doc, chosen_doc):
    return blocks_doc[:, chosen_doc]


def place_blocks(grad_doc, chosen_doc):
    holder = jnp.zeros((grad_doc.shape[0], 6, grad_doc.shape[3], grad_doc.shape[4]), jnp.float32)
    return holder.at[:, chosen_doc].add(grad_doc)


def shards(queries, keys, values, pattern, out_weight, cotangent):
    doc_count, tok_count, head_cols = queries.shape
    block = tok_count // 2
    heads = head_cols // HEAD_DIM
    seq_count = lax.axis_size("seq")
    levels = seq_count.bit_length() - 1
    position = lax.axis_index("seq")
    score_scale = 1.0 / math.sqrt(HEAD_DIM)
    near_width = (NEAR + 1) * block
    key_value = jnp.stack([keys, values])
    padded = extended(key_value, (("seq", 2),), tok_count)
    blocks_six = padded.reshape(2, doc_count, 6, block, head_cols)
    local_ids = jnp.arange(2, dtype=jnp.int32)[None, :, None]
    chosen = jnp.concatenate([local_ids, local_ids + pattern], axis=2) + 2
    near_pair = jax.vmap(pick_blocks, in_axes=(1, 0), out_axes=1)(blocks_six, chosen)
    near_pair = near_pair.reshape(2, doc_count, 2, near_width, head_cols)
    pooled = pool_pairs(key_value.astype(jnp.float32))
    siblings = []
    own_level = pooled
    for level_no in range(levels):
        other = swapped(own_level, "seq", level_no)
        siblings.append(other)
        if level_no + 1 < levels:
            upper = position >> level_no & 1 == 1
            joined = jnp.where(
                upper,
                jnp.concatenate([other, own_level], axis=2),
                jnp.concatenate([own_level, other], axis=2),
            )
            own_level = pool_pairs(joined)
    far_pair = jnp.concatenate(siblings, axis=2).astype(jnp.bfloat16)
    query_heads = queries.reshape(doc_count, 2, block, heads, HEAD_DIM)
    near_k = near_pair[0].reshape(doc_count, 2, near_width, heads, HEAD_DIM)
    near_v = near_pair[1].reshape(doc_count, 2, near_width, heads, HEAD_DIM)
    far_k = far_pair[0].reshape(doc_count, levels * block, heads, HEAD_DIM)
    far_v = far_pair[1].reshape(doc_count, levels * block, heads, HEAD_DIM)
    score_near = (
        jnp.einsum("dbqhe,dbkhe->dbhqk", query_heads, near_k, preferred_element_type=jnp.float32)
        * score_scale
    )
    score_far = (
        jnp.einsum("dbqhe,dkhe->dbhqk", query_heads, far_k, preferred_element_type=jnp.float32)
        * score_scale
    )
    top = jnp.maximum(
        jnp.max(score_near, axis=-1, keepdims=True), jnp.max(score_far, axis=-1, keepdims=True)
    )
    exp_near = jnp.exp(score_near - top)
    exp_far = jnp.exp(score_far - top)
    total = jnp.sum(exp_near, axis=-1, keepdims=True) + jnp.sum(exp_far, axis=-1, keepdims=True)
    weight_near = exp_near / total
    weight_far = exp_far / total
    rounded_near = weight_near.astype(jnp.bfloat16)
    rounded_far = weight_far.astype(jnp.bfloat16)
    output = jnp.einsum(
        "dbhqk,dbkhe->dbqhe", rounded_near, near_v, preferred_element_type=jnp.float32
    )
    output = output + jnp.einsum(
        "dbhqk,dkhe->dbqhe", rounded_far, far_v, preferred_element_type=jnp.float32
    )
    attention = output.reshape(doc_count, tok_count, head_cols).astype(jnp.bfloat16)
    feat_count = cotangent.shape[2] // seq_count
    cot_rows = cotangent.reshape(doc_count * tok_count, cotangent.shape[2])
    out_rows = attention.reshape(doc_count * tok_count, head_cols)
    own_cols = lax.dynamic_slice_in_dim(cot_rows, position * feat_count, feat_count, axis=1)
    grad_sum = jnp.dot(own_cols, out_weight, preferred_element_type=jnp.float32)
    feat_list = [own_cols]
    out_list = [out_rows]
    for step in range(1, seq_count):
        pairs = [(i, i ^ step) for i in range(seq_count)]
        sent = lax.dynamic_slice_in_dim(
            cot_rows, (position ^ step) * feat_count, feat_count, axis=1
        )
        half = sent.shape[0] // 2
        core = lax.axis_index("head")
        got_half = lax.ppermute(
            lax.dynamic_slice_in_dim(sent, core * half, half, axis=0), "seq", pairs
        )
        other_half = swapped(got_half, "head", 0)
        got = jnp.where(
            core == 0,
            jnp.concatenate([got_half, other_half], axis=0),
            jnp.concatenate([other_half, got_half], axis=0),
        )
        part = jnp.dot(got, out_weight, preferred_element_type=jnp.float32)
        back = lax.ppermute(part.astype(jnp.bfloat16), "seq", pairs)
        grad_sum = grad_sum + back.astype(jnp.float32)
        feat_list.append(got)
        out_list.append(lax.ppermute(out_rows, "seq", pairs))
    attn_grad = grad_sum.astype(jnp.bfloat16)
    feat_docs = jnp.concatenate(feat_list, axis=0)
    whole_output = jnp.concatenate(out_list, axis=0)
    dp_count = lax.axis_size("dp")
    if dp_count == 2:
        feat_docs = jnp.concatenate([feat_docs, swapped(feat_docs, "dp", 0)], axis=0)
        whole_output = jnp.concatenate([whole_output, swapped(whole_output, "dp", 0)], axis=0)
    else:
        feat_docs = lax.all_gather(feat_docs, "dp", axis=0, tiled=True)
        whole_output = lax.all_gather(whole_output, "dp", axis=0, tiled=True)
    weight_grad = jnp.einsum(
        "tc,tw->cw", feat_docs, whole_output, preferred_element_type=jnp.float32
    )
    grad_heads = attn_grad.reshape(doc_count, 2, block, heads, HEAD_DIM)
    prob_near = jnp.einsum(
        "dbqhe,dbkhe->dbhqk", grad_heads, near_v, preferred_element_type=jnp.float32
    )
    prob_far = jnp.einsum(
        "dbqhe,dkhe->dbhqk", grad_heads, far_v, preferred_element_type=jnp.float32
    )
    row_dot = jnp.sum(weight_near * prob_near, axis=-1, keepdims=True) + jnp.sum(
        weight_far * prob_far, axis=-1, keepdims=True
    )
    grad_near = (weight_near * (prob_near - row_dot)).astype(jnp.bfloat16)
    grad_far = (weight_far * (prob_far - row_dot)).astype(jnp.bfloat16)
    query_sum = jnp.einsum(
        "dbhqk,dbkhe->dbqhe", grad_near, near_k, preferred_element_type=jnp.float32
    )
    query_sum = query_sum + jnp.einsum(
        "dbhqk,dkhe->dbqhe", grad_far, far_k, preferred_element_type=jnp.float32
    )
    query_grad = (
        (query_sum * score_scale).reshape(doc_count, tok_count, head_cols).astype(jnp.bfloat16)
    )
    near_key_rows = (
        jnp.einsum("dbhqk,dbqhe->dbkhe", grad_near, query_heads, preferred_element_type=jnp.float32)
        * score_scale
    )
    near_value_rows = jnp.einsum(
        "dbhqk,dbqhe->dbkhe", rounded_near, grad_heads, preferred_element_type=jnp.float32
    )
    far_key_rows = (
        jnp.einsum("dbhqk,dbqhe->dkhe", grad_far, query_heads, preferred_element_type=jnp.float32)
        * score_scale
    )
    far_value_rows = jnp.einsum(
        "dbhqk,dbqhe->dkhe", rounded_far, grad_heads, preferred_element_type=jnp.float32
    )
    near_rows = jnp.stack([near_key_rows, near_value_rows]).reshape(
        2, doc_count, 2, NEAR + 1, block, head_cols
    )
    back_six = jax.vmap(place_blocks, in_axes=(1, 0), out_axes=1)(near_rows, chosen)
    rims = jnp.concatenate([back_six[:, :, 0:2], back_six[:, :, 4:6]], axis=2).reshape(
        2, doc_count, 2 * tok_count, head_cols
    )
    beside_all = extended(rims.astype(jnp.bfloat16), (("seq", 2),), tok_count).astype(
        jnp.float32
    )
    token_grad = back_six[:, :, 2:4].reshape(2, doc_count, tok_count, head_cols)
    token_grad = token_grad + beside_all[:, :, :tok_count] + beside_all[:, :, 3 * tok_count :]
    far_rows = jnp.stack([far_key_rows, far_value_rows]).reshape(
        2, doc_count, levels, block, head_cols
    )
    carried = jnp.zeros((2, doc_count, block, head_cols), jnp.float32)
    for level_no in reversed(range(levels)):
        message = far_rows[:, :, level_no]
        mine = jnp.zeros_like(message)
        if level_no + 1 < levels:
            upper = position >> level_no & 1 == 1
            spread = jnp.repeat(carried, 2, axis=2) * 0.5
            lower_half = spread[:, :, :block]
            upper_half = spread[:, :, block:]
            mine = jnp.where(upper, upper_half, lower_half)
            message = message + jnp.where(upper, lower_half, upper_half)
        returned = swapped(message.astype(jnp.bfloat16), "seq", level_no).astype(jnp.float32)
        carried = returned + mine
    token_grad = token_grad + jnp.repeat(carried, 2, axis=2) * 0.5
    key_grad = token_grad[0].astype(jnp.bfloat16)
    value_grad = token_grad[1].astype(jnp.bfloat16)
    return (attention, query_grad, key_grad, value_grad, weight_grad)


def solution(mesh):
    in_specs = (
        P(("groups", "dp"), "seq", "head"),
        P(("groups", "dp"), "seq", "head"),
        P(("groups", "dp"), "seq", "head"),
        P(("groups", "dp"), "seq", None),
        P("seq", "head"),
        P(("groups", "dp"), "seq", None),
    )
    out_specs = (
        P(("groups", "dp"), "seq", "head"),
        P(("groups", "dp"), "seq", "head"),
        P(("groups", "dp"), "seq", "head"),
        P(("groups", "dp"), "seq", "head"),
        P(("groups", "seq"), "head"),
    )
    return jax.shard_map(shards, mesh=mesh, in_specs=in_specs, out_specs=out_specs, check_vma=False)
```

```python
import math

import jax
import jax.numpy as jnp
from jax import lax
from jax.sharding import PartitionSpec as P

HEAD_DIM = 128
NEAR = 2


def extended(cells, sides, width):
    for axis, dim in sides:
        count = lax.axis_size(axis)
        ends = count - 1
        head = lax.slice_in_dim(cells, 0, width, axis=dim)
        tail = lax.slice_in_dim(cells, cells.shape[dim] - width, cells.shape[dim], axis=dim)
        cells = jnp.concatenate(
            [
                lax.ppermute(tail, axis, [(i, (i + 1) % count) for i in range(ends)]),
                cells,
                lax.ppermute(head, axis, [((i + 1) % count, i) for i in range(ends)]),
            ],
            axis=dim,
        )
    return cells


def swapped(shard, axis, stride):
    return lax.ppermute(shard, axis, [(i, i ^ 1 << stride) for i in range(lax.axis_size(axis))])


def pool_pairs(source):
    shaped = source.reshape(
        source.shape[0], source.shape[1], source.shape[2] // 2, 2, source.shape[3]
    )
    return jnp.sum(shaped, axis=3) * 0.5


def pick_blocks(blocks_doc, chosen_doc):
    return blocks_doc[:, chosen_doc]


def place_blocks(grad_doc, chosen_doc):
    holder = jnp.zeros((grad_doc.shape[0], 6, grad_doc.shape[3], grad_doc.shape[4]), jnp.float32)
    return holder.at[:, chosen_doc].add(grad_doc)


def shards(queries, keys, values, pattern, out_weight, cotangent):
    doc_count, tok_count, head_cols = queries.shape
    block = tok_count // 2
    heads = head_cols // HEAD_DIM
    seq_count = lax.axis_size("seq")
    levels = seq_count.bit_length() - 1
    position = lax.axis_index("seq")
    score_scale = 1.0 / math.sqrt(HEAD_DIM)
    near_width = (NEAR + 1) * block
    key_value = jnp.stack([keys, values])
    padded = extended(key_value, (("seq", 2),), tok_count)
    blocks_six = padded.reshape(2, doc_count, 6, block, head_cols)
    local_ids = jnp.arange(2, dtype=jnp.int32)[None, :, None]
    chosen = jnp.concatenate([local_ids, local_ids + pattern], axis=2) + 2
    near_pair = jax.vmap(pick_blocks, in_axes=(1, 0), out_axes=1)(blocks_six, chosen)
    near_pair = near_pair.reshape(2, doc_count, 2, near_width, head_cols)
    pooled = pool_pairs(key_value.astype(jnp.float32))
    siblings = []
    own_level = pooled
    for level_no in range(levels):
        other = swapped(own_level, "seq", level_no)
        siblings.append(other)
        if level_no + 1 < levels:
            upper = position >> level_no & 1 == 1
            joined = jnp.where(
                upper,
                jnp.concatenate([other, own_level], axis=2),
                jnp.concatenate([own_level, other], axis=2),
            )
            own_level = pool_pairs(joined)
    far_pair = jnp.concatenate(siblings, axis=2).astype(jnp.bfloat16)
    query_heads = queries.reshape(doc_count, 2, block, heads, HEAD_DIM)
    near_k = near_pair[0].reshape(doc_count, 2, near_width, heads, HEAD_DIM)
    near_v = near_pair[1].reshape(doc_count, 2, near_width, heads, HEAD_DIM)
    far_k = far_pair[0].reshape(doc_count, levels * block, heads, HEAD_DIM)
    far_v = far_pair[1].reshape(doc_count, levels * block, heads, HEAD_DIM)
    score_near = (
        jnp.einsum("dbqhe,dbkhe->dbhqk", query_heads, near_k, preferred_element_type=jnp.float32)
        * score_scale
    )
    score_far = (
        jnp.einsum("dbqhe,dkhe->dbhqk", query_heads, far_k, preferred_element_type=jnp.float32)
        * score_scale
    )
    top = jnp.maximum(
        jnp.max(score_near, axis=-1, keepdims=True), jnp.max(score_far, axis=-1, keepdims=True)
    )
    exp_near = jnp.exp(score_near - top)
    exp_far = jnp.exp(score_far - top)
    total = jnp.sum(exp_near, axis=-1, keepdims=True) + jnp.sum(exp_far, axis=-1, keepdims=True)
    weight_near = exp_near / total
    weight_far = exp_far / total
    rounded_near = weight_near.astype(jnp.bfloat16)
    rounded_far = weight_far.astype(jnp.bfloat16)
    output = jnp.einsum(
        "dbhqk,dbkhe->dbqhe", rounded_near, near_v, preferred_element_type=jnp.float32
    )
    output = output + jnp.einsum(
        "dbhqk,dkhe->dbqhe", rounded_far, far_v, preferred_element_type=jnp.float32
    )
    attention = output.reshape(doc_count, tok_count, head_cols).astype(jnp.bfloat16)
    feat_count = cotangent.shape[2] // seq_count
    cot_rows = cotangent.reshape(doc_count * tok_count, cotangent.shape[2])
    out_rows = attention.reshape(doc_count * tok_count, head_cols)
    own_cols = lax.dynamic_slice_in_dim(cot_rows, position * feat_count, feat_count, axis=1)
    grad_sum = jnp.dot(own_cols, out_weight, preferred_element_type=jnp.float32)
    feat_list = [own_cols]
    for step in range(1, seq_count):
        pairs = [(i, i ^ step) for i in range(seq_count)]
        sent = lax.dynamic_slice_in_dim(
            cot_rows, (position ^ step) * feat_count, feat_count, axis=1
        )
        half = sent.shape[0] // 2
        core = lax.axis_index("head")
        got_half = lax.ppermute(
            lax.dynamic_slice_in_dim(sent, core * half, half, axis=0), "seq", pairs
        )
        other_half = swapped(got_half, "head", 0)
        got = jnp.where(
            core == 0,
            jnp.concatenate([got_half, other_half], axis=0),
            jnp.concatenate([other_half, got_half], axis=0),
        )
        part = jnp.dot(got, out_weight, preferred_element_type=jnp.float32)
        back = lax.ppermute(part.astype(jnp.bfloat16), "seq", pairs)
        grad_sum = grad_sum + back.astype(jnp.float32)
        feat_list.append(got)
    attn_grad = grad_sum.astype(jnp.bfloat16)
    feat_order = jnp.arange(seq_count, dtype=jnp.int32) ^ position
    feat_docs = jnp.take(jnp.stack(feat_list, axis=0), feat_order, axis=0).reshape(
        seq_count * cot_rows.shape[0], feat_count
    )
    whole_output = lax.all_gather(out_rows, "seq", axis=0, tiled=True)
    dp_count = lax.axis_size("dp")
    if dp_count == 2:
        feat_docs = jnp.concatenate([feat_docs, swapped(feat_docs, "dp", 0)], axis=0)
        whole_output = jnp.concatenate([whole_output, swapped(whole_output, "dp", 0)], axis=0)
    else:
        feat_docs = lax.all_gather(feat_docs, "dp", axis=0, tiled=True)
        whole_output = lax.all_gather(whole_output, "dp", axis=0, tiled=True)
    weight_grad = jnp.einsum(
        "tc,tw->cw", feat_docs, whole_output, preferred_element_type=jnp.float32
    )
    grad_heads = attn_grad.reshape(doc_count, 2, block, heads, HEAD_DIM)
    prob_near = jnp.einsum(
        "dbqhe,dbkhe->dbhqk", grad_heads, near_v, preferred_element_type=jnp.float32
    )
    prob_far = jnp.einsum(
        "dbqhe,dkhe->dbhqk", grad_heads, far_v, preferred_element_type=jnp.float32
    )
    row_dot = jnp.sum(weight_near * prob_near, axis=-1, keepdims=True) + jnp.sum(
        weight_far * prob_far, axis=-1, keepdims=True
    )
    grad_near = (weight_near * (prob_near - row_dot)).astype(jnp.bfloat16)
    grad_far = (weight_far * (prob_far - row_dot)).astype(jnp.bfloat16)
    query_sum = jnp.einsum(
        "dbhqk,dbkhe->dbqhe", grad_near, near_k, preferred_element_type=jnp.float32
    )
    query_sum = query_sum + jnp.einsum(
        "dbhqk,dkhe->dbqhe", grad_far, far_k, preferred_element_type=jnp.float32
    )
    query_grad = (
        (query_sum * score_scale).reshape(doc_count, tok_count, head_cols).astype(jnp.bfloat16)
    )
    near_key_rows = (
        jnp.einsum("dbhqk,dbqhe->dbkhe", grad_near, query_heads, preferred_element_type=jnp.float32)
        * score_scale
    )
    near_value_rows = jnp.einsum(
        "dbhqk,dbqhe->dbkhe", rounded_near, grad_heads, preferred_element_type=jnp.float32
    )
    far_key_rows = (
        jnp.einsum("dbhqk,dbqhe->dkhe", grad_far, query_heads, preferred_element_type=jnp.float32)
        * score_scale
    )
    far_value_rows = jnp.einsum(
        "dbhqk,dbqhe->dkhe", rounded_far, grad_heads, preferred_element_type=jnp.float32
    )
    near_rows = jnp.stack([near_key_rows, near_value_rows]).reshape(
        2, doc_count, 2, NEAR + 1, block, head_cols
    )
    back_six = jax.vmap(place_blocks, in_axes=(1, 0), out_axes=1)(near_rows, chosen)
    rims = jnp.concatenate([back_six[:, :, 0:2], back_six[:, :, 4:6]], axis=2).reshape(
        2, doc_count, 2 * tok_count, head_cols
    )
    beside_all = extended(rims.astype(jnp.bfloat16), (("seq", 2),), tok_count).astype(
        jnp.float32
    )
    token_grad = back_six[:, :, 2:4].reshape(2, doc_count, tok_count, head_cols)
    token_grad = token_grad + beside_all[:, :, :tok_count] + beside_all[:, :, 3 * tok_count :]
    far_rows = jnp.stack([far_key_rows, far_value_rows]).reshape(
        2, doc_count, levels, block, head_cols
    )
    carried = jnp.zeros((2, doc_count, block, head_cols), jnp.float32)
    for level_no in reversed(range(levels)):
        message = far_rows[:, :, level_no]
        mine = jnp.zeros_like(message)
        if level_no + 1 < levels:
            upper = position >> level_no & 1 == 1
            spread = jnp.repeat(carried, 2, axis=2) * 0.5
            lower_half = spread[:, :, :block]
            upper_half = spread[:, :, block:]
            mine = jnp.where(upper, upper_half, lower_half)
            message = message + jnp.where(upper, lower_half, upper_half)
        returned = swapped(message.astype(jnp.bfloat16), "seq", level_no).astype(jnp.float32)
        carried = returned + mine
    token_grad = token_grad + jnp.repeat(carried, 2, axis=2) * 0.5
    key_grad = token_grad[0].astype(jnp.bfloat16)
    value_grad = token_grad[1].astype(jnp.bfloat16)
    return (attention, query_grad, key_grad, value_grad, weight_grad)


def solution(mesh):
    in_specs = (
        P(("groups", "dp"), "seq", "head"),
        P(("groups", "dp"), "seq", "head"),
        P(("groups", "dp"), "seq", "head"),
        P(("groups", "dp"), "seq", None),
        P("seq", "head"),
        P(("groups", "dp"), "seq", None),
    )
    out_specs = (
        P(("groups", "dp"), "seq", "head"),
        P(("groups", "dp"), "seq", "head"),
        P(("groups", "dp"), "seq", "head"),
        P(("groups", "dp"), "seq", "head"),
        P(("groups", "seq"), "head"),
    )
    return jax.shard_map(shards, mesh=mesh, in_specs=in_specs, out_specs=out_specs, check_vma=False)
```

```python
import math

import jax
import jax.numpy as jnp
from jax import lax
from jax.sharding import PartitionSpec as P

HEAD_DIM = 128
NEAR = 2


def extended(cells, sides, width):
    for axis, dim in sides:
        count = lax.axis_size(axis)
        ends = count - 1
        head = lax.slice_in_dim(cells, 0, width, axis=dim)
        tail = lax.slice_in_dim(cells, cells.shape[dim] - width, cells.shape[dim], axis=dim)
        cells = jnp.concatenate(
            [
                lax.ppermute(tail, axis, [(i, (i + 1) % count) for i in range(ends)]),
                cells,
                lax.ppermute(head, axis, [((i + 1) % count, i) for i in range(ends)]),
            ],
            axis=dim,
        )
    return cells


def swapped(shard, axis, stride):
    return lax.ppermute(shard, axis, [(i, i ^ 1 << stride) for i in range(lax.axis_size(axis))])


def pool_pairs(source):
    shaped = source.reshape(
        source.shape[0], source.shape[1], source.shape[2] // 2, 2, source.shape[3]
    )
    return jnp.sum(shaped, axis=3) * 0.5


def pick_blocks(blocks_doc, chosen_doc):
    return blocks_doc[:, chosen_doc]


def place_blocks(grad_doc, chosen_doc):
    holder = jnp.zeros((grad_doc.shape[0], 6, grad_doc.shape[3], grad_doc.shape[4]), jnp.float32)
    return holder.at[:, chosen_doc].add(grad_doc)


def shards(queries, keys, values, pattern, out_weight, cotangent):
    doc_count, tok_count, head_cols = queries.shape
    block = tok_count // 2
    heads = head_cols // HEAD_DIM
    seq_count = lax.axis_size("seq")
    levels = seq_count.bit_length() - 1
    position = lax.axis_index("seq")
    score_scale = 1.0 / math.sqrt(HEAD_DIM)
    near_width = (NEAR + 1) * block
    key_value = jnp.stack([keys, values])
    padded = extended(key_value, (("seq", 2),), tok_count)
    blocks_six = padded.reshape(2, doc_count, 6, block, head_cols)
    local_ids = jnp.arange(2, dtype=jnp.int32)[None, :, None]
    chosen = jnp.concatenate([local_ids, local_ids + pattern], axis=2) + 2
    near_pair = jax.vmap(pick_blocks, in_axes=(1, 0), out_axes=1)(blocks_six, chosen)
    near_pair = near_pair.reshape(2, doc_count, 2, near_width, head_cols)
    pieces = []
    level_rows = key_value.astype(jnp.float32)
    for level_no in range(levels):
        level_rows = pool_pairs(level_rows)
        pieces.append(level_rows.astype(jnp.bfloat16))
    feat_count = cotangent.shape[2] // seq_count
    cot_rows = cotangent.reshape(doc_count * tok_count, cotangent.shape[2])
    core = lax.axis_index("head")
    half = cot_rows.shape[0] // 2
    far_parts = []
    got_list = []
    for step in range(1, seq_count):
        pairs = [(i, i ^ step) for i in range(seq_count)]
        piece = pieces[step.bit_length() - 1]
        sent = lax.dynamic_slice_in_dim(
            cot_rows, (position ^ step) * feat_count, feat_count, axis=1
        )
        sent_half = lax.dynamic_slice_in_dim(sent, core * half, half, axis=0)
        if feat_count == head_cols:
            payload = jnp.concatenate([sent_half, piece.reshape(-1, head_cols)], axis=0)
            arrived = lax.ppermute(payload, "seq", pairs)
            got_half = arrived[:half]
            far_parts.append(arrived[half:].reshape(piece.shape))
        else:
            got_half = lax.ppermute(sent_half, "seq", pairs)
            far_parts.append(lax.ppermute(piece, "seq", pairs))
        other_half = swapped(got_half, "head", 0)
        got_list.append(
            jnp.where(
                core == 0,
                jnp.concatenate([got_half, other_half], axis=0),
                jnp.concatenate([other_half, got_half], axis=0),
            )
        )
    far_levels = []
    for level_no in range(levels):
        count = 1 << level_no
        group = jnp.stack(far_parts[count - 1 : 2 * count - 1], axis=0)
        order = jnp.arange(count, dtype=jnp.int32) ^ (position & (count - 1))
        group = jnp.take(group, order, axis=0)
        far_levels.append(
            jnp.moveaxis(group, 0, 2).reshape(2, doc_count, count * group.shape[3], head_cols)
        )
    far_pair = jnp.concatenate(far_levels, axis=2)
    query_heads = queries.reshape(doc_count, 2, block, heads, HEAD_DIM)
    near_k = near_pair[0].reshape(doc_count, 2, near_width, heads, HEAD_DIM)
    near_v = near_pair[1].reshape(doc_count, 2, near_width, heads, HEAD_DIM)
    far_k = far_pair[0].reshape(doc_count, levels * block, heads, HEAD_DIM)
    far_v = far_pair[1].reshape(doc_count, levels * block, heads, HEAD_DIM)
    score_near = (
        jnp.einsum("dbqhe,dbkhe->dbhqk", query_heads, near_k, preferred_element_type=jnp.float32)
        * score_scale
    )
    score_far = (
        jnp.einsum("dbqhe,dkhe->dbhqk", query_heads, far_k, preferred_element_type=jnp.float32)
        * score_scale
    )
    top = jnp.maximum(
        jnp.max(score_near, axis=-1, keepdims=True), jnp.max(score_far, axis=-1, keepdims=True)
    )
    exp_near = jnp.exp(score_near - top)
    exp_far = jnp.exp(score_far - top)
    total = jnp.sum(exp_near, axis=-1, keepdims=True) + jnp.sum(exp_far, axis=-1, keepdims=True)
    weight_near = exp_near / total
    weight_far = exp_far / total
    rounded_near = weight_near.astype(jnp.bfloat16)
    rounded_far = weight_far.astype(jnp.bfloat16)
    output = jnp.einsum(
        "dbhqk,dbkhe->dbqhe", rounded_near, near_v, preferred_element_type=jnp.float32
    )
    output = output + jnp.einsum(
        "dbhqk,dkhe->dbqhe", rounded_far, far_v, preferred_element_type=jnp.float32
    )
    attention = output.reshape(doc_count, tok_count, head_cols).astype(jnp.bfloat16)
    out_rows = attention.reshape(doc_count * tok_count, head_cols)
    own_cols = lax.dynamic_slice_in_dim(cot_rows, position * feat_count, feat_count, axis=1)
    grad_sum = jnp.dot(own_cols, out_weight, preferred_element_type=jnp.float32)
    feat_list = [own_cols]
    for step in range(1, seq_count):
        pairs = [(i, i ^ step) for i in range(seq_count)]
        got = got_list[step - 1]
        part = jnp.dot(got, out_weight, preferred_element_type=jnp.float32)
        back = lax.ppermute(part.astype(jnp.bfloat16), "seq", pairs)
        grad_sum = grad_sum + back.astype(jnp.float32)
        feat_list.append(got)
    attn_grad = grad_sum.astype(jnp.bfloat16)
    feat_order = jnp.arange(seq_count, dtype=jnp.int32) ^ position
    feat_docs = jnp.take(jnp.stack(feat_list, axis=0), feat_order, axis=0).reshape(
        seq_count * cot_rows.shape[0], feat_count
    )
    whole_output = lax.all_gather(out_rows, "seq", axis=0, tiled=True)
    dp_count = lax.axis_size("dp")
    if dp_count == 2:
        feat_docs = jnp.concatenate([feat_docs, swapped(feat_docs, "dp", 0)], axis=0)
        whole_output = jnp.concatenate([whole_output, swapped(whole_output, "dp", 0)], axis=0)
    else:
        feat_docs = lax.all_gather(feat_docs, "dp", axis=0, tiled=True)
        whole_output = lax.all_gather(whole_output, "dp", axis=0, tiled=True)
    weight_grad = jnp.einsum(
        "tc,tw->cw", feat_docs, whole_output, preferred_element_type=jnp.float32
    )
    grad_heads = attn_grad.reshape(doc_count, 2, block, heads, HEAD_DIM)
    prob_near = jnp.einsum(
        "dbqhe,dbkhe->dbhqk", grad_heads, near_v, preferred_element_type=jnp.float32
    )
    prob_far = jnp.einsum(
        "dbqhe,dkhe->dbhqk", grad_heads, far_v, preferred_element_type=jnp.float32
    )
    row_dot = jnp.sum(weight_near * prob_near, axis=-1, keepdims=True) + jnp.sum(
        weight_far * prob_far, axis=-1, keepdims=True
    )
    grad_near = (weight_near * (prob_near - row_dot)).astype(jnp.bfloat16)
    grad_far = (weight_far * (prob_far - row_dot)).astype(jnp.bfloat16)
    query_sum = jnp.einsum(
        "dbhqk,dbkhe->dbqhe", grad_near, near_k, preferred_element_type=jnp.float32
    )
    query_sum = query_sum + jnp.einsum(
        "dbhqk,dkhe->dbqhe", grad_far, far_k, preferred_element_type=jnp.float32
    )
    query_grad = (
        (query_sum * score_scale).reshape(doc_count, tok_count, head_cols).astype(jnp.bfloat16)
    )
    near_key_rows = (
        jnp.einsum("dbhqk,dbqhe->dbkhe", grad_near, query_heads, preferred_element_type=jnp.float32)
        * score_scale
    )
    near_value_rows = jnp.einsum(
        "dbhqk,dbqhe->dbkhe", rounded_near, grad_heads, preferred_element_type=jnp.float32
    )
    far_key_rows = (
        jnp.einsum("dbhqk,dbqhe->dkhe", grad_far, query_heads, preferred_element_type=jnp.float32)
        * score_scale
    )
    far_value_rows = jnp.einsum(
        "dbhqk,dbqhe->dkhe", rounded_far, grad_heads, preferred_element_type=jnp.float32
    )
    near_rows = jnp.stack([near_key_rows, near_value_rows]).reshape(
        2, doc_count, 2, NEAR + 1, block, head_cols
    )
    back_six = jax.vmap(place_blocks, in_axes=(1, 0), out_axes=1)(near_rows, chosen)
    rims = jnp.concatenate([back_six[:, :, 0:2], back_six[:, :, 4:6]], axis=2).reshape(
        2, doc_count, 2 * tok_count, head_cols
    )
    beside_all = extended(rims.astype(jnp.bfloat16), (("seq", 2),), tok_count).astype(
        jnp.float32
    )
    token_grad = back_six[:, :, 2:4].reshape(2, doc_count, tok_count, head_cols)
    token_grad = token_grad + beside_all[:, :, :tok_count] + beside_all[:, :, 3 * tok_count :]
    far_rows = jnp.stack([far_key_rows, far_value_rows]).reshape(
        2, doc_count, levels, block, head_cols
    )
    carried = jnp.zeros((2, doc_count, block, head_cols), jnp.float32)
    for level_no in reversed(range(levels)):
        message = far_rows[:, :, level_no]
        mine = jnp.zeros_like(message)
        if level_no + 1 < levels:
            upper = position >> level_no & 1 == 1
            spread = jnp.repeat(carried, 2, axis=2) * 0.5
            lower_half = spread[:, :, :block]
            upper_half = spread[:, :, block:]
            mine = jnp.where(upper, upper_half, lower_half)
            message = message + jnp.where(upper, lower_half, upper_half)
        returned = swapped(message.astype(jnp.bfloat16), "seq", level_no).astype(jnp.float32)
        carried = returned + mine
    token_grad = token_grad + jnp.repeat(carried, 2, axis=2) * 0.5
    key_grad = token_grad[0].astype(jnp.bfloat16)
    value_grad = token_grad[1].astype(jnp.bfloat16)
    return (attention, query_grad, key_grad, value_grad, weight_grad)


def solution(mesh):
    in_specs = (
        P(("groups", "dp"), "seq", "head"),
        P(("groups", "dp"), "seq", "head"),
        P(("groups", "dp"), "seq", "head"),
        P(("groups", "dp"), "seq", None),
        P("seq", "head"),
        P(("groups", "dp"), "seq", None),
    )
    out_specs = (
        P(("groups", "dp"), "seq", "head"),
        P(("groups", "dp"), "seq", "head"),
        P(("groups", "dp"), "seq", "head"),
        P(("groups", "dp"), "seq", "head"),
        P(("groups", "seq"), "head"),
    )
    return jax.shard_map(shards, mesh=mesh, in_specs=in_specs, out_specs=out_specs, check_vma=False)
```

```python
import math

import jax
import jax.numpy as jnp
from jax import lax
from jax.sharding import PartitionSpec as P

HEAD_DIM = 128
NEAR = 2


def extended(cells, sides, width):
    for axis, dim in sides:
        count = lax.axis_size(axis)
        ends = count - 1
        head = lax.slice_in_dim(cells, 0, width, axis=dim)
        tail = lax.slice_in_dim(cells, cells.shape[dim] - width, cells.shape[dim], axis=dim)
        cells = jnp.concatenate(
            [
                lax.ppermute(tail, axis, [(i, (i + 1) % count) for i in range(ends)]),
                cells,
                lax.ppermute(head, axis, [((i + 1) % count, i) for i in range(ends)]),
            ],
            axis=dim,
        )
    return cells


def swapped(shard, axis, stride):
    return lax.ppermute(shard, axis, [(i, i ^ 1 << stride) for i in range(lax.axis_size(axis))])


def pool_pairs(source):
    shaped = source.reshape(
        source.shape[0], source.shape[1], source.shape[2] // 2, 2, source.shape[3]
    )
    return jnp.sum(shaped, axis=3) * 0.5


def pick_blocks(blocks_doc, chosen_doc):
    return blocks_doc[:, chosen_doc]


def place_blocks(grad_doc, chosen_doc):
    holder = jnp.zeros((grad_doc.shape[0], 6, grad_doc.shape[3], grad_doc.shape[4]), jnp.float32)
    return holder.at[:, chosen_doc].add(grad_doc)


def shards(queries, keys, values, pattern, out_weight, cotangent):
    doc_count, tok_count, head_cols = queries.shape
    block = tok_count // 2
    heads = head_cols // HEAD_DIM
    seq_count = lax.axis_size("seq")
    levels = seq_count.bit_length() - 1
    position = lax.axis_index("seq")
    score_scale = 1.0 / math.sqrt(HEAD_DIM)
    near_width = (NEAR + 1) * block
    key_value = jnp.stack([keys, values])
    padded = extended(key_value, (("seq", 2),), tok_count)
    blocks_six = padded.reshape(2, doc_count, 6, block, head_cols)
    local_ids = jnp.arange(2, dtype=jnp.int32)[None, :, None]
    chosen = jnp.concatenate([local_ids, local_ids + pattern], axis=2) + 2
    near_pair = jax.vmap(pick_blocks, in_axes=(1, 0), out_axes=1)(blocks_six, chosen)
    near_pair = near_pair.reshape(2, doc_count, 2, near_width, head_cols)
    pooled = pool_pairs(key_value.astype(jnp.float32))
    siblings = []
    own_level = pooled
    for level_no in range(levels):
        other = swapped(own_level, "seq", level_no)
        siblings.append(other)
        if level_no + 1 < levels:
            upper = position >> level_no & 1 == 1
            joined = jnp.where(
                upper,
                jnp.concatenate([other, own_level], axis=2),
                jnp.concatenate([own_level, other], axis=2),
            )
            own_level = pool_pairs(joined)
    far_pair = jnp.concatenate(siblings, axis=2).astype(jnp.bfloat16)
    query_heads = queries.reshape(doc_count, 2, block, heads, HEAD_DIM)
    near_k = near_pair[0].reshape(doc_count, 2, near_width, heads, HEAD_DIM)
    near_v = near_pair[1].reshape(doc_count, 2, near_width, heads, HEAD_DIM)
    far_k = far_pair[0].reshape(doc_count, levels * block, heads, HEAD_DIM)
    far_v = far_pair[1].reshape(doc_count, levels * block, heads, HEAD_DIM)
    score_near = (
        jnp.einsum("dbqhe,dbkhe->dbhqk", query_heads, near_k, preferred_element_type=jnp.float32)
        * score_scale
    )
    score_far = (
        jnp.einsum("dbqhe,dkhe->dbhqk", query_heads, far_k, preferred_element_type=jnp.float32)
        * score_scale
    )
    top = jnp.maximum(
        jnp.max(score_near, axis=-1, keepdims=True), jnp.max(score_far, axis=-1, keepdims=True)
    )
    exp_near = jnp.exp(score_near - top)
    exp_far = jnp.exp(score_far - top)
    total = jnp.sum(exp_near, axis=-1, keepdims=True) + jnp.sum(exp_far, axis=-1, keepdims=True)
    weight_near = exp_near / total
    weight_far = exp_far / total
    rounded_near = weight_near.astype(jnp.bfloat16)
    rounded_far = weight_far.astype(jnp.bfloat16)
    output = jnp.einsum(
        "dbhqk,dbkhe->dbqhe", rounded_near, near_v, preferred_element_type=jnp.float32
    )
    output = output + jnp.einsum(
        "dbhqk,dkhe->dbqhe", rounded_far, far_v, preferred_element_type=jnp.float32
    )
    attention = output.reshape(doc_count, tok_count, head_cols).astype(jnp.bfloat16)
    feat_count = cotangent.shape[2] // seq_count
    cot_rows = cotangent.reshape(doc_count * tok_count, cotangent.shape[2])
    out_rows = attention.reshape(doc_count * tok_count, head_cols)
    own_cols = lax.dynamic_slice_in_dim(cot_rows, position * feat_count, feat_count, axis=1)
    grad_sum = jnp.dot(own_cols, out_weight, preferred_element_type=jnp.float32)
    feat_list = [own_cols]
    for step in range(1, seq_count):
        pairs = [(i, i ^ step) for i in range(seq_count)]
        sent = lax.dynamic_slice_in_dim(
            cot_rows, (position ^ step) * feat_count, feat_count, axis=1
        )
        half = sent.shape[0] // 2
        core = lax.axis_index("head")
        got_half = lax.ppermute(
            lax.dynamic_slice_in_dim(sent, core * half, half, axis=0), "seq", pairs
        )
        other_half = swapped(got_half, "head", 0)
        got = jnp.where(
            core == 0,
            jnp.concatenate([got_half, other_half], axis=0),
            jnp.concatenate([other_half, got_half], axis=0),
        )
        part = jnp.dot(got, out_weight, preferred_element_type=jnp.float32)
        back = lax.ppermute(part.astype(jnp.bfloat16), "seq", pairs)
        grad_sum = grad_sum + back.astype(jnp.float32)
        feat_list.append(got)
    attn_grad = grad_sum.astype(jnp.bfloat16)
    feat_order = jnp.arange(seq_count, dtype=jnp.int32) ^ position
    feat_docs = jnp.take(jnp.stack(feat_list, axis=0), feat_order, axis=0).reshape(
        seq_count * cot_rows.shape[0], feat_count
    )
    feat_docs = lax.all_gather(feat_docs, "dp", axis=0, tiled=True)
    whole_output = lax.all_gather(out_rows, ("dp", "seq"), axis=0, tiled=True)
    weight_grad = jnp.einsum(
        "tc,tw->cw", feat_docs, whole_output, preferred_element_type=jnp.float32
    )
    grad_heads = attn_grad.reshape(doc_count, 2, block, heads, HEAD_DIM)
    prob_near = jnp.einsum(
        "dbqhe,dbkhe->dbhqk", grad_heads, near_v, preferred_element_type=jnp.float32
    )
    prob_far = jnp.einsum(
        "dbqhe,dkhe->dbhqk", grad_heads, far_v, preferred_element_type=jnp.float32
    )
    row_dot = jnp.sum(weight_near * prob_near, axis=-1, keepdims=True) + jnp.sum(
        weight_far * prob_far, axis=-1, keepdims=True
    )
    grad_near = (weight_near * (prob_near - row_dot)).astype(jnp.bfloat16)
    grad_far = (weight_far * (prob_far - row_dot)).astype(jnp.bfloat16)
    query_sum = jnp.einsum(
        "dbhqk,dbkhe->dbqhe", grad_near, near_k, preferred_element_type=jnp.float32
    )
    query_sum = query_sum + jnp.einsum(
        "dbhqk,dkhe->dbqhe", grad_far, far_k, preferred_element_type=jnp.float32
    )
    query_grad = (
        (query_sum * score_scale).reshape(doc_count, tok_count, head_cols).astype(jnp.bfloat16)
    )
    near_key_rows = (
        jnp.einsum("dbhqk,dbqhe->dbkhe", grad_near, query_heads, preferred_element_type=jnp.float32)
        * score_scale
    )
    near_value_rows = jnp.einsum(
        "dbhqk,dbqhe->dbkhe", rounded_near, grad_heads, preferred_element_type=jnp.float32
    )
    far_key_rows = (
        jnp.einsum("dbhqk,dbqhe->dkhe", grad_far, query_heads, preferred_element_type=jnp.float32)
        * score_scale
    )
    far_value_rows = jnp.einsum(
        "dbhqk,dbqhe->dkhe", rounded_far, grad_heads, preferred_element_type=jnp.float32
    )
    near_rows = jnp.stack([near_key_rows, near_value_rows]).reshape(
        2, doc_count, 2, NEAR + 1, block, head_cols
    )
    back_six = jax.vmap(place_blocks, in_axes=(1, 0), out_axes=1)(near_rows, chosen)
    rims = jnp.concatenate([back_six[:, :, 0:2], back_six[:, :, 4:6]], axis=2).reshape(
        2, doc_count, 2 * tok_count, head_cols
    )
    beside_all = extended(rims.astype(jnp.bfloat16), (("seq", 2),), tok_count).astype(
        jnp.float32
    )
    token_grad = back_six[:, :, 2:4].reshape(2, doc_count, tok_count, head_cols)
    token_grad = token_grad + beside_all[:, :, :tok_count] + beside_all[:, :, 3 * tok_count :]
    far_rows = jnp.stack([far_key_rows, far_value_rows]).reshape(
        2, doc_count, levels, block, head_cols
    )
    carried = jnp.zeros((2, doc_count, block, head_cols), jnp.float32)
    for level_no in reversed(range(levels)):
        message = far_rows[:, :, level_no]
        mine = jnp.zeros_like(message)
        if level_no + 1 < levels:
            upper = position >> level_no & 1 == 1
            spread = jnp.repeat(carried, 2, axis=2) * 0.5
            lower_half = spread[:, :, :block]
            upper_half = spread[:, :, block:]
            mine = jnp.where(upper, upper_half, lower_half)
            message = message + jnp.where(upper, lower_half, upper_half)
        returned = swapped(message.astype(jnp.bfloat16), "seq", level_no).astype(jnp.float32)
        carried = returned + mine
    token_grad = token_grad + jnp.repeat(carried, 2, axis=2) * 0.5
    key_grad = token_grad[0].astype(jnp.bfloat16)
    value_grad = token_grad[1].astype(jnp.bfloat16)
    return (attention, query_grad, key_grad, value_grad, weight_grad)


def solution(mesh):
    in_specs = (
        P(("groups", "dp"), "seq", "head"),
        P(("groups", "dp"), "seq", "head"),
        P(("groups", "dp"), "seq", "head"),
        P(("groups", "dp"), "seq", None),
        P("seq", "head"),
        P(("groups", "dp"), "seq", None),
    )
    out_specs = (
        P(("groups", "dp"), "seq", "head"),
        P(("groups", "dp"), "seq", "head"),
        P(("groups", "dp"), "seq", "head"),
        P(("groups", "dp"), "seq", "head"),
        P(("groups", "seq"), "head"),
    )
    return jax.shard_map(shards, mesh=mesh, in_specs=in_specs, out_specs=out_specs, check_vma=False)
```

```python
import math

import jax
import jax.numpy as jnp
from jax import lax
from jax.sharding import PartitionSpec as P

HEAD_DIM = 128
NEAR = 2


def extended(cells, sides, width):
    for axis, dim in sides:
        count = lax.axis_size(axis)
        ends = count - 1
        head = lax.slice_in_dim(cells, 0, width, axis=dim)
        tail = lax.slice_in_dim(cells, cells.shape[dim] - width, cells.shape[dim], axis=dim)
        cells = jnp.concatenate(
            [
                lax.ppermute(tail, axis, [(i, (i + 1) % count) for i in range(ends)]),
                cells,
                lax.ppermute(head, axis, [((i + 1) % count, i) for i in range(ends)]),
            ],
            axis=dim,
        )
    return cells


def swapped(shard, axis, stride):
    return lax.ppermute(shard, axis, [(i, i ^ 1 << stride) for i in range(lax.axis_size(axis))])


def pool_pairs(source):
    shaped = source.reshape(
        source.shape[0], source.shape[1], source.shape[2] // 2, 2, source.shape[3]
    )
    return jnp.sum(shaped, axis=3) * 0.5


def pick_blocks(blocks_doc, chosen_doc):
    return blocks_doc[:, chosen_doc]


def place_blocks(grad_doc, chosen_doc):
    holder = jnp.zeros((grad_doc.shape[0], 6, grad_doc.shape[3], grad_doc.shape[4]), jnp.float32)
    return holder.at[:, chosen_doc].add(grad_doc)


def shards(queries, keys, values, pattern, out_weight, cotangent):
    doc_count, tok_count, head_cols = queries.shape
    block = tok_count // 2
    heads = head_cols // HEAD_DIM
    seq_count = lax.axis_size("seq")
    levels = seq_count.bit_length() - 1
    position = lax.axis_index("seq")
    score_scale = 1.0 / math.sqrt(HEAD_DIM)
    near_width = (NEAR + 1) * block
    key_value = jnp.stack([keys, values])
    padded = extended(key_value, (("seq", 2),), tok_count)
    blocks_six = padded.reshape(2, doc_count, 6, block, head_cols)
    local_ids = jnp.arange(2, dtype=jnp.int32)[None, :, None]
    chosen = jnp.concatenate([local_ids, local_ids + pattern], axis=2) + 2
    near_pair = jax.vmap(pick_blocks, in_axes=(1, 0), out_axes=1)(blocks_six, chosen)
    near_pair = near_pair.reshape(2, doc_count, 2, near_width, head_cols)
    pooled = pool_pairs(key_value.astype(jnp.float32))
    siblings = []
    own_level = pooled
    for level_no in range(levels):
        other = swapped(own_level, "seq", level_no)
        siblings.append(other)
        if level_no + 1 < levels:
            upper = position >> level_no & 1 == 1
            joined = jnp.where(
                upper,
                jnp.concatenate([other, own_level], axis=2),
                jnp.concatenate([own_level, other], axis=2),
            )
            own_level = pool_pairs(joined)
    far_pair = jnp.concatenate(siblings, axis=2).astype(jnp.bfloat16)
    query_heads = queries.reshape(doc_count, 2, block, heads, HEAD_DIM)
    near_k = near_pair[0].reshape(doc_count, 2, near_width, heads, HEAD_DIM)
    near_v = near_pair[1].reshape(doc_count, 2, near_width, heads, HEAD_DIM)
    far_k = far_pair[0].reshape(doc_count, levels * block, heads, HEAD_DIM)
    far_v = far_pair[1].reshape(doc_count, levels * block, heads, HEAD_DIM)
    score_near = (
        jnp.einsum("dbqhe,dbkhe->dbhqk", query_heads, near_k, preferred_element_type=jnp.float32)
        * score_scale
    )
    score_far = (
        jnp.einsum("dbqhe,dkhe->dbhqk", query_heads, far_k, preferred_element_type=jnp.float32)
        * score_scale
    )
    top = jnp.maximum(
        jnp.max(score_near, axis=-1, keepdims=True), jnp.max(score_far, axis=-1, keepdims=True)
    )
    exp_near = jnp.exp(score_near - top)
    exp_far = jnp.exp(score_far - top)
    total = jnp.sum(exp_near, axis=-1, keepdims=True) + jnp.sum(exp_far, axis=-1, keepdims=True)
    weight_near = exp_near / total
    weight_far = exp_far / total
    rounded_near = weight_near.astype(jnp.bfloat16)
    rounded_far = weight_far.astype(jnp.bfloat16)
    output = jnp.einsum(
        "dbhqk,dbkhe->dbqhe", rounded_near, near_v, preferred_element_type=jnp.float32
    )
    output = output + jnp.einsum(
        "dbhqk,dkhe->dbqhe", rounded_far, far_v, preferred_element_type=jnp.float32
    )
    attention = output.reshape(doc_count, tok_count, head_cols).astype(jnp.bfloat16)
    feat_count = cotangent.shape[2] // seq_count
    cot_rows = cotangent.reshape(doc_count * tok_count, cotangent.shape[2])
    out_rows = attention.reshape(doc_count * tok_count, head_cols)
    own_cols = lax.dynamic_slice_in_dim(cot_rows, position * feat_count, feat_count, axis=1)
    grad_sum = jnp.dot(own_cols, out_weight, preferred_element_type=jnp.float32)
    feat_list = [own_cols]
    for step in range(1, seq_count):
        pairs = [(i, i ^ step) for i in range(seq_count)]
        sent = lax.dynamic_slice_in_dim(
            cot_rows, (position ^ step) * feat_count, feat_count, axis=1
        )
        half = sent.shape[0] // 2
        core = lax.axis_index("head")
        got_half = lax.ppermute(
            lax.dynamic_slice_in_dim(sent, core * half, half, axis=0), "seq", pairs
        )
        other_half = swapped(got_half, "head", 0)
        got = jnp.where(
            core == 0,
            jnp.concatenate([got_half, other_half], axis=0),
            jnp.concatenate([other_half, got_half], axis=0),
        )
        part = jnp.dot(got, out_weight, preferred_element_type=jnp.float32)
        back = lax.ppermute(part.astype(jnp.bfloat16), "seq", pairs)
        grad_sum = grad_sum + back.astype(jnp.float32)
        feat_list.append(got)
    attn_grad = grad_sum.astype(jnp.bfloat16)
    feat_order = jnp.arange(seq_count, dtype=jnp.int32) ^ position
    feat_docs = jnp.take(jnp.stack(feat_list, axis=0), feat_order, axis=0).reshape(
        seq_count * cot_rows.shape[0], feat_count
    )
    feat_docs = lax.all_gather(feat_docs, "dp", axis=0, tiled=True)
    whole_output = lax.all_gather(out_rows, ("dp", "seq"), axis=0, tiled=True)
    weight_grad = jnp.einsum(
        "tc,tw->cw", feat_docs, whole_output, preferred_element_type=jnp.float32
    )
    grad_heads = attn_grad.reshape(doc_count, 2, block, heads, HEAD_DIM)
    prob_near = jnp.einsum(
        "dbqhe,dbkhe->dbhqk", grad_heads, near_v, preferred_element_type=jnp.float32
    )
    prob_far = jnp.einsum(
        "dbqhe,dkhe->dbhqk", grad_heads, far_v, preferred_element_type=jnp.float32
    )
    row_dot = jnp.sum(weight_near * prob_near, axis=-1, keepdims=True) + jnp.sum(
        weight_far * prob_far, axis=-1, keepdims=True
    )
    grad_near = (weight_near * (prob_near - row_dot)).astype(jnp.bfloat16)
    grad_far = (weight_far * (prob_far - row_dot)).astype(jnp.bfloat16)
    query_sum = jnp.einsum(
        "dbhqk,dbkhe->dbqhe", grad_near, near_k, preferred_element_type=jnp.float32
    )
    query_sum = query_sum + jnp.einsum(
        "dbhqk,dkhe->dbqhe", grad_far, far_k, preferred_element_type=jnp.float32
    )
    query_grad = (
        (query_sum * score_scale).reshape(doc_count, tok_count, head_cols).astype(jnp.bfloat16)
    )
    near_key_rows = (
        jnp.einsum("dbhqk,dbqhe->dbkhe", grad_near, query_heads, preferred_element_type=jnp.float32)
        * score_scale
    )
    near_value_rows = jnp.einsum(
        "dbhqk,dbqhe->dbkhe", rounded_near, grad_heads, preferred_element_type=jnp.float32
    )
    far_key_rows = (
        jnp.einsum("dbhqk,dbqhe->dkhe", grad_far, query_heads, preferred_element_type=jnp.float32)
        * score_scale
    )
    far_value_rows = jnp.einsum(
        "dbhqk,dbqhe->dkhe", rounded_far, grad_heads, preferred_element_type=jnp.float32
    )
    near_rows = jnp.stack([near_key_rows, near_value_rows]).reshape(
        2, doc_count, 2, NEAR + 1, block, head_cols
    )
    back_six = jax.vmap(place_blocks, in_axes=(1, 0), out_axes=1)(near_rows, chosen)
    rims = jnp.concatenate([back_six[:, :, 0:2], back_six[:, :, 4:6]], axis=2).reshape(
        2, doc_count, 2 * tok_count, head_cols
    )
    beside_all = extended(rims.astype(jnp.bfloat16), (("seq", 2),), tok_count).astype(
        jnp.float32
    )
    token_grad = back_six[:, :, 2:4].reshape(2, doc_count, tok_count, head_cols)
    token_grad = token_grad + beside_all[:, :, :tok_count] + beside_all[:, :, 3 * tok_count :]
    far_rows = jnp.stack([far_key_rows, far_value_rows]).reshape(
        2, doc_count, levels, block, head_cols
    )
    for level_no in range(levels):
        count = 1 << level_no
        height = block // count
        level_sum = None
        for step in range(count, 2 * count):
            slot = (position ^ step) & (count - 1)
            segment = lax.dynamic_slice_in_dim(far_rows[:, :, level_no], slot * height, height, axis=2)
            returned = lax.ppermute(
                segment.astype(jnp.bfloat16), "seq", [(i, i ^ step) for i in range(seq_count)]
            ).astype(jnp.float32)
            level_sum = returned if level_sum is None else level_sum + returned
        spread = 2 ** (level_no + 1)
        token_grad = token_grad + jnp.repeat(level_sum, spread, axis=2) / float(spread)
    key_grad = token_grad[0].astype(jnp.bfloat16)
    value_grad = token_grad[1].astype(jnp.bfloat16)
    return (attention, query_grad, key_grad, value_grad, weight_grad)


def solution(mesh):
    in_specs = (
        P(("groups", "dp"), "seq", "head"),
        P(("groups", "dp"), "seq", "head"),
        P(("groups", "dp"), "seq", "head"),
        P(("groups", "dp"), "seq", None),
        P("seq", "head"),
        P(("groups", "dp"), "seq", None),
    )
    out_specs = (
        P(("groups", "dp"), "seq", "head"),
        P(("groups", "dp"), "seq", "head"),
        P(("groups", "dp"), "seq", "head"),
        P(("groups", "dp"), "seq", "head"),
        P(("groups", "seq"), "head"),
    )
    return jax.shard_map(shards, mesh=mesh, in_specs=in_specs, out_specs=out_specs, check_vma=False)
```

```python
import math

import jax
import jax.numpy as jnp
from jax import lax
from jax.sharding import PartitionSpec as P

HEAD_DIM = 128
NEAR = 2


def extended(cells, sides, width):
    for axis, dim in sides:
        count = lax.axis_size(axis)
        ends = count - 1
        head = lax.slice_in_dim(cells, 0, width, axis=dim)
        tail = lax.slice_in_dim(cells, cells.shape[dim] - width, cells.shape[dim], axis=dim)
        cells = jnp.concatenate(
            [
                lax.ppermute(tail, axis, [(i, (i + 1) % count) for i in range(ends)]),
                cells,
                lax.ppermute(head, axis, [((i + 1) % count, i) for i in range(ends)]),
            ],
            axis=dim,
        )
    return cells


def swapped(shard, axis, stride):
    return lax.ppermute(shard, axis, [(i, i ^ 1 << stride) for i in range(lax.axis_size(axis))])


def pool_pairs(source):
    shaped = source.reshape(
        source.shape[0], source.shape[1], source.shape[2] // 2, 2, source.shape[3]
    )
    return jnp.sum(shaped, axis=3) * 0.5


def pick_blocks(blocks_doc, chosen_doc):
    return blocks_doc[:, chosen_doc]


def place_blocks(grad_doc, chosen_doc):
    holder = jnp.zeros((grad_doc.shape[0], 6, grad_doc.shape[3], grad_doc.shape[4]), jnp.float32)
    return holder.at[:, chosen_doc].add(grad_doc)


def shards(queries, keys, values, pattern, out_weight, cotangent):
    doc_count, tok_count, head_cols = queries.shape
    block = tok_count // 2
    heads = head_cols // HEAD_DIM
    seq_count = lax.axis_size("seq")
    levels = seq_count.bit_length() - 1
    position = lax.axis_index("seq")
    score_scale = 1.0 / math.sqrt(HEAD_DIM)
    near_width = (NEAR + 1) * block
    key_value = jnp.stack([keys, values])
    padded = extended(key_value, (("seq", 2),), tok_count)
    blocks_six = padded.reshape(2, doc_count, 6, block, head_cols)
    local_ids = jnp.arange(2, dtype=jnp.int32)[None, :, None]
    chosen = jnp.concatenate([local_ids, local_ids + pattern], axis=2) + 2
    near_pair = jax.vmap(pick_blocks, in_axes=(1, 0), out_axes=1)(blocks_six, chosen)
    near_pair = near_pair.reshape(2, doc_count, 2, near_width, head_cols)
    pooled = pool_pairs(key_value.astype(jnp.float32))
    siblings = []
    own_level = pooled
    for level_no in range(levels):
        other = swapped(own_level, "seq", level_no)
        if level_no == 0:
            cotangent, other = lax.optimization_barrier((cotangent, other))
        siblings.append(other)
        if level_no + 1 < levels:
            upper = position >> level_no & 1 == 1
            joined = jnp.where(
                upper,
                jnp.concatenate([other, own_level], axis=2),
                jnp.concatenate([own_level, other], axis=2),
            )
            own_level = pool_pairs(joined)
    far_pair = jnp.concatenate(siblings, axis=2).astype(jnp.bfloat16)
    query_heads = queries.reshape(doc_count, 2, block, heads, HEAD_DIM)
    near_k = near_pair[0].reshape(doc_count, 2, near_width, heads, HEAD_DIM)
    near_v = near_pair[1].reshape(doc_count, 2, near_width, heads, HEAD_DIM)
    far_k = far_pair[0].reshape(doc_count, levels * block, heads, HEAD_DIM)
    far_v = far_pair[1].reshape(doc_count, levels * block, heads, HEAD_DIM)
    score_near = (
        jnp.einsum("dbqhe,dbkhe->dbhqk", query_heads, near_k, preferred_element_type=jnp.float32)
        * score_scale
    )
    score_far = (
        jnp.einsum("dbqhe,dkhe->dbhqk", query_heads, far_k, preferred_element_type=jnp.float32)
        * score_scale
    )
    top = jnp.maximum(
        jnp.max(score_near, axis=-1, keepdims=True), jnp.max(score_far, axis=-1, keepdims=True)
    )
    exp_near = jnp.exp(score_near - top)
    exp_far = jnp.exp(score_far - top)
    total = jnp.sum(exp_near, axis=-1, keepdims=True) + jnp.sum(exp_far, axis=-1, keepdims=True)
    weight_near = exp_near / total
    weight_far = exp_far / total
    rounded_near = weight_near.astype(jnp.bfloat16)
    rounded_far = weight_far.astype(jnp.bfloat16)
    output = jnp.einsum(
        "dbhqk,dbkhe->dbqhe", rounded_near, near_v, preferred_element_type=jnp.float32
    )
    output = output + jnp.einsum(
        "dbhqk,dkhe->dbqhe", rounded_far, far_v, preferred_element_type=jnp.float32
    )
    attention = output.reshape(doc_count, tok_count, head_cols).astype(jnp.bfloat16)
    feat_count = cotangent.shape[2] // seq_count
    cot_rows = cotangent.reshape(doc_count * tok_count, cotangent.shape[2])
    out_rows = attention.reshape(doc_count * tok_count, head_cols)
    own_cols = lax.dynamic_slice_in_dim(cot_rows, position * feat_count, feat_count, axis=1)
    grad_sum = jnp.dot(own_cols, out_weight, preferred_element_type=jnp.float32)
    feat_list = [own_cols]
    for step in range(1, seq_count):
        pairs = [(i, i ^ step) for i in range(seq_count)]
        sent = lax.dynamic_slice_in_dim(
            cot_rows, (position ^ step) * feat_count, feat_count, axis=1
        )
        half = sent.shape[0] // 2
        core = lax.axis_index("head")
        got_half = lax.ppermute(
            lax.dynamic_slice_in_dim(sent, core * half, half, axis=0), "seq", pairs
        )
        other_half = swapped(got_half, "head", 0)
        got = jnp.where(
            core == 0,
            jnp.concatenate([got_half, other_half], axis=0),
            jnp.concatenate([other_half, got_half], axis=0),
        )
        part = jnp.dot(got, out_weight, preferred_element_type=jnp.float32)
        back = lax.ppermute(part.astype(jnp.bfloat16), "seq", pairs)
        grad_sum = grad_sum + back.astype(jnp.float32)
        feat_list.append(got)
    attn_grad = grad_sum.astype(jnp.bfloat16)
    feat_order = jnp.arange(seq_count, dtype=jnp.int32) ^ position
    feat_docs = jnp.take(jnp.stack(feat_list, axis=0), feat_order, axis=0).reshape(
        seq_count * cot_rows.shape[0], feat_count
    )
    feat_docs = lax.all_gather(feat_docs, "dp", axis=0, tiled=True)
    whole_output = lax.all_gather(out_rows, ("dp", "seq"), axis=0, tiled=True)
    weight_grad = jnp.einsum(
        "tc,tw->cw", feat_docs, whole_output, preferred_element_type=jnp.float32
    )
    grad_heads = attn_grad.reshape(doc_count, 2, block, heads, HEAD_DIM)
    prob_near = jnp.einsum(
        "dbqhe,dbkhe->dbhqk", grad_heads, near_v, preferred_element_type=jnp.float32
    )
    prob_far = jnp.einsum(
        "dbqhe,dkhe->dbhqk", grad_heads, far_v, preferred_element_type=jnp.float32
    )
    row_dot = jnp.sum(weight_near * prob_near, axis=-1, keepdims=True) + jnp.sum(
        weight_far * prob_far, axis=-1, keepdims=True
    )
    grad_near = (weight_near * (prob_near - row_dot)).astype(jnp.bfloat16)
    grad_far = (weight_far * (prob_far - row_dot)).astype(jnp.bfloat16)
    query_sum = jnp.einsum(
        "dbhqk,dbkhe->dbqhe", grad_near, near_k, preferred_element_type=jnp.float32
    )
    query_sum = query_sum + jnp.einsum(
        "dbhqk,dkhe->dbqhe", grad_far, far_k, preferred_element_type=jnp.float32
    )
    query_grad = (
        (query_sum * score_scale).reshape(doc_count, tok_count, head_cols).astype(jnp.bfloat16)
    )
    near_key_rows = (
        jnp.einsum("dbhqk,dbqhe->dbkhe", grad_near, query_heads, preferred_element_type=jnp.float32)
        * score_scale
    )
    near_value_rows = jnp.einsum(
        "dbhqk,dbqhe->dbkhe", rounded_near, grad_heads, preferred_element_type=jnp.float32
    )
    far_key_rows = (
        jnp.einsum("dbhqk,dbqhe->dkhe", grad_far, query_heads, preferred_element_type=jnp.float32)
        * score_scale
    )
    far_value_rows = jnp.einsum(
        "dbhqk,dbqhe->dkhe", rounded_far, grad_heads, preferred_element_type=jnp.float32
    )
    near_rows = jnp.stack([near_key_rows, near_value_rows]).reshape(
        2, doc_count, 2, NEAR + 1, block, head_cols
    )
    back_six = jax.vmap(place_blocks, in_axes=(1, 0), out_axes=1)(near_rows, chosen)
    rims = jnp.concatenate([back_six[:, :, 0:2], back_six[:, :, 4:6]], axis=2).reshape(
        2, doc_count, 2 * tok_count, head_cols
    )
    beside_all = extended(rims.astype(jnp.bfloat16), (("seq", 2),), tok_count).astype(
        jnp.float32
    )
    token_grad = back_six[:, :, 2:4].reshape(2, doc_count, tok_count, head_cols)
    token_grad = token_grad + beside_all[:, :, :tok_count] + beside_all[:, :, 3 * tok_count :]
    far_rows = jnp.stack([far_key_rows, far_value_rows]).reshape(
        2, doc_count, levels, block, head_cols
    )
    for level_no in range(levels):
        count = 1 << level_no
        height = block // count
        level_sum = None
        for step in range(count, 2 * count):
            slot = (position ^ step) & (count - 1)
            segment = lax.dynamic_slice_in_dim(far_rows[:, :, level_no], slot * height, height, axis=2)
            returned = lax.ppermute(
                segment.astype(jnp.bfloat16), "seq", [(i, i ^ step) for i in range(seq_count)]
            ).astype(jnp.float32)
            level_sum = returned if level_sum is None else level_sum + returned
        spread = 2 ** (level_no + 1)
        token_grad = token_grad + jnp.repeat(level_sum, spread, axis=2) / float(spread)
    key_grad = token_grad[0].astype(jnp.bfloat16)
    value_grad = token_grad[1].astype(jnp.bfloat16)
    return (attention, query_grad, key_grad, value_grad, weight_grad)


def solution(mesh):
    in_specs = (
        P(("groups", "dp"), "seq", "head"),
        P(("groups", "dp"), "seq", "head"),
        P(("groups", "dp"), "seq", "head"),
        P(("groups", "dp"), "seq", None),
        P("seq", "head"),
        P(("groups", "dp"), "seq", None),
    )
    out_specs = (
        P(("groups", "dp"), "seq", "head"),
        P(("groups", "dp"), "seq", "head"),
        P(("groups", "dp"), "seq", "head"),
        P(("groups", "dp"), "seq", "head"),
        P(("groups", "seq"), "head"),
    )
    return jax.shard_map(shards, mesh=mesh, in_specs=in_specs, out_specs=out_specs, check_vma=False)
```

```python
import math

import jax
import jax.numpy as jnp
from jax import lax
from jax.sharding import PartitionSpec as P

HEAD_DIM = 128
NEAR = 2


def extended(cells, sides, width):
    for axis, dim in sides:
        count = lax.axis_size(axis)
        ends = count - 1
        head = lax.slice_in_dim(cells, 0, width, axis=dim)
        tail = lax.slice_in_dim(cells, cells.shape[dim] - width, cells.shape[dim], axis=dim)
        cells = jnp.concatenate(
            [
                lax.ppermute(tail, axis, [(i, (i + 1) % count) for i in range(ends)]),
                cells,
                lax.ppermute(head, axis, [((i + 1) % count, i) for i in range(ends)]),
            ],
            axis=dim,
        )
    return cells


def swapped(shard, axis, stride):
    return lax.ppermute(shard, axis, [(i, i ^ 1 << stride) for i in range(lax.axis_size(axis))])


def pool_pairs(source):
    shaped = source.reshape(
        source.shape[0], source.shape[1], source.shape[2] // 2, 2, source.shape[3]
    )
    return jnp.sum(shaped, axis=3) * 0.5


def pick_blocks(blocks_doc, chosen_doc):
    return blocks_doc[:, chosen_doc]


def place_blocks(grad_doc, chosen_doc):
    holder = jnp.zeros((grad_doc.shape[0], 6, grad_doc.shape[3], grad_doc.shape[4]), jnp.float32)
    return holder.at[:, chosen_doc].add(grad_doc)


def shards(queries, keys, values, pattern, out_weight, cotangent):
    doc_count, tok_count, head_cols = queries.shape
    block = tok_count // 2
    heads = head_cols // HEAD_DIM
    seq_count = lax.axis_size("seq")
    levels = seq_count.bit_length() - 1
    position = lax.axis_index("seq")
    score_scale = 1.0 / math.sqrt(HEAD_DIM)
    near_width = (NEAR + 1) * block
    key_value = jnp.stack([keys, values])
    padded = extended(key_value, (("seq", 2),), tok_count)
    blocks_six = padded.reshape(2, doc_count, 6, block, head_cols)
    local_ids = jnp.arange(2, dtype=jnp.int32)[None, :, None]
    chosen = jnp.concatenate([local_ids, local_ids + pattern], axis=2) + 2
    near_pair = jax.vmap(pick_blocks, in_axes=(1, 0), out_axes=1)(blocks_six, chosen)
    near_pair = near_pair.reshape(2, doc_count, 2, near_width, head_cols)
    pooled = pool_pairs(key_value.astype(jnp.float32))
    siblings = []
    own_level = pooled
    for level_no in range(levels):
        other = swapped(own_level, "seq", level_no)
        siblings.append(other)
        if level_no + 1 < levels:
            upper = position >> level_no & 1 == 1
            joined = jnp.where(
                upper,
                jnp.concatenate([other, own_level], axis=2),
                jnp.concatenate([own_level, other], axis=2),
            )
            own_level = pool_pairs(joined)
    far_pair = jnp.concatenate(siblings, axis=2).astype(jnp.bfloat16)
    query_heads = queries.reshape(doc_count, 2, block, heads, HEAD_DIM)
    near_k = near_pair[0].reshape(doc_count, 2, near_width, heads, HEAD_DIM)
    near_v = near_pair[1].reshape(doc_count, 2, near_width, heads, HEAD_DIM)
    far_k = far_pair[0].reshape(doc_count, levels * block, heads, HEAD_DIM)
    far_v = far_pair[1].reshape(doc_count, levels * block, heads, HEAD_DIM)
    score_near = (
        jnp.einsum("dbqhe,dbkhe->dbhqk", query_heads, near_k, preferred_element_type=jnp.float32)
        * score_scale
    )
    score_far = (
        jnp.einsum("dbqhe,dkhe->dbhqk", query_heads, far_k, preferred_element_type=jnp.float32)
        * score_scale
    )
    top = jnp.maximum(
        jnp.max(score_near, axis=-1, keepdims=True), jnp.max(score_far, axis=-1, keepdims=True)
    )
    exp_near = jnp.exp(score_near - top)
    exp_far = jnp.exp(score_far - top)
    total = jnp.sum(exp_near, axis=-1, keepdims=True) + jnp.sum(exp_far, axis=-1, keepdims=True)
    weight_near = exp_near / total
    weight_far = exp_far / total
    rounded_near = weight_near.astype(jnp.bfloat16)
    rounded_far = weight_far.astype(jnp.bfloat16)
    output = jnp.einsum(
        "dbhqk,dbkhe->dbqhe", rounded_near, near_v, preferred_element_type=jnp.float32
    )
    output = output + jnp.einsum(
        "dbhqk,dkhe->dbqhe", rounded_far, far_v, preferred_element_type=jnp.float32
    )
    attention = output.reshape(doc_count, tok_count, head_cols).astype(jnp.bfloat16)
    feat_count = cotangent.shape[2] // seq_count
    cot_rows = cotangent.reshape(doc_count * tok_count, cotangent.shape[2])
    out_rows = attention.reshape(doc_count * tok_count, head_cols)
    own_cols = lax.dynamic_slice_in_dim(cot_rows, position * feat_count, feat_count, axis=1)
    grad_sum = jnp.dot(own_cols, out_weight, preferred_element_type=jnp.float32)
    feat_list = [own_cols]
    for step in range(1, seq_count):
        pairs = [(i, i ^ step) for i in range(seq_count)]
        sent = lax.dynamic_slice_in_dim(
            cot_rows, (position ^ step) * feat_count, feat_count, axis=1
        )
        got = lax.ppermute(sent, "seq", pairs)
        part = jnp.dot(got, out_weight, preferred_element_type=jnp.float32)
        back = lax.ppermute(part.astype(jnp.bfloat16), "seq", pairs)
        grad_sum = grad_sum + back.astype(jnp.float32)
        feat_list.append(got)
    attn_grad = grad_sum.astype(jnp.bfloat16)
    feat_order = jnp.arange(seq_count, dtype=jnp.int32) ^ position
    feat_docs = jnp.take(jnp.stack(feat_list, axis=0), feat_order, axis=0).reshape(
        seq_count * cot_rows.shape[0], feat_count
    )
    feat_docs = lax.all_gather(feat_docs, "dp", axis=0, tiled=True)
    whole_output = lax.all_gather(out_rows, ("dp", "seq"), axis=0, tiled=True)
    weight_grad = jnp.einsum(
        "tc,tw->cw", feat_docs, whole_output, preferred_element_type=jnp.float32
    )
    grad_heads = attn_grad.reshape(doc_count, 2, block, heads, HEAD_DIM)
    prob_near = jnp.einsum(
        "dbqhe,dbkhe->dbhqk", grad_heads, near_v, preferred_element_type=jnp.float32
    )
    prob_far = jnp.einsum(
        "dbqhe,dkhe->dbhqk", grad_heads, far_v, preferred_element_type=jnp.float32
    )
    row_dot = jnp.sum(weight_near * prob_near, axis=-1, keepdims=True) + jnp.sum(
        weight_far * prob_far, axis=-1, keepdims=True
    )
    grad_near = (weight_near * (prob_near - row_dot)).astype(jnp.bfloat16)
    grad_far = (weight_far * (prob_far - row_dot)).astype(jnp.bfloat16)
    query_sum = jnp.einsum(
        "dbhqk,dbkhe->dbqhe", grad_near, near_k, preferred_element_type=jnp.float32
    )
    query_sum = query_sum + jnp.einsum(
        "dbhqk,dkhe->dbqhe", grad_far, far_k, preferred_element_type=jnp.float32
    )
    query_grad = (
        (query_sum * score_scale).reshape(doc_count, tok_count, head_cols).astype(jnp.bfloat16)
    )
    near_key_rows = (
        jnp.einsum("dbhqk,dbqhe->dbkhe", grad_near, query_heads, preferred_element_type=jnp.float32)
        * score_scale
    )
    near_value_rows = jnp.einsum(
        "dbhqk,dbqhe->dbkhe", rounded_near, grad_heads, preferred_element_type=jnp.float32
    )
    far_key_rows = (
        jnp.einsum("dbhqk,dbqhe->dkhe", grad_far, query_heads, preferred_element_type=jnp.float32)
        * score_scale
    )
    far_value_rows = jnp.einsum(
        "dbhqk,dbqhe->dkhe", rounded_far, grad_heads, preferred_element_type=jnp.float32
    )
    near_rows = jnp.stack([near_key_rows, near_value_rows]).reshape(
        2, doc_count, 2, NEAR + 1, block, head_cols
    )
    back_six = jax.vmap(place_blocks, in_axes=(1, 0), out_axes=1)(near_rows, chosen)
    rims = jnp.concatenate([back_six[:, :, 0:2], back_six[:, :, 4:6]], axis=2).reshape(
        2, doc_count, 2 * tok_count, head_cols
    )
    beside_all = extended(rims.astype(jnp.bfloat16), (("seq", 2),), tok_count).astype(
        jnp.float32
    )
    token_grad = back_six[:, :, 2:4].reshape(2, doc_count, tok_count, head_cols)
    token_grad = token_grad + beside_all[:, :, :tok_count] + beside_all[:, :, 3 * tok_count :]
    far_rows = jnp.stack([far_key_rows, far_value_rows]).reshape(
        2, doc_count, levels, block, head_cols
    )
    for level_no in range(levels):
        count = 1 << level_no
        height = block // count
        level_sum = None
        for step in range(count, 2 * count):
            slot = (position ^ step) & (count - 1)
            segment = lax.dynamic_slice_in_dim(far_rows[:, :, level_no], slot * height, height, axis=2)
            returned = lax.ppermute(
                segment.astype(jnp.bfloat16), "seq", [(i, i ^ step) for i in range(seq_count)]
            ).astype(jnp.float32)
            level_sum = returned if level_sum is None else level_sum + returned
        spread = 2 ** (level_no + 1)
        token_grad = token_grad + jnp.repeat(level_sum, spread, axis=2) / float(spread)
    key_grad = token_grad[0].astype(jnp.bfloat16)
    value_grad = token_grad[1].astype(jnp.bfloat16)
    return (attention, query_grad, key_grad, value_grad, weight_grad)


def solution(mesh):
    in_specs = (
        P(("groups", "dp"), "seq", "head"),
        P(("groups", "dp"), "seq", "head"),
        P(("groups", "dp"), "seq", "head"),
        P(("groups", "dp"), "seq", None),
        P("seq", "head"),
        P(("groups", "dp"), "seq", None),
    )
    out_specs = (
        P(("groups", "dp"), "seq", "head"),
        P(("groups", "dp"), "seq", "head"),
        P(("groups", "dp"), "seq", "head"),
        P(("groups", "dp"), "seq", "head"),
        P(("groups", "seq"), "head"),
    )
    return jax.shard_map(shards, mesh=mesh, in_specs=in_specs, out_specs=out_specs, check_vma=False)
```

```python
import math

import jax
import jax.numpy as jnp
from jax import lax
from jax.sharding import PartitionSpec as P

HEAD_DIM = 128
NEAR = 2


def extended(cells, sides, width):
    for axis, dim in sides:
        count = lax.axis_size(axis)
        ends = count - 1
        head = lax.slice_in_dim(cells, 0, width, axis=dim)
        tail = lax.slice_in_dim(cells, cells.shape[dim] - width, cells.shape[dim], axis=dim)
        cells = jnp.concatenate(
            [
                lax.ppermute(tail, axis, [(i, (i + 1) % count) for i in range(ends)]),
                cells,
                lax.ppermute(head, axis, [((i + 1) % count, i) for i in range(ends)]),
            ],
            axis=dim,
        )
    return cells


def swapped(shard, axis, stride):
    return lax.ppermute(shard, axis, [(i, i ^ 1 << stride) for i in range(lax.axis_size(axis))])


def pool_pairs(source):
    shaped = source.reshape(
        source.shape[0], source.shape[1], source.shape[2] // 2, 2, source.shape[3]
    )
    return jnp.sum(shaped, axis=3) * 0.5


def pick_blocks(blocks_doc, chosen_doc):
    return blocks_doc[:, chosen_doc]


def place_blocks(grad_doc, chosen_doc):
    holder = jnp.zeros((grad_doc.shape[0], 6, grad_doc.shape[3], grad_doc.shape[4]), jnp.float32)
    return holder.at[:, chosen_doc].add(grad_doc)


def shards(queries, keys, values, pattern, out_weight, cotangent):
    doc_count, tok_count, head_cols = queries.shape
    block = tok_count // 2
    heads = head_cols // HEAD_DIM
    seq_count = lax.axis_size("seq")
    levels = seq_count.bit_length() - 1
    position = lax.axis_index("seq")
    score_scale = 1.0 / math.sqrt(HEAD_DIM)
    near_width = (NEAR + 1) * block
    key_value = jnp.stack([keys, values])
    padded = extended(key_value, (("seq", 2),), tok_count)
    blocks_six = padded.reshape(2, doc_count, 6, block, head_cols)
    local_ids = jnp.arange(2, dtype=jnp.int32)[None, :, None]
    chosen = jnp.concatenate([local_ids, local_ids + pattern], axis=2) + 2
    near_pair = jax.vmap(pick_blocks, in_axes=(1, 0), out_axes=1)(blocks_six, chosen)
    near_pair = near_pair.reshape(2, doc_count, 2, near_width, head_cols)
    pieces = []
    level_rows = key_value.astype(jnp.float32)
    for level_no in range(levels):
        level_rows = pool_pairs(level_rows)
        pieces.append(level_rows.astype(jnp.bfloat16))
    far_levels = []
    for level_no in range(levels):
        count = 1 << level_no
        group = jnp.stack(
            [
                lax.ppermute(pieces[level_no], "seq", [(i, i ^ step) for i in range(seq_count)])
                for step in range(count, 2 * count)
            ],
            axis=0,
        )
        order = jnp.arange(count, dtype=jnp.int32) ^ (position & (count - 1))
        group = jnp.take(group, order, axis=0)
        far_levels.append(
            jnp.moveaxis(group, 0, 2).reshape(2, doc_count, count * group.shape[3], head_cols)
        )
    far_pair = jnp.concatenate(far_levels, axis=2)
    query_heads = queries.reshape(doc_count, 2, block, heads, HEAD_DIM)
    near_k = near_pair[0].reshape(doc_count, 2, near_width, heads, HEAD_DIM)
    near_v = near_pair[1].reshape(doc_count, 2, near_width, heads, HEAD_DIM)
    far_k = far_pair[0].reshape(doc_count, levels * block, heads, HEAD_DIM)
    far_v = far_pair[1].reshape(doc_count, levels * block, heads, HEAD_DIM)
    score_near = (
        jnp.einsum("dbqhe,dbkhe->dbhqk", query_heads, near_k, preferred_element_type=jnp.float32)
        * score_scale
    )
    score_far = (
        jnp.einsum("dbqhe,dkhe->dbhqk", query_heads, far_k, preferred_element_type=jnp.float32)
        * score_scale
    )
    top = jnp.maximum(
        jnp.max(score_near, axis=-1, keepdims=True), jnp.max(score_far, axis=-1, keepdims=True)
    )
    exp_near = jnp.exp(score_near - top)
    exp_far = jnp.exp(score_far - top)
    total = jnp.sum(exp_near, axis=-1, keepdims=True) + jnp.sum(exp_far, axis=-1, keepdims=True)
    weight_near = exp_near / total
    weight_far = exp_far / total
    rounded_near = weight_near.astype(jnp.bfloat16)
    rounded_far = weight_far.astype(jnp.bfloat16)
    output = jnp.einsum(
        "dbhqk,dbkhe->dbqhe", rounded_near, near_v, preferred_element_type=jnp.float32
    )
    output = output + jnp.einsum(
        "dbhqk,dkhe->dbqhe", rounded_far, far_v, preferred_element_type=jnp.float32
    )
    attention = output.reshape(doc_count, tok_count, head_cols).astype(jnp.bfloat16)
    feat_count = cotangent.shape[2] // seq_count
    cot_rows = cotangent.reshape(doc_count * tok_count, cotangent.shape[2])
    out_rows = attention.reshape(doc_count * tok_count, head_cols)
    own_cols = lax.dynamic_slice_in_dim(cot_rows, position * feat_count, feat_count, axis=1)
    grad_sum = jnp.dot(own_cols, out_weight, preferred_element_type=jnp.float32)
    feat_list = [own_cols]
    for step in range(1, seq_count):
        pairs = [(i, i ^ step) for i in range(seq_count)]
        sent = lax.dynamic_slice_in_dim(
            cot_rows, (position ^ step) * feat_count, feat_count, axis=1
        )
        half = sent.shape[0] // 2
        core = lax.axis_index("head")
        got_half = lax.ppermute(
            lax.dynamic_slice_in_dim(sent, core * half, half, axis=0), "seq", pairs
        )
        other_half = swapped(got_half, "head", 0)
        got = jnp.where(
            core == 0,
            jnp.concatenate([got_half, other_half], axis=0),
            jnp.concatenate([other_half, got_half], axis=0),
        )
        part = jnp.dot(got, out_weight, preferred_element_type=jnp.float32)
        back = lax.ppermute(part.astype(jnp.bfloat16), "seq", pairs)
        grad_sum = grad_sum + back.astype(jnp.float32)
        feat_list.append(got)
    attn_grad = grad_sum.astype(jnp.bfloat16)
    feat_order = jnp.arange(seq_count, dtype=jnp.int32) ^ position
    feat_docs = jnp.take(jnp.stack(feat_list, axis=0), feat_order, axis=0).reshape(
        seq_count * cot_rows.shape[0], feat_count
    )
    feat_docs = lax.all_gather(feat_docs, "dp", axis=0, tiled=True)
    whole_output = lax.all_gather(out_rows, ("dp", "seq"), axis=0, tiled=True)
    weight_grad = jnp.einsum(
        "tc,tw->cw", feat_docs, whole_output, preferred_element_type=jnp.float32
    )
    grad_heads = attn_grad.reshape(doc_count, 2, block, heads, HEAD_DIM)
    prob_near = jnp.einsum(
        "dbqhe,dbkhe->dbhqk", grad_heads, near_v, preferred_element_type=jnp.float32
    )
    prob_far = jnp.einsum(
        "dbqhe,dkhe->dbhqk", grad_heads, far_v, preferred_element_type=jnp.float32
    )
    row_dot = jnp.sum(weight_near * prob_near, axis=-1, keepdims=True) + jnp.sum(
        weight_far * prob_far, axis=-1, keepdims=True
    )
    grad_near = (weight_near * (prob_near - row_dot)).astype(jnp.bfloat16)
    grad_far = (weight_far * (prob_far - row_dot)).astype(jnp.bfloat16)
    query_sum = jnp.einsum(
        "dbhqk,dbkhe->dbqhe", grad_near, near_k, preferred_element_type=jnp.float32
    )
    query_sum = query_sum + jnp.einsum(
        "dbhqk,dkhe->dbqhe", grad_far, far_k, preferred_element_type=jnp.float32
    )
    query_grad = (
        (query_sum * score_scale).reshape(doc_count, tok_count, head_cols).astype(jnp.bfloat16)
    )
    near_key_rows = (
        jnp.einsum("dbhqk,dbqhe->dbkhe", grad_near, query_heads, preferred_element_type=jnp.float32)
        * score_scale
    )
    near_value_rows = jnp.einsum(
        "dbhqk,dbqhe->dbkhe", rounded_near, grad_heads, preferred_element_type=jnp.float32
    )
    far_key_rows = (
        jnp.einsum("dbhqk,dbqhe->dkhe", grad_far, query_heads, preferred_element_type=jnp.float32)
        * score_scale
    )
    far_value_rows = jnp.einsum(
        "dbhqk,dbqhe->dkhe", rounded_far, grad_heads, preferred_element_type=jnp.float32
    )
    near_rows = jnp.stack([near_key_rows, near_value_rows]).reshape(
        2, doc_count, 2, NEAR + 1, block, head_cols
    )
    back_six = jax.vmap(place_blocks, in_axes=(1, 0), out_axes=1)(near_rows, chosen)
    rims = jnp.concatenate([back_six[:, :, 0:2], back_six[:, :, 4:6]], axis=2).reshape(
        2, doc_count, 2 * tok_count, head_cols
    )
    beside_all = extended(rims.astype(jnp.bfloat16), (("seq", 2),), tok_count).astype(
        jnp.float32
    )
    token_grad = back_six[:, :, 2:4].reshape(2, doc_count, tok_count, head_cols)
    token_grad = token_grad + beside_all[:, :, :tok_count] + beside_all[:, :, 3 * tok_count :]
    far_rows = jnp.stack([far_key_rows, far_value_rows]).reshape(
        2, doc_count, levels, block, head_cols
    )
    for level_no in range(levels):
        count = 1 << level_no
        height = block // count
        level_sum = None
        for step in range(count, 2 * count):
            slot = (position ^ step) & (count - 1)
            segment = lax.dynamic_slice_in_dim(far_rows[:, :, level_no], slot * height, height, axis=2)
            returned = lax.ppermute(
                segment.astype(jnp.bfloat16), "seq", [(i, i ^ step) for i in range(seq_count)]
            ).astype(jnp.float32)
            level_sum = returned if level_sum is None else level_sum + returned
        spread = 2 ** (level_no + 1)
        token_grad = token_grad + jnp.repeat(level_sum, spread, axis=2) / float(spread)
    key_grad = token_grad[0].astype(jnp.bfloat16)
    value_grad = token_grad[1].astype(jnp.bfloat16)
    return (attention, query_grad, key_grad, value_grad, weight_grad)


def solution(mesh):
    in_specs = (
        P(("groups", "dp"), "seq", "head"),
        P(("groups", "dp"), "seq", "head"),
        P(("groups", "dp"), "seq", "head"),
        P(("groups", "dp"), "seq", None),
        P("seq", "head"),
        P(("groups", "dp"), "seq", None),
    )
    out_specs = (
        P(("groups", "dp"), "seq", "head"),
        P(("groups", "dp"), "seq", "head"),
        P(("groups", "dp"), "seq", "head"),
        P(("groups", "dp"), "seq", "head"),
        P(("groups", "seq"), "head"),
    )
    return jax.shard_map(shards, mesh=mesh, in_specs=in_specs, out_specs=out_specs, check_vma=False)
```

```python
import math

import jax
import jax.numpy as jnp
from jax import lax
from jax.sharding import PartitionSpec as P

HEAD_DIM = 128
NEAR = 2


def extended(cells, sides, width):
    for axis, dim in sides:
        count = lax.axis_size(axis)
        ends = count - 1
        head = lax.slice_in_dim(cells, 0, width, axis=dim)
        tail = lax.slice_in_dim(cells, cells.shape[dim] - width, cells.shape[dim], axis=dim)
        cells = jnp.concatenate(
            [
                lax.ppermute(tail, axis, [(i, (i + 1) % count) for i in range(ends)]),
                cells,
                lax.ppermute(head, axis, [((i + 1) % count, i) for i in range(ends)]),
            ],
            axis=dim,
        )
    return cells


def swapped(shard, axis, stride):
    return lax.ppermute(shard, axis, [(i, i ^ 1 << stride) for i in range(lax.axis_size(axis))])


def pool_pairs(source):
    shaped = source.reshape(
        source.shape[0], source.shape[1], source.shape[2] // 2, 2, source.shape[3]
    )
    return jnp.sum(shaped, axis=3) * 0.5


def pick_blocks(blocks_doc, chosen_doc):
    return blocks_doc[:, chosen_doc]


def place_blocks(grad_doc, chosen_doc):
    holder = jnp.zeros((grad_doc.shape[0], 6, grad_doc.shape[3], grad_doc.shape[4]), jnp.float32)
    return holder.at[:, chosen_doc].add(grad_doc)


def shards(queries, keys, values, pattern, out_weight, cotangent):
    doc_count, tok_count, head_cols = queries.shape
    block = tok_count // 2
    heads = head_cols // HEAD_DIM
    seq_count = lax.axis_size("seq")
    levels = seq_count.bit_length() - 1
    position = lax.axis_index("seq")
    score_scale = 1.0 / math.sqrt(HEAD_DIM)
    near_width = (NEAR + 1) * block
    key_value = jnp.stack([keys, values])
    padded = extended(key_value, (("seq", 2),), tok_count)
    blocks_six = padded.reshape(2, doc_count, 6, block, head_cols)
    local_ids = jnp.arange(2, dtype=jnp.int32)[None, :, None]
    chosen = jnp.concatenate([local_ids, local_ids + pattern], axis=2) + 2
    near_pair = jax.vmap(pick_blocks, in_axes=(1, 0), out_axes=1)(blocks_six, chosen)
    near_pair = near_pair.reshape(2, doc_count, 2, near_width, head_cols)
    pieces = []
    level_rows = key_value.astype(jnp.float32)
    for level_no in range(levels):
        level_rows = pool_pairs(level_rows)
        pieces.append(level_rows.astype(jnp.bfloat16))
    far_levels = []
    for level_no in range(levels):
        count = 1 << level_no
        group = jnp.stack(
            [
                lax.ppermute(pieces[level_no], "seq", [(i, i ^ step) for i in range(seq_count)])
                for step in range(count, 2 * count)
            ],
            axis=0,
        )
        order = jnp.arange(count, dtype=jnp.int32) ^ (position & (count - 1))
        group = jnp.take(group, order, axis=0)
        far_levels.append(
            jnp.moveaxis(group, 0, 2).reshape(2, doc_count, count * group.shape[3], head_cols)
        )
    far_pair = jnp.concatenate(far_levels, axis=2)
    query_heads = queries.reshape(doc_count, 2, block, heads, HEAD_DIM)
    near_k = near_pair[0].reshape(doc_count, 2, near_width, heads, HEAD_DIM)
    near_v = near_pair[1].reshape(doc_count, 2, near_width, heads, HEAD_DIM)
    far_k = far_pair[0].reshape(doc_count, levels * block, heads, HEAD_DIM)
    far_v = far_pair[1].reshape(doc_count, levels * block, heads, HEAD_DIM)
    score_near = (
        jnp.einsum("dbqhe,dbkhe->dbhqk", query_heads, near_k, preferred_element_type=jnp.float32)
        * score_scale
    )
    score_far = (
        jnp.einsum("dbqhe,dkhe->dbhqk", query_heads, far_k, preferred_element_type=jnp.float32)
        * score_scale
    )
    top = jnp.maximum(
        jnp.max(score_near, axis=-1, keepdims=True), jnp.max(score_far, axis=-1, keepdims=True)
    )
    exp_near = jnp.exp(score_near - top)
    exp_far = jnp.exp(score_far - top)
    total = jnp.sum(exp_near, axis=-1, keepdims=True) + jnp.sum(exp_far, axis=-1, keepdims=True)
    weight_near = exp_near / total
    weight_far = exp_far / total
    rounded_near = weight_near.astype(jnp.bfloat16)
    rounded_far = weight_far.astype(jnp.bfloat16)
    output = jnp.einsum(
        "dbhqk,dbkhe->dbqhe", rounded_near, near_v, preferred_element_type=jnp.float32
    )
    output = output + jnp.einsum(
        "dbhqk,dkhe->dbqhe", rounded_far, far_v, preferred_element_type=jnp.float32
    )
    attention = output.reshape(doc_count, tok_count, head_cols).astype(jnp.bfloat16)
    feat_count = cotangent.shape[2] // seq_count
    cot_rows = cotangent.reshape(doc_count * tok_count, cotangent.shape[2])
    out_rows = attention.reshape(doc_count * tok_count, head_cols)
    own_cols = lax.dynamic_slice_in_dim(cot_rows, position * feat_count, feat_count, axis=1)
    grad_sum = jnp.dot(own_cols, out_weight, preferred_element_type=jnp.float32)
    feat_list = [own_cols]
    for step in range(1, seq_count):
        pairs = [(i, i ^ step) for i in range(seq_count)]
        sent = lax.dynamic_slice_in_dim(
            cot_rows, (position ^ step) * feat_count, feat_count, axis=1
        )
        half = sent.shape[0] // 2
        core = lax.axis_index("head")
        got_half = lax.ppermute(
            lax.dynamic_slice_in_dim(sent, core * half, half, axis=0), "seq", pairs
        )
        other_half = swapped(got_half, "head", 0)
        got = jnp.where(
            core == 0,
            jnp.concatenate([got_half, other_half], axis=0),
            jnp.concatenate([other_half, got_half], axis=0),
        )
        part = jnp.dot(got, out_weight, preferred_element_type=jnp.float32)
        back = lax.ppermute(part.astype(jnp.bfloat16), "seq", pairs)
        grad_sum = grad_sum + back.astype(jnp.float32)
        feat_list.append(got)
    attn_grad = grad_sum.astype(jnp.bfloat16)
    feat_order = jnp.arange(seq_count, dtype=jnp.int32) ^ position
    feat_docs = jnp.take(jnp.stack(feat_list, axis=0), feat_order, axis=0).reshape(
        seq_count * cot_rows.shape[0], feat_count
    )
    if lax.axis_size("dp") == 2:
        feat_docs = jnp.take(
            jnp.stack([feat_docs, swapped(feat_docs, "dp", 0)], axis=0),
            jnp.arange(2, dtype=jnp.int32) ^ lax.axis_index("dp"),
            axis=0,
        ).reshape(2 * feat_docs.shape[0], feat_count)
    else:
        feat_docs = lax.all_gather(feat_docs, "dp", axis=0, tiled=True)
    whole_output = lax.all_gather(out_rows, ("dp", "seq"), axis=0, tiled=True)
    weight_grad = jnp.einsum(
        "tc,tw->cw", feat_docs, whole_output, preferred_element_type=jnp.float32
    )
    grad_heads = attn_grad.reshape(doc_count, 2, block, heads, HEAD_DIM)
    prob_near = jnp.einsum(
        "dbqhe,dbkhe->dbhqk", grad_heads, near_v, preferred_element_type=jnp.float32
    )
    prob_far = jnp.einsum(
        "dbqhe,dkhe->dbhqk", grad_heads, far_v, preferred_element_type=jnp.float32
    )
    row_dot = jnp.sum(weight_near * prob_near, axis=-1, keepdims=True) + jnp.sum(
        weight_far * prob_far, axis=-1, keepdims=True
    )
    grad_near = (weight_near * (prob_near - row_dot)).astype(jnp.bfloat16)
    grad_far = (weight_far * (prob_far - row_dot)).astype(jnp.bfloat16)
    query_sum = jnp.einsum(
        "dbhqk,dbkhe->dbqhe", grad_near, near_k, preferred_element_type=jnp.float32
    )
    query_sum = query_sum + jnp.einsum(
        "dbhqk,dkhe->dbqhe", grad_far, far_k, preferred_element_type=jnp.float32
    )
    query_grad = (
        (query_sum * score_scale).reshape(doc_count, tok_count, head_cols).astype(jnp.bfloat16)
    )
    near_key_rows = (
        jnp.einsum("dbhqk,dbqhe->dbkhe", grad_near, query_heads, preferred_element_type=jnp.float32)
        * score_scale
    )
    near_value_rows = jnp.einsum(
        "dbhqk,dbqhe->dbkhe", rounded_near, grad_heads, preferred_element_type=jnp.float32
    )
    far_key_rows = (
        jnp.einsum("dbhqk,dbqhe->dkhe", grad_far, query_heads, preferred_element_type=jnp.float32)
        * score_scale
    )
    far_value_rows = jnp.einsum(
        "dbhqk,dbqhe->dkhe", rounded_far, grad_heads, preferred_element_type=jnp.float32
    )
    near_rows = jnp.stack([near_key_rows, near_value_rows]).reshape(
        2, doc_count, 2, NEAR + 1, block, head_cols
    )
    back_six = jax.vmap(place_blocks, in_axes=(1, 0), out_axes=1)(near_rows, chosen)
    rims = jnp.concatenate([back_six[:, :, 0:2], back_six[:, :, 4:6]], axis=2).reshape(
        2, doc_count, 2 * tok_count, head_cols
    )
    beside_all = extended(rims.astype(jnp.bfloat16), (("seq", 2),), tok_count).astype(
        jnp.float32
    )
    token_grad = back_six[:, :, 2:4].reshape(2, doc_count, tok_count, head_cols)
    token_grad = token_grad + beside_all[:, :, :tok_count] + beside_all[:, :, 3 * tok_count :]
    far_rows = jnp.stack([far_key_rows, far_value_rows]).reshape(
        2, doc_count, levels, block, head_cols
    )
    for level_no in range(levels):
        count = 1 << level_no
        height = block // count
        level_sum = None
        for step in range(count, 2 * count):
            slot = (position ^ step) & (count - 1)
            segment = lax.dynamic_slice_in_dim(far_rows[:, :, level_no], slot * height, height, axis=2)
            returned = lax.ppermute(
                segment.astype(jnp.bfloat16), "seq", [(i, i ^ step) for i in range(seq_count)]
            ).astype(jnp.float32)
            level_sum = returned if level_sum is None else level_sum + returned
        spread = 2 ** (level_no + 1)
        token_grad = token_grad + jnp.repeat(level_sum, spread, axis=2) / float(spread)
    key_grad = token_grad[0].astype(jnp.bfloat16)
    value_grad = token_grad[1].astype(jnp.bfloat16)
    return (attention, query_grad, key_grad, value_grad, weight_grad)


def solution(mesh):
    in_specs = (
        P(("groups", "dp"), "seq", "head"),
        P(("groups", "dp"), "seq", "head"),
        P(("groups", "dp"), "seq", "head"),
        P(("groups", "dp"), "seq", None),
        P("seq", "head"),
        P(("groups", "dp"), "seq", None),
    )
    out_specs = (
        P(("groups", "dp"), "seq", "head"),
        P(("groups", "dp"), "seq", "head"),
        P(("groups", "dp"), "seq", "head"),
        P(("groups", "dp"), "seq", "head"),
        P(("groups", "seq"), "head"),
    )
    return jax.shard_map(shards, mesh=mesh, in_specs=in_specs, out_specs=out_specs, check_vma=False)
```

```python
import math

import jax
import jax.numpy as jnp
from jax import lax
from jax.sharding import PartitionSpec as P

HEAD_DIM = 128
NEAR = 2


def extended(cells, sides, width):
    for axis, dim in sides:
        count = lax.axis_size(axis)
        ends = count - 1
        head = lax.slice_in_dim(cells, 0, width, axis=dim)
        tail = lax.slice_in_dim(cells, cells.shape[dim] - width, cells.shape[dim], axis=dim)
        cells = jnp.concatenate(
            [
                lax.ppermute(tail, axis, [(i, (i + 1) % count) for i in range(ends)]),
                cells,
                lax.ppermute(head, axis, [((i + 1) % count, i) for i in range(ends)]),
            ],
            axis=dim,
        )
    return cells


def swapped(shard, axis, stride):
    return lax.ppermute(shard, axis, [(i, i ^ 1 << stride) for i in range(lax.axis_size(axis))])


def pool_pairs(source):
    shaped = source.reshape(
        source.shape[0], source.shape[1], source.shape[2] // 2, 2, source.shape[3]
    )
    return jnp.sum(shaped, axis=3) * 0.5


def pick_blocks(blocks_doc, chosen_doc):
    return blocks_doc[:, chosen_doc]


def place_blocks(grad_doc, chosen_doc):
    holder = jnp.zeros((grad_doc.shape[0], 6, grad_doc.shape[3], grad_doc.shape[4]), jnp.float32)
    return holder.at[:, chosen_doc].add(grad_doc)


def shards(queries, keys, values, pattern, out_weight, cotangent):
    doc_count, tok_count, head_cols = queries.shape
    block = tok_count // 2
    heads = head_cols // HEAD_DIM
    seq_count = lax.axis_size("seq")
    levels = seq_count.bit_length() - 1
    position = lax.axis_index("seq")
    score_scale = 1.0 / math.sqrt(HEAD_DIM)
    near_width = (NEAR + 1) * block
    key_value = jnp.stack([keys, values])
    padded = extended(key_value, (("seq", 2),), tok_count)
    blocks_six = padded.reshape(2, doc_count, 6, block, head_cols)
    local_ids = jnp.arange(2, dtype=jnp.int32)[None, :, None]
    chosen = jnp.concatenate([local_ids, local_ids + pattern], axis=2) + 2
    near_pair = jax.vmap(pick_blocks, in_axes=(1, 0), out_axes=1)(blocks_six, chosen)
    near_pair = near_pair.reshape(2, doc_count, 2, near_width, head_cols)
    pieces = []
    level_rows = key_value.astype(jnp.float32)
    for level_no in range(levels):
        level_rows = pool_pairs(level_rows)
        pieces.append(level_rows.astype(jnp.bfloat16))
    far_levels = []
    for level_no in range(levels):
        count = 1 << level_no
        group = jnp.stack(
            [
                lax.ppermute(pieces[level_no], "seq", [(i, i ^ step) for i in range(seq_count)])
                for step in range(count, 2 * count)
            ],
            axis=0,
        )
        order = jnp.arange(count, dtype=jnp.int32) ^ (position & (count - 1))
        group = jnp.take(group, order, axis=0)
        far_levels.append(
            jnp.moveaxis(group, 0, 2).reshape(2, doc_count, count * group.shape[3], head_cols)
        )
    far_pair = jnp.concatenate(far_levels, axis=2)
    query_heads = queries.reshape(doc_count, 2, block, heads, HEAD_DIM)
    near_k = near_pair[0].reshape(doc_count, 2, near_width, heads, HEAD_DIM)
    near_v = near_pair[1].reshape(doc_count, 2, near_width, heads, HEAD_DIM)
    far_k = far_pair[0].reshape(doc_count, levels * block, heads, HEAD_DIM)
    far_v = far_pair[1].reshape(doc_count, levels * block, heads, HEAD_DIM)
    score_near = (
        jnp.einsum("dbqhe,dbkhe->dbhqk", query_heads, near_k, preferred_element_type=jnp.float32)
        * score_scale
    )
    score_far = (
        jnp.einsum("dbqhe,dkhe->dbhqk", query_heads, far_k, preferred_element_type=jnp.float32)
        * score_scale
    )
    top = jnp.maximum(
        jnp.max(score_near, axis=-1, keepdims=True), jnp.max(score_far, axis=-1, keepdims=True)
    )
    exp_near = jnp.exp(score_near - top)
    exp_far = jnp.exp(score_far - top)
    total = jnp.sum(exp_near, axis=-1, keepdims=True) + jnp.sum(exp_far, axis=-1, keepdims=True)
    weight_near = exp_near / total
    weight_far = exp_far / total
    rounded_near = weight_near.astype(jnp.bfloat16)
    rounded_far = weight_far.astype(jnp.bfloat16)
    output = jnp.einsum(
        "dbhqk,dbkhe->dbqhe", rounded_near, near_v, preferred_element_type=jnp.float32
    )
    output = output + jnp.einsum(
        "dbhqk,dkhe->dbqhe", rounded_far, far_v, preferred_element_type=jnp.float32
    )
    attention = output.reshape(doc_count, tok_count, head_cols).astype(jnp.bfloat16)
    feat_count = cotangent.shape[2] // seq_count
    cot_rows = cotangent.reshape(doc_count * tok_count, cotangent.shape[2])
    out_rows = attention.reshape(doc_count * tok_count, head_cols)
    own_cols = lax.dynamic_slice_in_dim(cot_rows, position * feat_count, feat_count, axis=1)
    grad_sum = jnp.dot(own_cols, out_weight, preferred_element_type=jnp.float32)
    feat_list = [own_cols]
    for step in range(1, seq_count):
        pairs = [(i, i ^ step) for i in range(seq_count)]
        sent = lax.dynamic_slice_in_dim(
            cot_rows, (position ^ step) * feat_count, feat_count, axis=1
        )
        half = sent.shape[0] // 2
        core = lax.axis_index("head")
        got_half = lax.ppermute(
            lax.dynamic_slice_in_dim(sent, core * half, half, axis=0), "seq", pairs
        )
        other_half = swapped(got_half, "head", 0)
        got = jnp.where(
            core == 0,
            jnp.concatenate([got_half, other_half], axis=0),
            jnp.concatenate([other_half, got_half], axis=0),
        )
        feat_list.append(got)
    feat_list, attention = lax.optimization_barrier((feat_list, attention))
    out_rows = attention.reshape(doc_count * tok_count, head_cols)
    for step in range(1, seq_count):
        pairs = [(i, i ^ step) for i in range(seq_count)]
        part = jnp.dot(feat_list[step], out_weight, preferred_element_type=jnp.float32)
        back = lax.ppermute(part.astype(jnp.bfloat16), "seq", pairs)
        grad_sum = grad_sum + back.astype(jnp.float32)
    attn_grad = grad_sum.astype(jnp.bfloat16)
    feat_order = jnp.arange(seq_count, dtype=jnp.int32) ^ position
    feat_docs = jnp.take(jnp.stack(feat_list, axis=0), feat_order, axis=0).reshape(
        seq_count * cot_rows.shape[0], feat_count
    )
    if lax.axis_size("dp") == 2:
        feat_docs = jnp.take(
            jnp.stack([feat_docs, swapped(feat_docs, "dp", 0)], axis=0),
            jnp.arange(2, dtype=jnp.int32) ^ lax.axis_index("dp"),
            axis=0,
        ).reshape(2 * feat_docs.shape[0], feat_count)
    else:
        feat_docs = lax.all_gather(feat_docs, "dp", axis=0, tiled=True)
    whole_output = lax.all_gather(out_rows, ("dp", "seq"), axis=0, tiled=True)
    weight_grad = jnp.einsum(
        "tc,tw->cw", feat_docs, whole_output, preferred_element_type=jnp.float32
    )
    grad_heads = attn_grad.reshape(doc_count, 2, block, heads, HEAD_DIM)
    prob_near = jnp.einsum(
        "dbqhe,dbkhe->dbhqk", grad_heads, near_v, preferred_element_type=jnp.float32
    )
    prob_far = jnp.einsum(
        "dbqhe,dkhe->dbhqk", grad_heads, far_v, preferred_element_type=jnp.float32
    )
    row_dot = jnp.sum(weight_near * prob_near, axis=-1, keepdims=True) + jnp.sum(
        weight_far * prob_far, axis=-1, keepdims=True
    )
    grad_near = (weight_near * (prob_near - row_dot)).astype(jnp.bfloat16)
    grad_far = (weight_far * (prob_far - row_dot)).astype(jnp.bfloat16)
    query_sum = jnp.einsum(
        "dbhqk,dbkhe->dbqhe", grad_near, near_k, preferred_element_type=jnp.float32
    )
    query_sum = query_sum + jnp.einsum(
        "dbhqk,dkhe->dbqhe", grad_far, far_k, preferred_element_type=jnp.float32
    )
    query_grad = (
        (query_sum * score_scale).reshape(doc_count, tok_count, head_cols).astype(jnp.bfloat16)
    )
    near_key_rows = (
        jnp.einsum("dbhqk,dbqhe->dbkhe", grad_near, query_heads, preferred_element_type=jnp.float32)
        * score_scale
    )
    near_value_rows = jnp.einsum(
        "dbhqk,dbqhe->dbkhe", rounded_near, grad_heads, preferred_element_type=jnp.float32
    )
    far_key_rows = (
        jnp.einsum("dbhqk,dbqhe->dkhe", grad_far, query_heads, preferred_element_type=jnp.float32)
        * score_scale
    )
    far_value_rows = jnp.einsum(
        "dbhqk,dbqhe->dkhe", rounded_far, grad_heads, preferred_element_type=jnp.float32
    )
    near_rows = jnp.stack([near_key_rows, near_value_rows]).reshape(
        2, doc_count, 2, NEAR + 1, block, head_cols
    )
    back_six = jax.vmap(place_blocks, in_axes=(1, 0), out_axes=1)(near_rows, chosen)
    rims = jnp.concatenate([back_six[:, :, 0:2], back_six[:, :, 4:6]], axis=2).reshape(
        2, doc_count, 2 * tok_count, head_cols
    )
    beside_all = extended(rims.astype(jnp.bfloat16), (("seq", 2),), tok_count).astype(
        jnp.float32
    )
    token_grad = back_six[:, :, 2:4].reshape(2, doc_count, tok_count, head_cols)
    token_grad = token_grad + beside_all[:, :, :tok_count] + beside_all[:, :, 3 * tok_count :]
    far_rows = jnp.stack([far_key_rows, far_value_rows]).reshape(
        2, doc_count, levels, block, head_cols
    )
    for level_no in range(levels):
        count = 1 << level_no
        height = block // count
        level_sum = None
        for step in range(count, 2 * count):
            slot = (position ^ step) & (count - 1)
            segment = lax.dynamic_slice_in_dim(far_rows[:, :, level_no], slot * height, height, axis=2)
            returned = lax.ppermute(
                segment.astype(jnp.bfloat16), "seq", [(i, i ^ step) for i in range(seq_count)]
            ).astype(jnp.float32)
            level_sum = returned if level_sum is None else level_sum + returned
        spread = 2 ** (level_no + 1)
        token_grad = token_grad + jnp.repeat(level_sum, spread, axis=2) / float(spread)
    key_grad = token_grad[0].astype(jnp.bfloat16)
    value_grad = token_grad[1].astype(jnp.bfloat16)
    return (attention, query_grad, key_grad, value_grad, weight_grad)


def solution(mesh):
    in_specs = (
        P(("groups", "dp"), "seq", "head"),
        P(("groups", "dp"), "seq", "head"),
        P(("groups", "dp"), "seq", "head"),
        P(("groups", "dp"), "seq", None),
        P("seq", "head"),
        P(("groups", "dp"), "seq", None),
    )
    out_specs = (
        P(("groups", "dp"), "seq", "head"),
        P(("groups", "dp"), "seq", "head"),
        P(("groups", "dp"), "seq", "head"),
        P(("groups", "dp"), "seq", "head"),
        P(("groups", "seq"), "head"),
    )
    return jax.shard_map(shards, mesh=mesh, in_specs=in_specs, out_specs=out_specs, check_vma=False)
```

```python
import math

import jax
import jax.numpy as jnp
from jax import lax
from jax.sharding import PartitionSpec as P

HEAD_DIM = 128
NEAR = 2


def extended(cells, sides, width):
    for axis, dim in sides:
        count = lax.axis_size(axis)
        ends = count - 1
        head = lax.slice_in_dim(cells, 0, width, axis=dim)
        tail = lax.slice_in_dim(cells, cells.shape[dim] - width, cells.shape[dim], axis=dim)
        cells = jnp.concatenate(
            [
                lax.ppermute(tail, axis, [(i, (i + 1) % count) for i in range(ends)]),
                cells,
                lax.ppermute(head, axis, [((i + 1) % count, i) for i in range(ends)]),
            ],
            axis=dim,
        )
    return cells


def swapped(shard, axis, stride):
    return lax.ppermute(shard, axis, [(i, i ^ 1 << stride) for i in range(lax.axis_size(axis))])


def pool_pairs(source):
    shaped = source.reshape(
        source.shape[0], source.shape[1], source.shape[2] // 2, 2, source.shape[3]
    )
    return jnp.sum(shaped, axis=3) * 0.5


def pick_blocks(blocks_doc, chosen_doc):
    return blocks_doc[:, chosen_doc]


def place_blocks(grad_doc, chosen_doc):
    holder = jnp.zeros((grad_doc.shape[0], 6, grad_doc.shape[3], grad_doc.shape[4]), jnp.float32)
    return holder.at[:, chosen_doc].add(grad_doc)


def shards(queries, keys, values, pattern, out_weight, cotangent):
    doc_count, tok_count, head_cols = queries.shape
    block = tok_count // 2
    heads = head_cols // HEAD_DIM
    seq_count = lax.axis_size("seq")
    levels = seq_count.bit_length() - 1
    position = lax.axis_index("seq")
    score_scale = 1.0 / math.sqrt(HEAD_DIM)
    near_width = (NEAR + 1) * block
    key_value = jnp.stack([keys, values])
    padded = extended(key_value, (("seq", 2),), tok_count)
    blocks_six = padded.reshape(2, doc_count, 6, block, head_cols)
    local_ids = jnp.arange(2, dtype=jnp.int32)[None, :, None]
    chosen = jnp.concatenate([local_ids, local_ids + pattern], axis=2) + 2
    near_pair = jax.vmap(pick_blocks, in_axes=(1, 0), out_axes=1)(blocks_six, chosen)
    near_pair = near_pair.reshape(2, doc_count, 2, near_width, head_cols)
    pooled = pool_pairs(key_value.astype(jnp.float32))
    siblings = []
    own_level = pooled
    for level_no in range(levels):
        other = swapped(own_level, "seq", level_no)
        siblings.append(other)
        if level_no + 1 < levels:
            upper = position >> level_no & 1 == 1
            joined = jnp.where(
                upper,
                jnp.concatenate([other, own_level], axis=2),
                jnp.concatenate([own_level, other], axis=2),
            )
            own_level = pool_pairs(joined)
    far_pair = jnp.concatenate(siblings, axis=2).astype(jnp.bfloat16)
    query_heads = queries.reshape(doc_count, 2, block, heads, HEAD_DIM)
    near_k = near_pair[0].reshape(doc_count, 2, near_width, heads, HEAD_DIM)
    near_v = near_pair[1].reshape(doc_count, 2, near_width, heads, HEAD_DIM)
    far_k = far_pair[0].reshape(doc_count, levels * block, heads, HEAD_DIM)
    far_v = far_pair[1].reshape(doc_count, levels * block, heads, HEAD_DIM)
    score_near = (
        jnp.einsum("dbqhe,dbkhe->dbhqk", query_heads, near_k, preferred_element_type=jnp.float32)
        * score_scale
    )
    score_far = (
        jnp.einsum("dbqhe,dkhe->dbhqk", query_heads, far_k, preferred_element_type=jnp.float32)
        * score_scale
    )
    top = jnp.maximum(
        jnp.max(score_near, axis=-1, keepdims=True), jnp.max(score_far, axis=-1, keepdims=True)
    )
    exp_near = jnp.exp(score_near - top)
    exp_far = jnp.exp(score_far - top)
    total = jnp.sum(exp_near, axis=-1, keepdims=True) + jnp.sum(exp_far, axis=-1, keepdims=True)
    weight_near = exp_near / total
    weight_far = exp_far / total
    rounded_near = weight_near.astype(jnp.bfloat16)
    rounded_far = weight_far.astype(jnp.bfloat16)
    output = jnp.einsum(
        "dbhqk,dbkhe->dbqhe", rounded_near, near_v, preferred_element_type=jnp.float32
    )
    output = output + jnp.einsum(
        "dbhqk,dkhe->dbqhe", rounded_far, far_v, preferred_element_type=jnp.float32
    )
    attention = output.reshape(doc_count, tok_count, head_cols).astype(jnp.bfloat16)
    feat_count = cotangent.shape[2] // seq_count
    cot_rows = cotangent.reshape(doc_count * tok_count, cotangent.shape[2])
    out_rows = attention.reshape(doc_count * tok_count, head_cols)
    own_cols = lax.dynamic_slice_in_dim(cot_rows, position * feat_count, feat_count, axis=1)
    grad_sum = jnp.dot(own_cols, out_weight, preferred_element_type=jnp.float32)
    feat_list = [own_cols]
    for step in range(1, seq_count):
        pairs = [(i, i ^ step) for i in range(seq_count)]
        sent = lax.dynamic_slice_in_dim(
            cot_rows, (position ^ step) * feat_count, feat_count, axis=1
        )
        half = sent.shape[0] // 2
        core = lax.axis_index("head")
        got_half = lax.ppermute(
            lax.dynamic_slice_in_dim(sent, core * half, half, axis=0), "seq", pairs
        )
        other_half = swapped(got_half, "head", 0)
        got = jnp.where(
            core == 0,
            jnp.concatenate([got_half, other_half], axis=0),
            jnp.concatenate([other_half, got_half], axis=0),
        )
        part = jnp.dot(got, out_weight, preferred_element_type=jnp.float32)
        back = lax.ppermute(part.astype(jnp.bfloat16), "seq", pairs)
        grad_sum = grad_sum + back.astype(jnp.float32)
        feat_list.append(got)
    attn_grad = grad_sum.astype(jnp.bfloat16)
    feat_order = jnp.arange(seq_count, dtype=jnp.int32) ^ position
    feat_docs = jnp.take(jnp.stack(feat_list, axis=0), feat_order, axis=0).reshape(
        seq_count * cot_rows.shape[0], feat_count
    )
    dp_count = lax.axis_size("dp")
    feat_docs = lax.all_gather(feat_docs, "dp", axis=0, tiled=False)
    feat_docs = jnp.swapaxes(
        feat_docs.reshape(dp_count, seq_count, cot_rows.shape[0], feat_count), 0, 1
    ).reshape(dp_count * seq_count * cot_rows.shape[0], feat_count)
    whole_output = lax.all_gather(out_rows, ("seq", "dp"), axis=0, tiled=True)
    weight_grad = jnp.einsum(
        "tc,tw->cw", feat_docs, whole_output, preferred_element_type=jnp.float32
    )
    grad_heads = attn_grad.reshape(doc_count, 2, block, heads, HEAD_DIM)
    prob_near = jnp.einsum(
        "dbqhe,dbkhe->dbhqk", grad_heads, near_v, preferred_element_type=jnp.float32
    )
    prob_far = jnp.einsum(
        "dbqhe,dkhe->dbhqk", grad_heads, far_v, preferred_element_type=jnp.float32
    )
    row_dot = jnp.sum(weight_near * prob_near, axis=-1, keepdims=True) + jnp.sum(
        weight_far * prob_far, axis=-1, keepdims=True
    )
    grad_near = (weight_near * (prob_near - row_dot)).astype(jnp.bfloat16)
    grad_far = (weight_far * (prob_far - row_dot)).astype(jnp.bfloat16)
    query_sum = jnp.einsum(
        "dbhqk,dbkhe->dbqhe", grad_near, near_k, preferred_element_type=jnp.float32
    )
    query_sum = query_sum + jnp.einsum(
        "dbhqk,dkhe->dbqhe", grad_far, far_k, preferred_element_type=jnp.float32
    )
    query_grad = (
        (query_sum * score_scale).reshape(doc_count, tok_count, head_cols).astype(jnp.bfloat16)
    )
    near_key_rows = (
        jnp.einsum("dbhqk,dbqhe->dbkhe", grad_near, query_heads, preferred_element_type=jnp.float32)
        * score_scale
    )
    near_value_rows = jnp.einsum(
        "dbhqk,dbqhe->dbkhe", rounded_near, grad_heads, preferred_element_type=jnp.float32
    )
    far_key_rows = (
        jnp.einsum("dbhqk,dbqhe->dkhe", grad_far, query_heads, preferred_element_type=jnp.float32)
        * score_scale
    )
    far_value_rows = jnp.einsum(
        "dbhqk,dbqhe->dkhe", rounded_far, grad_heads, preferred_element_type=jnp.float32
    )
    near_rows = jnp.stack([near_key_rows, near_value_rows]).reshape(
        2, doc_count, 2, NEAR + 1, block, head_cols
    )
    back_six = jax.vmap(place_blocks, in_axes=(1, 0), out_axes=1)(near_rows, chosen)
    rims = jnp.concatenate([back_six[:, :, 0:2], back_six[:, :, 4:6]], axis=2).reshape(
        2, doc_count, 2 * tok_count, head_cols
    )
    beside_all = extended(rims.astype(jnp.bfloat16), (("seq", 2),), tok_count).astype(
        jnp.float32
    )
    token_grad = back_six[:, :, 2:4].reshape(2, doc_count, tok_count, head_cols)
    token_grad = token_grad + beside_all[:, :, :tok_count] + beside_all[:, :, 3 * tok_count :]
    far_rows = jnp.stack([far_key_rows, far_value_rows]).reshape(
        2, doc_count, levels, block, head_cols
    )
    for level_no in range(levels):
        count = 1 << level_no
        height = block // count
        level_sum = None
        for step in range(count, 2 * count):
            slot = (position ^ step) & (count - 1)
            segment = lax.dynamic_slice_in_dim(far_rows[:, :, level_no], slot * height, height, axis=2)
            returned = lax.ppermute(
                segment.astype(jnp.bfloat16), "seq", [(i, i ^ step) for i in range(seq_count)]
            ).astype(jnp.float32)
            level_sum = returned if level_sum is None else level_sum + returned
        spread = 2 ** (level_no + 1)
        token_grad = token_grad + jnp.repeat(level_sum, spread, axis=2) / float(spread)
    key_grad = token_grad[0].astype(jnp.bfloat16)
    value_grad = token_grad[1].astype(jnp.bfloat16)
    return (attention, query_grad, key_grad, value_grad, weight_grad)


def solution(mesh):
    in_specs = (
        P(("groups", "dp"), "seq", "head"),
        P(("groups", "dp"), "seq", "head"),
        P(("groups", "dp"), "seq", "head"),
        P(("groups", "dp"), "seq", None),
        P("seq", "head"),
        P(("groups", "dp"), "seq", None),
    )
    out_specs = (
        P(("groups", "dp"), "seq", "head"),
        P(("groups", "dp"), "seq", "head"),
        P(("groups", "dp"), "seq", "head"),
        P(("groups", "dp"), "seq", "head"),
        P(("groups", "seq"), "head"),
    )
    return jax.shard_map(shards, mesh=mesh, in_specs=in_specs, out_specs=out_specs, check_vma=False)
```

```python
import math

import jax
import jax.numpy as jnp
from jax import lax
from jax.sharding import PartitionSpec as P

HEAD_DIM = 128
NEAR = 2


def extended(cells, sides, width):
    for axis, dim in sides:
        count = lax.axis_size(axis)
        ends = count - 1
        head = lax.slice_in_dim(cells, 0, width, axis=dim)
        tail = lax.slice_in_dim(cells, cells.shape[dim] - width, cells.shape[dim], axis=dim)
        cells = jnp.concatenate(
            [
                lax.ppermute(tail, axis, [(i, (i + 1) % count) for i in range(ends)]),
                cells,
                lax.ppermute(head, axis, [((i + 1) % count, i) for i in range(ends)]),
            ],
            axis=dim,
        )
    return cells


def swapped(shard, axis, stride):
    return lax.ppermute(shard, axis, [(i, i ^ 1 << stride) for i in range(lax.axis_size(axis))])


def pool_pairs(source):
    shaped = source.reshape(
        source.shape[0], source.shape[1], source.shape[2] // 2, 2, source.shape[3]
    )
    return jnp.sum(shaped, axis=3) * 0.5


def pick_blocks(blocks_doc, chosen_doc):
    return blocks_doc[:, chosen_doc]


def place_blocks(grad_doc, chosen_doc):
    holder = jnp.zeros((grad_doc.shape[0], 6, grad_doc.shape[3], grad_doc.shape[4]), jnp.float32)
    return holder.at[:, chosen_doc].add(grad_doc)


def shards(queries, keys, values, pattern, out_weight, cotangent):
    doc_count, tok_count, head_cols = queries.shape
    block = tok_count // 2
    heads = head_cols // HEAD_DIM
    seq_count = lax.axis_size("seq")
    levels = seq_count.bit_length() - 1
    position = lax.axis_index("seq")
    score_scale = 1.0 / math.sqrt(HEAD_DIM)
    near_width = (NEAR + 1) * block
    key_value = jnp.stack([keys, values])
    padded = extended(key_value, (("seq", 2),), tok_count)
    blocks_six = padded.reshape(2, doc_count, 6, block, head_cols)
    local_ids = jnp.arange(2, dtype=jnp.int32)[None, :, None]
    chosen = jnp.concatenate([local_ids, local_ids + pattern], axis=2) + 2
    candidates = [[b + p + 2 for p in (-2, -1, 1, 2)] for b in range(2)]
    picked = []
    for b in range(2):
        picked.append(blocks_six[:, :, b + 2])
        for n in range(1, NEAR + 1):
            index = chosen[:, b, n][None, :, None, None]
            acc = jnp.zeros_like(blocks_six[:, :, 0])
            for j in candidates[b]:
                acc = jnp.where(index == j, blocks_six[:, :, j], acc)
            picked.append(acc)
    near_pair = jnp.stack(picked, axis=2).reshape(2, doc_count, 2, near_width, head_cols)
    pooled = pool_pairs(key_value.astype(jnp.float32))
    siblings = []
    own_level = pooled
    for level_no in range(levels):
        other = swapped(own_level, "seq", level_no)
        siblings.append(other)
        if level_no + 1 < levels:
            upper = position >> level_no & 1 == 1
            joined = jnp.where(
                upper,
                jnp.concatenate([other, own_level], axis=2),
                jnp.concatenate([own_level, other], axis=2),
            )
            own_level = pool_pairs(joined)
    far_pair = jnp.concatenate(siblings, axis=2).astype(jnp.bfloat16)
    query_heads = queries.reshape(doc_count, 2, block, heads, HEAD_DIM)
    near_k = near_pair[0].reshape(doc_count, 2, near_width, heads, HEAD_DIM)
    near_v = near_pair[1].reshape(doc_count, 2, near_width, heads, HEAD_DIM)
    far_k = far_pair[0].reshape(doc_count, levels * block, heads, HEAD_DIM)
    far_v = far_pair[1].reshape(doc_count, levels * block, heads, HEAD_DIM)
    score_near = (
        jnp.einsum("dbqhe,dbkhe->dbhqk", query_heads, near_k, preferred_element_type=jnp.float32)
        * score_scale
    )
    score_far = (
        jnp.einsum("dbqhe,dkhe->dbhqk", query_heads, far_k, preferred_element_type=jnp.float32)
        * score_scale
    )
    top = jnp.maximum(
        jnp.max(score_near, axis=-1, keepdims=True), jnp.max(score_far, axis=-1, keepdims=True)
    )
    exp_near = jnp.exp(score_near - top)
    exp_far = jnp.exp(score_far - top)
    total = jnp.sum(exp_near, axis=-1, keepdims=True) + jnp.sum(exp_far, axis=-1, keepdims=True)
    weight_near = exp_near / total
    weight_far = exp_far / total
    rounded_near = weight_near.astype(jnp.bfloat16)
    rounded_far = weight_far.astype(jnp.bfloat16)
    output = jnp.einsum(
        "dbhqk,dbkhe->dbqhe", rounded_near, near_v, preferred_element_type=jnp.float32
    )
    output = output + jnp.einsum(
        "dbhqk,dkhe->dbqhe", rounded_far, far_v, preferred_element_type=jnp.float32
    )
    attention = output.reshape(doc_count, tok_count, head_cols).astype(jnp.bfloat16)
    feat_count = cotangent.shape[2] // seq_count
    cot_rows = cotangent.reshape(doc_count * tok_count, cotangent.shape[2])
    out_rows = attention.reshape(doc_count * tok_count, head_cols)
    own_cols = lax.dynamic_slice_in_dim(cot_rows, position * feat_count, feat_count, axis=1)
    grad_sum = jnp.dot(own_cols, out_weight, preferred_element_type=jnp.float32)
    feat_list = [own_cols]
    for step in range(1, seq_count):
        pairs = [(i, i ^ step) for i in range(seq_count)]
        sent = lax.dynamic_slice_in_dim(
            cot_rows, (position ^ step) * feat_count, feat_count, axis=1
        )
        half = sent.shape[0] // 2
        core = lax.axis_index("head")
        got_half = lax.ppermute(
            lax.dynamic_slice_in_dim(sent, core * half, half, axis=0), "seq", pairs
        )
        other_half = swapped(got_half, "head", 0)
        got = jnp.where(
            core == 0,
            jnp.concatenate([got_half, other_half], axis=0),
            jnp.concatenate([other_half, got_half], axis=0),
        )
        part = jnp.dot(got, out_weight, preferred_element_type=jnp.float32)
        back = lax.ppermute(part.astype(jnp.bfloat16), "seq", pairs)
        grad_sum = grad_sum + back.astype(jnp.float32)
        feat_list.append(got)
    attn_grad = grad_sum.astype(jnp.bfloat16)
    feat_order = jnp.arange(seq_count, dtype=jnp.int32) ^ position
    feat_docs = jnp.take(jnp.stack(feat_list, axis=0), feat_order, axis=0).reshape(
        seq_count * cot_rows.shape[0], feat_count
    )
    feat_docs = lax.all_gather(feat_docs, "dp", axis=0, tiled=True)
    whole_output = lax.all_gather(out_rows, ("dp", "seq"), axis=0, tiled=True)
    weight_grad = jnp.einsum(
        "tc,tw->cw", feat_docs, whole_output, preferred_element_type=jnp.float32
    )
    grad_heads = attn_grad.reshape(doc_count, 2, block, heads, HEAD_DIM)
    prob_near = jnp.einsum(
        "dbqhe,dbkhe->dbhqk", grad_heads, near_v, preferred_element_type=jnp.float32
    )
    prob_far = jnp.einsum(
        "dbqhe,dkhe->dbhqk", grad_heads, far_v, preferred_element_type=jnp.float32
    )
    row_dot = jnp.sum(weight_near * prob_near, axis=-1, keepdims=True) + jnp.sum(
        weight_far * prob_far, axis=-1, keepdims=True
    )
    grad_near = (weight_near * (prob_near - row_dot)).astype(jnp.bfloat16)
    grad_far = (weight_far * (prob_far - row_dot)).astype(jnp.bfloat16)
    query_sum = jnp.einsum(
        "dbhqk,dbkhe->dbqhe", grad_near, near_k, preferred_element_type=jnp.float32
    )
    query_sum = query_sum + jnp.einsum(
        "dbhqk,dkhe->dbqhe", grad_far, far_k, preferred_element_type=jnp.float32
    )
    query_grad = (
        (query_sum * score_scale).reshape(doc_count, tok_count, head_cols).astype(jnp.bfloat16)
    )
    near_key_rows = (
        jnp.einsum("dbhqk,dbqhe->dbkhe", grad_near, query_heads, preferred_element_type=jnp.float32)
        * score_scale
    )
    near_value_rows = jnp.einsum(
        "dbhqk,dbqhe->dbkhe", rounded_near, grad_heads, preferred_element_type=jnp.float32
    )
    far_key_rows = (
        jnp.einsum("dbhqk,dbqhe->dkhe", grad_far, query_heads, preferred_element_type=jnp.float32)
        * score_scale
    )
    far_value_rows = jnp.einsum(
        "dbhqk,dbqhe->dkhe", rounded_far, grad_heads, preferred_element_type=jnp.float32
    )
    near_rows = jnp.stack([near_key_rows, near_value_rows]).reshape(
        2, doc_count, 2, NEAR + 1, block, head_cols
    )
    slots = []
    for j in range(6):
        total = jnp.zeros_like(near_rows[:, :, 0, 0])
        for b in range(2):
            if j == b + 2:
                total = total + near_rows[:, :, b, 0]
            if j in candidates[b]:
                for n in range(1, NEAR + 1):
                    index = chosen[:, b, n][None, :, None, None]
                    total = total + jnp.where(index == j, near_rows[:, :, b, n], 0.0)
        slots.append(total)
    back_six = jnp.stack(slots, axis=2)
    rims = jnp.concatenate([back_six[:, :, 0:2], back_six[:, :, 4:6]], axis=2).reshape(
        2, doc_count, 2 * tok_count, head_cols
    )
    beside_all = extended(rims.astype(jnp.bfloat16), (("seq", 2),), tok_count).astype(
        jnp.float32
    )
    token_grad = back_six[:, :, 2:4].reshape(2, doc_count, tok_count, head_cols)
    token_grad = token_grad + beside_all[:, :, :tok_count] + beside_all[:, :, 3 * tok_count :]
    far_rows = jnp.stack([far_key_rows, far_value_rows]).reshape(
        2, doc_count, levels, block, head_cols
    )
    for level_no in range(levels):
        count = 1 << level_no
        height = block // count
        level_sum = None
        for step in range(count, 2 * count):
            slot = (position ^ step) & (count - 1)
            segment = lax.dynamic_slice_in_dim(far_rows[:, :, level_no], slot * height, height, axis=2)
            returned = lax.ppermute(
                segment.astype(jnp.bfloat16), "seq", [(i, i ^ step) for i in range(seq_count)]
            ).astype(jnp.float32)
            level_sum = returned if level_sum is None else level_sum + returned
        spread = 2 ** (level_no + 1)
        token_grad = token_grad + jnp.repeat(level_sum, spread, axis=2) / float(spread)
    key_grad = token_grad[0].astype(jnp.bfloat16)
    value_grad = token_grad[1].astype(jnp.bfloat16)
    return (attention, query_grad, key_grad, value_grad, weight_grad)


def solution(mesh):
    in_specs = (
        P(("groups", "dp"), "seq", "head"),
        P(("groups", "dp"), "seq", "head"),
        P(("groups", "dp"), "seq", "head"),
        P(("groups", "dp"), "seq", None),
        P("seq", "head"),
        P(("groups", "dp"), "seq", None),
    )
    out_specs = (
        P(("groups", "dp"), "seq", "head"),
        P(("groups", "dp"), "seq", "head"),
        P(("groups", "dp"), "seq", "head"),
        P(("groups", "dp"), "seq", "head"),
        P(("groups", "seq"), "head"),
    )
    return jax.shard_map(shards, mesh=mesh, in_specs=in_specs, out_specs=out_specs, check_vma=False)
```

```python
import math

import jax
import jax.numpy as jnp
from jax import lax
from jax.sharding import PartitionSpec as P

HEAD_DIM = 128
NEAR = 2


def extended(cells, sides, width):
    for axis, dim in sides:
        count = lax.axis_size(axis)
        ends = count - 1
        head = lax.slice_in_dim(cells, 0, width, axis=dim)
        tail = lax.slice_in_dim(cells, cells.shape[dim] - width, cells.shape[dim], axis=dim)
        cells = jnp.concatenate(
            [
                lax.ppermute(tail, axis, [(i, (i + 1) % count) for i in range(ends)]),
                cells,
                lax.ppermute(head, axis, [((i + 1) % count, i) for i in range(ends)]),
            ],
            axis=dim,
        )
    return cells


def swapped(shard, axis, stride):
    return lax.ppermute(shard, axis, [(i, i ^ 1 << stride) for i in range(lax.axis_size(axis))])


def pool_pairs(source):
    shaped = source.reshape(
        source.shape[0], source.shape[1], source.shape[2] // 2, 2, source.shape[3]
    )
    return jnp.sum(shaped, axis=3) * 0.5


def pick_blocks(blocks_doc, chosen_doc):
    return blocks_doc[:, chosen_doc]


def place_blocks(grad_doc, chosen_doc):
    holder = jnp.zeros((grad_doc.shape[0], 6, grad_doc.shape[3], grad_doc.shape[4]), jnp.float32)
    return holder.at[:, chosen_doc].add(grad_doc)


def shards(queries, keys, values, pattern, out_weight, cotangent):
    doc_count, tok_count, head_cols = queries.shape
    block = tok_count // 2
    heads = head_cols // HEAD_DIM
    seq_count = lax.axis_size("seq")
    levels = seq_count.bit_length() - 1
    position = lax.axis_index("seq")
    score_scale = 1.0 / math.sqrt(HEAD_DIM)
    near_width = (NEAR + 1) * block
    key_value = jnp.stack([keys, values])
    padded = extended(key_value, (("seq", 2),), tok_count)
    blocks_six = padded.reshape(2, doc_count, 6, block, head_cols)
    local_ids = jnp.arange(2, dtype=jnp.int32)[None, :, None]
    chosen = jnp.concatenate([local_ids, local_ids + pattern], axis=2) + 2
    near_pair = jax.vmap(pick_blocks, in_axes=(1, 0), out_axes=1)(blocks_six, chosen)
    near_pair = near_pair.reshape(2, doc_count, 2, near_width, head_cols)
    pooled = pool_pairs(key_value.astype(jnp.float32))
    siblings = []
    own_level = pooled
    for level_no in range(levels):
        other = swapped(own_level, "seq", level_no)
        siblings.append(other)
        if level_no + 1 < levels:
            upper = position >> level_no & 1 == 1
            joined = jnp.where(
                upper,
                jnp.concatenate([other, own_level], axis=2),
                jnp.concatenate([own_level, other], axis=2),
            )
            own_level = pool_pairs(joined)
    far_pair = jnp.concatenate(siblings, axis=2).astype(jnp.bfloat16)
    query_heads = queries.reshape(doc_count, 2, block, heads, HEAD_DIM)
    near_k = near_pair[0].reshape(doc_count, 2, near_width, heads, HEAD_DIM)
    near_v = near_pair[1].reshape(doc_count, 2, near_width, heads, HEAD_DIM)
    far_k = far_pair[0].reshape(doc_count, levels * block, heads, HEAD_DIM)
    far_v = far_pair[1].reshape(doc_count, levels * block, heads, HEAD_DIM)
    score_near = (
        jnp.einsum("dbqhe,dbkhe->dbhqk", query_heads, near_k, preferred_element_type=jnp.float32)
        * score_scale
    )
    score_far = (
        jnp.einsum("dbqhe,dkhe->dbhqk", query_heads, far_k, preferred_element_type=jnp.float32)
        * score_scale
    )
    top = jnp.maximum(
        jnp.max(score_near, axis=-1, keepdims=True), jnp.max(score_far, axis=-1, keepdims=True)
    )
    exp_near = jnp.exp(score_near - top)
    exp_far = jnp.exp(score_far - top)
    total = jnp.sum(exp_near, axis=-1, keepdims=True) + jnp.sum(exp_far, axis=-1, keepdims=True)
    weight_near = exp_near / total
    weight_far = exp_far / total
    rounded_near = weight_near.astype(jnp.bfloat16)
    rounded_far = weight_far.astype(jnp.bfloat16)
    output = jnp.einsum(
        "dbhqk,dbkhe->dbqhe", rounded_near, near_v, preferred_element_type=jnp.float32
    )
    output = output + jnp.einsum(
        "dbhqk,dkhe->dbqhe", rounded_far, far_v, preferred_element_type=jnp.float32
    )
    attention = output.reshape(doc_count, tok_count, head_cols).astype(jnp.bfloat16)
    feat_count = cotangent.shape[2] // seq_count
    cot_rows = cotangent.reshape(doc_count * tok_count, cotangent.shape[2])
    out_rows = attention.reshape(doc_count * tok_count, head_cols)
    own_cols = lax.dynamic_slice_in_dim(cot_rows, position * feat_count, feat_count, axis=1)
    grad_sum = jnp.dot(own_cols, out_weight, preferred_element_type=jnp.float32)
    feat_list = [own_cols]
    for step in range(1, seq_count):
        pairs = [(i, i ^ step) for i in range(seq_count)]
        sent = lax.dynamic_slice_in_dim(
            cot_rows, (position ^ step) * feat_count, feat_count, axis=1
        )
        half = sent.shape[0] // 2
        core = lax.axis_index("head")
        got_half = lax.ppermute(
            lax.dynamic_slice_in_dim(sent, core * half, half, axis=0), "seq", pairs
        )
        other_half = swapped(got_half, "head", 0)
        got = jnp.where(
            core == 0,
            jnp.concatenate([got_half, other_half], axis=0),
            jnp.concatenate([other_half, got_half], axis=0),
        )
        part = jnp.dot(got, out_weight, preferred_element_type=jnp.float32)
        back = lax.ppermute(part.astype(jnp.bfloat16), "seq", pairs)
        grad_sum = grad_sum + back.astype(jnp.float32)
        feat_list.append(got)
    attn_grad = grad_sum.astype(jnp.bfloat16)
    feat_order = jnp.arange(seq_count, dtype=jnp.int32) ^ position
    feat_docs = jnp.take(jnp.stack(feat_list, axis=0), feat_order, axis=0).reshape(
        seq_count * cot_rows.shape[0], feat_count
    )
    feat_docs = lax.all_gather(feat_docs, "dp", axis=0, tiled=True)
    whole_output = lax.all_gather(out_rows, ("dp", "seq"), axis=0, tiled=True)
    weight_grad = jnp.einsum(
        "tc,tw->cw", feat_docs, whole_output, preferred_element_type=jnp.float32
    )
    grad_heads = attn_grad.reshape(doc_count, 2, block, heads, HEAD_DIM)
    prob_near = jnp.einsum(
        "dbqhe,dbkhe->dbhqk", grad_heads, near_v, preferred_element_type=jnp.float32
    )
    prob_far = jnp.einsum(
        "dbqhe,dkhe->dbhqk", grad_heads, far_v, preferred_element_type=jnp.float32
    )
    row_dot = jnp.sum(weight_near * prob_near, axis=-1, keepdims=True) + jnp.sum(
        weight_far * prob_far, axis=-1, keepdims=True
    )
    grad_near = (weight_near * (prob_near - row_dot)).astype(jnp.bfloat16)
    grad_far = (weight_far * (prob_far - row_dot)).astype(jnp.bfloat16)
    query_sum = jnp.einsum(
        "dbhqk,dbkhe->dbqhe", grad_near, near_k, preferred_element_type=jnp.float32
    )
    query_sum = query_sum + jnp.einsum(
        "dbhqk,dkhe->dbqhe", grad_far, far_k, preferred_element_type=jnp.float32
    )
    query_grad = (
        (query_sum * score_scale).reshape(doc_count, tok_count, head_cols).astype(jnp.bfloat16)
    )
    near_key_rows = (
        jnp.einsum("dbhqk,dbqhe->dbkhe", grad_near, query_heads, preferred_element_type=jnp.float32)
        * score_scale
    )
    near_value_rows = jnp.einsum(
        "dbhqk,dbqhe->dbkhe", rounded_near, grad_heads, preferred_element_type=jnp.float32
    )
    far_key_rows = (
        jnp.einsum("dbhqk,dbqhe->dkhe", grad_far, query_heads, preferred_element_type=jnp.float32)
        * score_scale
    )
    far_value_rows = jnp.einsum(
        "dbhqk,dbqhe->dkhe", rounded_far, grad_heads, preferred_element_type=jnp.float32
    )
    near_rows = jnp.stack([near_key_rows, near_value_rows]).reshape(
        2, doc_count, 2, NEAR + 1, block, head_cols
    )
    candidates = [[b + p + 2 for p in (-2, -1, 1, 2)] for b in range(2)]
    slots = []
    for j in range(6):
        total = jnp.zeros_like(near_rows[:, :, 0, 0])
        for b in range(2):
            if j == b + 2:
                total = total + near_rows[:, :, b, 0]
            if j in candidates[b]:
                for n in range(1, NEAR + 1):
                    index = chosen[:, b, n][None, :, None, None]
                    total = total + jnp.where(index == j, near_rows[:, :, b, n], 0.0)
        slots.append(total)
    back_six = jnp.stack(slots, axis=2)
    rims = jnp.concatenate([back_six[:, :, 0:2], back_six[:, :, 4:6]], axis=2).reshape(
        2, doc_count, 2 * tok_count, head_cols
    )
    beside_all = extended(rims.astype(jnp.bfloat16), (("seq", 2),), tok_count).astype(
        jnp.float32
    )
    token_grad = back_six[:, :, 2:4].reshape(2, doc_count, tok_count, head_cols)
    token_grad = token_grad + beside_all[:, :, :tok_count] + beside_all[:, :, 3 * tok_count :]
    far_rows = jnp.stack([far_key_rows, far_value_rows]).reshape(
        2, doc_count, levels, block, head_cols
    )
    for level_no in range(levels):
        count = 1 << level_no
        height = block // count
        level_sum = None
        for step in range(count, 2 * count):
            slot = (position ^ step) & (count - 1)
            segment = lax.dynamic_slice_in_dim(far_rows[:, :, level_no], slot * height, height, axis=2)
            returned = lax.ppermute(
                segment.astype(jnp.bfloat16), "seq", [(i, i ^ step) for i in range(seq_count)]
            ).astype(jnp.float32)
            level_sum = returned if level_sum is None else level_sum + returned
        spread = 2 ** (level_no + 1)
        token_grad = token_grad + jnp.repeat(level_sum, spread, axis=2) / float(spread)
    key_grad = token_grad[0].astype(jnp.bfloat16)
    value_grad = token_grad[1].astype(jnp.bfloat16)
    return (attention, query_grad, key_grad, value_grad, weight_grad)


def solution(mesh):
    in_specs = (
        P(("groups", "dp"), "seq", "head"),
        P(("groups", "dp"), "seq", "head"),
        P(("groups", "dp"), "seq", "head"),
        P(("groups", "dp"), "seq", None),
        P("seq", "head"),
        P(("groups", "dp"), "seq", None),
    )
    out_specs = (
        P(("groups", "dp"), "seq", "head"),
        P(("groups", "dp"), "seq", "head"),
        P(("groups", "dp"), "seq", "head"),
        P(("groups", "dp"), "seq", "head"),
        P(("groups", "seq"), "head"),
    )
    return jax.shard_map(shards, mesh=mesh, in_specs=in_specs, out_specs=out_specs, check_vma=False)
```

```python
import math

import jax
import jax.numpy as jnp
from jax import lax
from jax.sharding import PartitionSpec as P

HEAD_DIM = 128
NEAR = 2


def extended(cells, sides, width):
    for axis, dim in sides:
        count = lax.axis_size(axis)
        ends = count - 1
        head = lax.slice_in_dim(cells, 0, width, axis=dim)
        tail = lax.slice_in_dim(cells, cells.shape[dim] - width, cells.shape[dim], axis=dim)
        cells = jnp.concatenate(
            [
                lax.ppermute(tail, axis, [(i, (i + 1) % count) for i in range(ends)]),
                cells,
                lax.ppermute(head, axis, [((i + 1) % count, i) for i in range(ends)]),
            ],
            axis=dim,
        )
    return cells


def swapped(shard, axis, stride):
    return lax.ppermute(shard, axis, [(i, i ^ 1 << stride) for i in range(lax.axis_size(axis))])


def pool_pairs(source):
    shaped = source.reshape(
        source.shape[0], source.shape[1], source.shape[2] // 2, 2, source.shape[3]
    )
    return jnp.sum(shaped, axis=3) * 0.5


def pick_blocks(blocks_doc, chosen_doc):
    return blocks_doc[:, chosen_doc]


def place_blocks(grad_doc, chosen_doc):
    holder = jnp.zeros((grad_doc.shape[0], 6, grad_doc.shape[3], grad_doc.shape[4]), jnp.float32)
    return holder.at[:, chosen_doc].add(grad_doc)


def shards(queries, keys, values, pattern, out_weight, cotangent):
    doc_count, tok_count, head_cols = queries.shape
    block = tok_count // 2
    heads = head_cols // HEAD_DIM
    seq_count = lax.axis_size("seq")
    levels = seq_count.bit_length() - 1
    position = lax.axis_index("seq")
    score_scale = 1.0 / math.sqrt(HEAD_DIM)
    near_width = (NEAR + 1) * block
    key_value = jnp.stack([keys, values])
    padded = extended(key_value, (("seq", 2),), tok_count)
    blocks_six = padded.reshape(2, doc_count, 6, block, head_cols)
    local_ids = jnp.arange(2, dtype=jnp.int32)[None, :, None]
    chosen = jnp.concatenate([local_ids, local_ids + pattern], axis=2) + 2
    near_pair = jax.vmap(pick_blocks, in_axes=(1, 0), out_axes=1)(blocks_six, chosen)
    near_pair = near_pair.reshape(2, doc_count, 2, near_width, head_cols)
    pooled = pool_pairs(key_value.astype(jnp.float32))
    siblings = []
    own_level = pooled
    for level_no in range(levels):
        other = swapped(own_level, "seq", level_no)
        siblings.append(other)
        if level_no + 1 < levels:
            upper = position >> level_no & 1 == 1
            joined = jnp.where(
                upper,
                jnp.concatenate([other, own_level], axis=2),
                jnp.concatenate([own_level, other], axis=2),
            )
            own_level = pool_pairs(joined)
    far_pair = jnp.concatenate(siblings, axis=2).astype(jnp.bfloat16)
    query_heads = queries.reshape(doc_count, 2, block, heads, HEAD_DIM)
    near_k = near_pair[0].reshape(doc_count, 2, near_width, heads, HEAD_DIM)
    near_v = near_pair[1].reshape(doc_count, 2, near_width, heads, HEAD_DIM)
    far_k = far_pair[0].reshape(doc_count, levels * block, heads, HEAD_DIM)
    far_v = far_pair[1].reshape(doc_count, levels * block, heads, HEAD_DIM)
    score_near = (
        jnp.einsum("dbqhe,dbkhe->dbhqk", query_heads, near_k, preferred_element_type=jnp.float32)
        * score_scale
    )
    score_far = (
        jnp.einsum("dbqhe,dkhe->dbhqk", query_heads, far_k, preferred_element_type=jnp.float32)
        * score_scale
    )
    top = jnp.maximum(
        jnp.max(score_near, axis=-1, keepdims=True), jnp.max(score_far, axis=-1, keepdims=True)
    )
    exp_near = jnp.exp(score_near - top)
    exp_far = jnp.exp(score_far - top)
    total = jnp.sum(exp_near, axis=-1, keepdims=True) + jnp.sum(exp_far, axis=-1, keepdims=True)
    weight_near = exp_near / total
    weight_far = exp_far / total
    rounded_near = weight_near.astype(jnp.bfloat16)
    rounded_far = weight_far.astype(jnp.bfloat16)
    output = jnp.einsum(
        "dbhqk,dbkhe->dbqhe", rounded_near, near_v, preferred_element_type=jnp.float32
    )
    output = output + jnp.einsum(
        "dbhqk,dkhe->dbqhe", rounded_far, far_v, preferred_element_type=jnp.float32
    )
    attention = output.reshape(doc_count, tok_count, head_cols).astype(jnp.bfloat16)
    feat_count = cotangent.shape[2] // seq_count
    cot_rows = cotangent.reshape(doc_count * tok_count, cotangent.shape[2])
    out_rows = attention.reshape(doc_count * tok_count, head_cols)
    own_cols = lax.dynamic_slice_in_dim(cot_rows, position * feat_count, feat_count, axis=1)
    grad_sum = jnp.dot(own_cols, out_weight, preferred_element_type=jnp.float32)
    feat_list = [own_cols]
    for step in range(1, seq_count):
        pairs = [(i, i ^ step) for i in range(seq_count)]
        sent = lax.dynamic_slice_in_dim(
            cot_rows, (position ^ step) * feat_count, feat_count, axis=1
        )
        half = sent.shape[0] // 2
        core = lax.axis_index("head")
        got_half = lax.ppermute(
            lax.dynamic_slice_in_dim(sent, core * half, half, axis=0), "seq", pairs
        )
        other_half = swapped(got_half, "head", 0)
        got = jnp.where(
            core == 0,
            jnp.concatenate([got_half, other_half], axis=0),
            jnp.concatenate([other_half, got_half], axis=0),
        )
        part = jnp.dot(got, out_weight, preferred_element_type=jnp.float32)
        back = lax.ppermute(part.astype(jnp.bfloat16), "seq", pairs)
        grad_sum = grad_sum + back.astype(jnp.float32)
        feat_list.append(got)
    attn_grad = grad_sum.astype(jnp.bfloat16)
    feat_order = jnp.arange(seq_count, dtype=jnp.int32) ^ position
    feat_docs = jnp.take(jnp.stack(feat_list, axis=0), feat_order, axis=0).reshape(
        seq_count * cot_rows.shape[0], feat_count
    )
    feat_docs = lax.all_gather(feat_docs, "dp", axis=0, tiled=True)
    chunk_rows = out_rows.shape[0]
    feat_chunks = feat_docs.reshape(-1, chunk_rows, feat_count)
    split = chunk_rows // 2
    weight_grad = None
    for lo, hi in ((0, split), (split, chunk_rows)):
        gathered = lax.all_gather(out_rows[lo:hi], ("dp", "seq"), axis=0, tiled=True)
        part = jnp.einsum(
            "tc,tw->cw",
            feat_chunks[:, lo:hi].reshape(-1, feat_count),
            gathered,
            preferred_element_type=jnp.float32,
        )
        weight_grad = part if weight_grad is None else weight_grad + part
    grad_heads = attn_grad.reshape(doc_count, 2, block, heads, HEAD_DIM)
    prob_near = jnp.einsum(
        "dbqhe,dbkhe->dbhqk", grad_heads, near_v, preferred_element_type=jnp.float32
    )
    prob_far = jnp.einsum(
        "dbqhe,dkhe->dbhqk", grad_heads, far_v, preferred_element_type=jnp.float32
    )
    row_dot = jnp.sum(weight_near * prob_near, axis=-1, keepdims=True) + jnp.sum(
        weight_far * prob_far, axis=-1, keepdims=True
    )
    grad_near = (weight_near * (prob_near - row_dot)).astype(jnp.bfloat16)
    grad_far = (weight_far * (prob_far - row_dot)).astype(jnp.bfloat16)
    query_sum = jnp.einsum(
        "dbhqk,dbkhe->dbqhe", grad_near, near_k, preferred_element_type=jnp.float32
    )
    query_sum = query_sum + jnp.einsum(
        "dbhqk,dkhe->dbqhe", grad_far, far_k, preferred_element_type=jnp.float32
    )
    query_grad = (
        (query_sum * score_scale).reshape(doc_count, tok_count, head_cols).astype(jnp.bfloat16)
    )
    near_key_rows = (
        jnp.einsum("dbhqk,dbqhe->dbkhe", grad_near, query_heads, preferred_element_type=jnp.float32)
        * score_scale
    )
    near_value_rows = jnp.einsum(
        "dbhqk,dbqhe->dbkhe", rounded_near, grad_heads, preferred_element_type=jnp.float32
    )
    far_key_rows = (
        jnp.einsum("dbhqk,dbqhe->dkhe", grad_far, query_heads, preferred_element_type=jnp.float32)
        * score_scale
    )
    far_value_rows = jnp.einsum(
        "dbhqk,dbqhe->dkhe", rounded_far, grad_heads, preferred_element_type=jnp.float32
    )
    near_rows = jnp.stack([near_key_rows, near_value_rows]).reshape(
        2, doc_count, 2, NEAR + 1, block, head_cols
    )
    back_six = jax.vmap(place_blocks, in_axes=(1, 0), out_axes=1)(near_rows, chosen)
    rims = jnp.concatenate([back_six[:, :, 0:2], back_six[:, :, 4:6]], axis=2).reshape(
        2, doc_count, 2 * tok_count, head_cols
    )
    beside_all = extended(rims.astype(jnp.bfloat16), (("seq", 2),), tok_count).astype(
        jnp.float32
    )
    token_grad = back_six[:, :, 2:4].reshape(2, doc_count, tok_count, head_cols)
    token_grad = token_grad + beside_all[:, :, :tok_count] + beside_all[:, :, 3 * tok_count :]
    far_rows = jnp.stack([far_key_rows, far_value_rows]).reshape(
        2, doc_count, levels, block, head_cols
    )
    for level_no in range(levels):
        count = 1 << level_no
        height = block // count
        level_sum = None
        for step in range(count, 2 * count):
            slot = (position ^ step) & (count - 1)
            segment = lax.dynamic_slice_in_dim(far_rows[:, :, level_no], slot * height, height, axis=2)
            returned = lax.ppermute(
                segment.astype(jnp.bfloat16), "seq", [(i, i ^ step) for i in range(seq_count)]
            ).astype(jnp.float32)
            level_sum = returned if level_sum is None else level_sum + returned
        spread = 2 ** (level_no + 1)
        token_grad = token_grad + jnp.repeat(level_sum, spread, axis=2) / float(spread)
    key_grad = token_grad[0].astype(jnp.bfloat16)
    value_grad = token_grad[1].astype(jnp.bfloat16)
    return (attention, query_grad, key_grad, value_grad, weight_grad)


def solution(mesh):
    in_specs = (
        P(("groups", "dp"), "seq", "head"),
        P(("groups", "dp"), "seq", "head"),
        P(("groups", "dp"), "seq", "head"),
        P(("groups", "dp"), "seq", None),
        P("seq", "head"),
        P(("groups", "dp"), "seq", None),
    )
    out_specs = (
        P(("groups", "dp"), "seq", "head"),
        P(("groups", "dp"), "seq", "head"),
        P(("groups", "dp"), "seq", "head"),
        P(("groups", "dp"), "seq", "head"),
        P(("groups", "seq"), "head"),
    )
    return jax.shard_map(shards, mesh=mesh, in_specs=in_specs, out_specs=out_specs, check_vma=False)
```

```python
import math

import jax
import jax.numpy as jnp
from jax import lax
from jax.sharding import PartitionSpec as P

HEAD_DIM = 128
NEAR = 2


def extended(cells, sides, width):
    for axis, dim in sides:
        count = lax.axis_size(axis)
        ends = count - 1
        head = lax.slice_in_dim(cells, 0, width, axis=dim)
        tail = lax.slice_in_dim(cells, cells.shape[dim] - width, cells.shape[dim], axis=dim)
        cells = jnp.concatenate(
            [
                lax.ppermute(tail, axis, [(i, (i + 1) % count) for i in range(ends)]),
                cells,
                lax.ppermute(head, axis, [((i + 1) % count, i) for i in range(ends)]),
            ],
            axis=dim,
        )
    return cells


def swapped(shard, axis, stride):
    return lax.ppermute(shard, axis, [(i, i ^ 1 << stride) for i in range(lax.axis_size(axis))])


def pool_pairs(source):
    shaped = source.reshape(
        source.shape[0], source.shape[1], source.shape[2] // 2, 2, source.shape[3]
    )
    return jnp.sum(shaped, axis=3) * 0.5


def pick_blocks(blocks_doc, chosen_doc):
    return blocks_doc[:, chosen_doc]


def place_blocks(grad_doc, chosen_doc):
    holder = jnp.zeros((grad_doc.shape[0], 6, grad_doc.shape[3], grad_doc.shape[4]), jnp.float32)
    return holder.at[:, chosen_doc].add(grad_doc)


def shards(queries, keys, values, pattern, out_weight, cotangent):
    doc_count, tok_count, head_cols = queries.shape
    block = tok_count // 2
    heads = head_cols // HEAD_DIM
    seq_count = lax.axis_size("seq")
    levels = seq_count.bit_length() - 1
    position = lax.axis_index("seq")
    score_scale = 1.0 / math.sqrt(HEAD_DIM)
    near_width = (NEAR + 1) * block
    key_value = jnp.stack([keys, values])
    padded = extended(key_value, (("seq", 2),), tok_count)
    blocks_six = padded.reshape(2, doc_count, 6, block, head_cols)
    local_ids = jnp.arange(2, dtype=jnp.int32)[None, :, None]
    chosen = jnp.concatenate([local_ids, local_ids + pattern], axis=2) + 2
    near_pair = jax.vmap(pick_blocks, in_axes=(1, 0), out_axes=1)(blocks_six, chosen)
    near_pair = near_pair.reshape(2, doc_count, 2, near_width, head_cols)
    pooled = pool_pairs(key_value.astype(jnp.float32))
    siblings = []
    own_level = pooled
    for level_no in range(levels):
        other = swapped(own_level, "seq", level_no)
        siblings.append(other)
        if level_no + 1 < levels:
            upper = position >> level_no & 1 == 1
            joined = jnp.where(
                upper,
                jnp.concatenate([other, own_level], axis=2),
                jnp.concatenate([own_level, other], axis=2),
            )
            own_level = pool_pairs(joined)
    far_pair = jnp.concatenate(siblings, axis=2).astype(jnp.bfloat16)
    query_heads = queries.reshape(doc_count, 2, block, heads, HEAD_DIM)
    near_k = near_pair[0].reshape(doc_count, 2, near_width, heads, HEAD_DIM)
    near_v = near_pair[1].reshape(doc_count, 2, near_width, heads, HEAD_DIM)
    far_k = far_pair[0].reshape(doc_count, levels * block, heads, HEAD_DIM)
    far_v = far_pair[1].reshape(doc_count, levels * block, heads, HEAD_DIM)
    score_near = (
        jnp.einsum("dbqhe,dbkhe->dbhqk", query_heads, near_k, preferred_element_type=jnp.float32)
        * score_scale
    )
    score_far = (
        jnp.einsum("dbqhe,dkhe->dbhqk", query_heads, far_k, preferred_element_type=jnp.float32)
        * score_scale
    )
    top = jnp.maximum(
        jnp.max(score_near, axis=-1, keepdims=True), jnp.max(score_far, axis=-1, keepdims=True)
    )
    exp_near = jnp.exp(score_near - top)
    exp_far = jnp.exp(score_far - top)
    total = jnp.sum(exp_near, axis=-1, keepdims=True) + jnp.sum(exp_far, axis=-1, keepdims=True)
    weight_near = exp_near / total
    weight_far = exp_far / total
    rounded_near = weight_near.astype(jnp.bfloat16)
    rounded_far = weight_far.astype(jnp.bfloat16)
    output = jnp.einsum(
        "dbhqk,dbkhe->dbqhe", rounded_near, near_v, preferred_element_type=jnp.float32
    )
    output = output + jnp.einsum(
        "dbhqk,dkhe->dbqhe", rounded_far, far_v, preferred_element_type=jnp.float32
    )
    attention = output.reshape(doc_count, tok_count, head_cols).astype(jnp.bfloat16)
    feat_count = cotangent.shape[2] // seq_count
    cot_rows = cotangent.reshape(doc_count * tok_count, cotangent.shape[2])
    out_rows = attention.reshape(doc_count * tok_count, head_cols)
    own_cols = lax.dynamic_slice_in_dim(cot_rows, position * feat_count, feat_count, axis=1)
    grad_sum = jnp.dot(own_cols, out_weight, preferred_element_type=jnp.float32)
    feat_list = [own_cols]
    for step in range(1, seq_count):
        pairs = [(i, i ^ step) for i in range(seq_count)]
        sent = lax.dynamic_slice_in_dim(
            cot_rows, (position ^ step) * feat_count, feat_count, axis=1
        )
        half = sent.shape[0] // 2
        core = lax.axis_index("head")
        got_half = lax.ppermute(
            lax.dynamic_slice_in_dim(sent, core * half, half, axis=0), "seq", pairs
        )
        other_half = swapped(got_half, "head", 0)
        got = jnp.where(
            core == 0,
            jnp.concatenate([got_half, other_half], axis=0),
            jnp.concatenate([other_half, got_half], axis=0),
        )
        part = jnp.dot(got, out_weight, preferred_element_type=jnp.float32)
        back = lax.ppermute(part.astype(jnp.bfloat16), "seq", pairs)
        grad_sum = grad_sum + back.astype(jnp.float32)
        feat_list.append(got)
    attn_grad = grad_sum.astype(jnp.bfloat16)
    feat_order = jnp.arange(seq_count, dtype=jnp.int32) ^ position
    feat_docs = jnp.take(jnp.stack(feat_list, axis=0), feat_order, axis=0).reshape(
        seq_count * cot_rows.shape[0], feat_count
    )
    if lax.axis_size("dp") == 2:
        feat_docs = jnp.take(
            jnp.stack([feat_docs, swapped(feat_docs, "dp", 0)], axis=0),
            jnp.arange(2, dtype=jnp.int32) ^ lax.axis_index("dp"),
            axis=0,
        ).reshape(2 * feat_docs.shape[0], feat_count)
    else:
        feat_docs = lax.all_gather(feat_docs, "dp", axis=0, tiled=True)
    whole_output = lax.all_gather(out_rows, ("dp", "seq"), axis=0, tiled=True)
    weight_grad = jnp.einsum(
        "tc,tw->cw", feat_docs, whole_output, preferred_element_type=jnp.float32
    )
    grad_heads = attn_grad.reshape(doc_count, 2, block, heads, HEAD_DIM)
    prob_near = jnp.einsum(
        "dbqhe,dbkhe->dbhqk", grad_heads, near_v, preferred_element_type=jnp.float32
    )
    prob_far = jnp.einsum(
        "dbqhe,dkhe->dbhqk", grad_heads, far_v, preferred_element_type=jnp.float32
    )
    row_dot = jnp.sum(weight_near * prob_near, axis=-1, keepdims=True) + jnp.sum(
        weight_far * prob_far, axis=-1, keepdims=True
    )
    grad_near = (weight_near * (prob_near - row_dot)).astype(jnp.bfloat16)
    grad_far = (weight_far * (prob_far - row_dot)).astype(jnp.bfloat16)
    query_sum = jnp.einsum(
        "dbhqk,dbkhe->dbqhe", grad_near, near_k, preferred_element_type=jnp.float32
    )
    query_sum = query_sum + jnp.einsum(
        "dbhqk,dkhe->dbqhe", grad_far, far_k, preferred_element_type=jnp.float32
    )
    query_grad = (
        (query_sum * score_scale).reshape(doc_count, tok_count, head_cols).astype(jnp.bfloat16)
    )
    near_key_rows = (
        jnp.einsum("dbhqk,dbqhe->dbkhe", grad_near, query_heads, preferred_element_type=jnp.float32)
        * score_scale
    )
    near_value_rows = jnp.einsum(
        "dbhqk,dbqhe->dbkhe", rounded_near, grad_heads, preferred_element_type=jnp.float32
    )
    far_key_rows = (
        jnp.einsum("dbhqk,dbqhe->dkhe", grad_far, query_heads, preferred_element_type=jnp.float32)
        * score_scale
    )
    far_value_rows = jnp.einsum(
        "dbhqk,dbqhe->dkhe", rounded_far, grad_heads, preferred_element_type=jnp.float32
    )
    near_rows = jnp.stack([near_key_rows, near_value_rows]).reshape(
        2, doc_count, 2, NEAR + 1, block, head_cols
    )
    back_six = jax.vmap(place_blocks, in_axes=(1, 0), out_axes=1)(near_rows, chosen)
    rims = jnp.concatenate([back_six[:, :, 0:2], back_six[:, :, 4:6]], axis=2).reshape(
        2, doc_count, 2 * tok_count, head_cols
    )
    beside_all = extended(rims.astype(jnp.bfloat16), (("seq", 2),), tok_count).astype(
        jnp.float32
    )
    token_grad = back_six[:, :, 2:4].reshape(2, doc_count, tok_count, head_cols)
    token_grad = token_grad + beside_all[:, :, :tok_count] + beside_all[:, :, 3 * tok_count :]
    far_rows = jnp.stack([far_key_rows, far_value_rows]).reshape(
        2, doc_count, levels, block, head_cols
    )
    for level_no in range(levels):
        count = 1 << level_no
        height = block // count
        level_sum = None
        for step in range(count, 2 * count):
            slot = (position ^ step) & (count - 1)
            segment = lax.dynamic_slice_in_dim(far_rows[:, :, level_no], slot * height, height, axis=2)
            returned = lax.ppermute(
                segment.astype(jnp.bfloat16), "seq", [(i, i ^ step) for i in range(seq_count)]
            ).astype(jnp.float32)
            level_sum = returned if level_sum is None else level_sum + returned
        spread = 2 ** (level_no + 1)
        token_grad = token_grad + jnp.repeat(level_sum, spread, axis=2) / float(spread)
    key_grad = token_grad[0].astype(jnp.bfloat16)
    value_grad = token_grad[1].astype(jnp.bfloat16)
    return (attention, query_grad, key_grad, value_grad, weight_grad)


def solution(mesh):
    in_specs = (
        P(("groups", "dp"), "seq", "head"),
        P(("groups", "dp"), "seq", "head"),
        P(("groups", "dp"), "seq", "head"),
        P(("groups", "dp"), "seq", None),
        P("seq", "head"),
        P(("groups", "dp"), "seq", None),
    )
    out_specs = (
        P(("groups", "dp"), "seq", "head"),
        P(("groups", "dp"), "seq", "head"),
        P(("groups", "dp"), "seq", "head"),
        P(("groups", "dp"), "seq", "head"),
        P(("groups", "seq"), "head"),
    )
    return jax.shard_map(shards, mesh=mesh, in_specs=in_specs, out_specs=out_specs, check_vma=False)
```

```python
import math

import jax
import jax.numpy as jnp
from jax import lax
from jax.sharding import PartitionSpec as P

HEAD_DIM = 128
NEAR = 2


def extended(cells, sides, width):
    for axis, dim in sides:
        count = lax.axis_size(axis)
        ends = count - 1
        head = lax.slice_in_dim(cells, 0, width, axis=dim)
        tail = lax.slice_in_dim(cells, cells.shape[dim] - width, cells.shape[dim], axis=dim)
        cells = jnp.concatenate(
            [
                lax.ppermute(tail, axis, [(i, (i + 1) % count) for i in range(ends)]),
                cells,
                lax.ppermute(head, axis, [((i + 1) % count, i) for i in range(ends)]),
            ],
            axis=dim,
        )
    return cells


def swapped(shard, axis, stride):
    return lax.ppermute(shard, axis, [(i, i ^ 1 << stride) for i in range(lax.axis_size(axis))])


def pool_pairs(source):
    shaped = source.reshape(
        source.shape[0], source.shape[1], source.shape[2] // 2, 2, source.shape[3]
    )
    return jnp.sum(shaped, axis=3) * 0.5


def pick_blocks(blocks_doc, chosen_doc):
    return blocks_doc[:, chosen_doc]


def place_blocks(grad_doc, chosen_doc):
    holder = jnp.zeros((grad_doc.shape[0], 6, grad_doc.shape[3], grad_doc.shape[4]), jnp.float32)
    return holder.at[:, chosen_doc].add(grad_doc)


def shards(queries, keys, values, pattern, out_weight, cotangent):
    doc_count, tok_count, head_cols = queries.shape
    block = tok_count // 2
    heads = head_cols // HEAD_DIM
    seq_count = lax.axis_size("seq")
    levels = seq_count.bit_length() - 1
    position = lax.axis_index("seq")
    score_scale = 1.0 / math.sqrt(HEAD_DIM)
    near_width = (NEAR + 1) * block
    key_value = jnp.stack([keys, values])
    padded = extended(key_value, (("seq", 2),), tok_count)
    blocks_six = padded.reshape(2, doc_count, 6, block, head_cols)
    local_ids = jnp.arange(2, dtype=jnp.int32)[None, :, None]
    chosen = jnp.concatenate([local_ids, local_ids + pattern], axis=2) + 2
    near_pair = jax.vmap(pick_blocks, in_axes=(1, 0), out_axes=1)(blocks_six, chosen)
    near_pair = near_pair.reshape(2, doc_count, 2, near_width, head_cols)
    pooled = pool_pairs(key_value.astype(jnp.float32))
    siblings = []
    own_level = pooled
    for level_no in range(levels):
        other = swapped(own_level, "seq", level_no)
        siblings.append(other)
        if level_no + 1 < levels:
            upper = position >> level_no & 1 == 1
            joined = jnp.where(
                upper,
                jnp.concatenate([other, own_level], axis=2),
                jnp.concatenate([own_level, other], axis=2),
            )
            own_level = pool_pairs(joined)
    far_pair = jnp.concatenate(siblings, axis=2).astype(jnp.bfloat16)
    query_heads = queries.reshape(doc_count, 2, block, heads, HEAD_DIM)
    near_k = near_pair[0].reshape(doc_count, 2, near_width, heads, HEAD_DIM)
    near_v = near_pair[1].reshape(doc_count, 2, near_width, heads, HEAD_DIM)
    far_k = far_pair[0].reshape(doc_count, levels * block, heads, HEAD_DIM)
    far_v = far_pair[1].reshape(doc_count, levels * block, heads, HEAD_DIM)
    score_near = (
        jnp.einsum("dbqhe,dbkhe->dbhqk", query_heads, near_k, preferred_element_type=jnp.float32)
        * score_scale
    )
    score_far = (
        jnp.einsum("dbqhe,dkhe->dbhqk", query_heads, far_k, preferred_element_type=jnp.float32)
        * score_scale
    )
    top = jnp.maximum(
        jnp.max(score_near, axis=-1, keepdims=True), jnp.max(score_far, axis=-1, keepdims=True)
    )
    exp_near = jnp.exp(score_near - top)
    exp_far = jnp.exp(score_far - top)
    total = jnp.sum(exp_near, axis=-1, keepdims=True) + jnp.sum(exp_far, axis=-1, keepdims=True)
    weight_near = exp_near / total
    weight_far = exp_far / total
    rounded_near = weight_near.astype(jnp.bfloat16)
    rounded_far = weight_far.astype(jnp.bfloat16)
    output = jnp.einsum(
        "dbhqk,dbkhe->dbqhe", rounded_near, near_v, preferred_element_type=jnp.float32
    )
    output = output + jnp.einsum(
        "dbhqk,dkhe->dbqhe", rounded_far, far_v, preferred_element_type=jnp.float32
    )
    attention = output.reshape(doc_count, tok_count, head_cols).astype(jnp.bfloat16)
    feat_count = cotangent.shape[2] // seq_count
    cot_rows = cotangent.reshape(doc_count * tok_count, cotangent.shape[2])
    out_rows = attention.reshape(doc_count * tok_count, head_cols)
    own_cols = lax.dynamic_slice_in_dim(cot_rows, position * feat_count, feat_count, axis=1)
    grad_sum = jnp.dot(own_cols, out_weight, preferred_element_type=jnp.float32)
    feat_list = [own_cols]
    for step in range(1, seq_count):
        pairs = [(i, i ^ step) for i in range(seq_count)]
        sent = lax.dynamic_slice_in_dim(
            cot_rows, (position ^ step) * feat_count, feat_count, axis=1
        )
        half = sent.shape[0] // 2
        core = lax.axis_index("head")
        got_half = lax.ppermute(
            lax.dynamic_slice_in_dim(sent, core * half, half, axis=0), "seq", pairs
        )
        other_half = swapped(got_half, "head", 0)
        got = lax.dynamic_update_slice_in_dim(
            lax.dynamic_update_slice_in_dim(jnp.zeros_like(sent), got_half, core * half, axis=0),
            other_half,
            (1 - core) * half,
            axis=0,
        )
        part = jnp.dot(got, out_weight, preferred_element_type=jnp.float32)
        back = lax.ppermute(part.astype(jnp.bfloat16), "seq", pairs)
        grad_sum = grad_sum + back.astype(jnp.float32)
        feat_list.append(got)
    attn_grad = grad_sum.astype(jnp.bfloat16)
    feat_order = jnp.arange(seq_count, dtype=jnp.int32) ^ position
    feat_docs = jnp.take(jnp.stack(feat_list, axis=0), feat_order, axis=0).reshape(
        seq_count * cot_rows.shape[0], feat_count
    )
    feat_docs = lax.all_gather(feat_docs, "dp", axis=0, tiled=True)
    whole_output = lax.all_gather(out_rows, ("dp", "seq"), axis=0, tiled=True)
    weight_grad = jnp.einsum(
        "tc,tw->cw", feat_docs, whole_output, preferred_element_type=jnp.float32
    )
    grad_heads = attn_grad.reshape(doc_count, 2, block, heads, HEAD_DIM)
    prob_near = jnp.einsum(
        "dbqhe,dbkhe->dbhqk", grad_heads, near_v, preferred_element_type=jnp.float32
    )
    prob_far = jnp.einsum(
        "dbqhe,dkhe->dbhqk", grad_heads, far_v, preferred_element_type=jnp.float32
    )
    row_dot = jnp.sum(weight_near * prob_near, axis=-1, keepdims=True) + jnp.sum(
        weight_far * prob_far, axis=-1, keepdims=True
    )
    grad_near = (weight_near * (prob_near - row_dot)).astype(jnp.bfloat16)
    grad_far = (weight_far * (prob_far - row_dot)).astype(jnp.bfloat16)
    query_sum = jnp.einsum(
        "dbhqk,dbkhe->dbqhe", grad_near, near_k, preferred_element_type=jnp.float32
    )
    query_sum = query_sum + jnp.einsum(
        "dbhqk,dkhe->dbqhe", grad_far, far_k, preferred_element_type=jnp.float32
    )
    query_grad = (
        (query_sum * score_scale).reshape(doc_count, tok_count, head_cols).astype(jnp.bfloat16)
    )
    near_key_rows = (
        jnp.einsum("dbhqk,dbqhe->dbkhe", grad_near, query_heads, preferred_element_type=jnp.float32)
        * score_scale
    )
    near_value_rows = jnp.einsum(
        "dbhqk,dbqhe->dbkhe", rounded_near, grad_heads, preferred_element_type=jnp.float32
    )
    far_key_rows = (
        jnp.einsum("dbhqk,dbqhe->dkhe", grad_far, query_heads, preferred_element_type=jnp.float32)
        * score_scale
    )
    far_value_rows = jnp.einsum(
        "dbhqk,dbqhe->dkhe", rounded_far, grad_heads, preferred_element_type=jnp.float32
    )
    near_rows = jnp.stack([near_key_rows, near_value_rows]).reshape(
        2, doc_count, 2, NEAR + 1, block, head_cols
    )
    back_six = jax.vmap(place_blocks, in_axes=(1, 0), out_axes=1)(near_rows, chosen)
    rims = jnp.concatenate([back_six[:, :, 0:2], back_six[:, :, 4:6]], axis=2).reshape(
        2, doc_count, 2 * tok_count, head_cols
    )
    beside_all = extended(rims.astype(jnp.bfloat16), (("seq", 2),), tok_count).astype(
        jnp.float32
    )
    token_grad = back_six[:, :, 2:4].reshape(2, doc_count, tok_count, head_cols)
    token_grad = token_grad + beside_all[:, :, :tok_count] + beside_all[:, :, 3 * tok_count :]
    far_rows = jnp.stack([far_key_rows, far_value_rows]).reshape(
        2, doc_count, levels, block, head_cols
    )
    for level_no in range(levels):
        count = 1 << level_no
        height = block // count
        level_sum = None
        for step in range(count, 2 * count):
            slot = (position ^ step) & (count - 1)
            segment = lax.dynamic_slice_in_dim(far_rows[:, :, level_no], slot * height, height, axis=2)
            returned = lax.ppermute(
                segment.astype(jnp.bfloat16), "seq", [(i, i ^ step) for i in range(seq_count)]
            ).astype(jnp.float32)
            level_sum = returned if level_sum is None else level_sum + returned
        spread = 2 ** (level_no + 1)
        token_grad = token_grad + jnp.repeat(level_sum, spread, axis=2) / float(spread)
    key_grad = token_grad[0].astype(jnp.bfloat16)
    value_grad = token_grad[1].astype(jnp.bfloat16)
    return (attention, query_grad, key_grad, value_grad, weight_grad)


def solution(mesh):
    in_specs = (
        P(("groups", "dp"), "seq", "head"),
        P(("groups", "dp"), "seq", "head"),
        P(("groups", "dp"), "seq", "head"),
        P(("groups", "dp"), "seq", None),
        P("seq", "head"),
        P(("groups", "dp"), "seq", None),
    )
    out_specs = (
        P(("groups", "dp"), "seq", "head"),
        P(("groups", "dp"), "seq", "head"),
        P(("groups", "dp"), "seq", "head"),
        P(("groups", "dp"), "seq", "head"),
        P(("groups", "seq"), "head"),
    )
    return jax.shard_map(shards, mesh=mesh, in_specs=in_specs, out_specs=out_specs, check_vma=False)
```
